256 devices in a mesh: seq: 64 (over z, x, core), tp: 4 (over y).
Axes of the slice: x: 4, y: 4, z: 8, core: 2. Of those that a mesh axis runs over, the one named last changes fastest.
Arguments:
- hidden: bfloat16 [8192, 1024], P('seq'), may hold values from -120 to 120
- page_table: int32 [16, 256], replicated, may hold values from -1 to 2111, as said below
- cache_len: int32 [16], replicated, may hold values from 129 to 32768, as said below
- expert_ids: int32 [8192, 2], P('seq'), may hold values from 0 to 31, all different within a row; in each aligned block of 128 rows (0 to 127, 128 to 255, ...) at most 10 rows name the same one
- w_query: bfloat16 [1024, 1024], P(None, 'tp'), may hold values from -4 to 4
- w_key: bfloat16 [1024, 1024], P(None, 'tp'), may hold values from -0.1875 to 0.1875
- w_value: bfloat16 [1024, 1024], P(None, 'tp'), may hold values from -0.1875 to 0.1875
- w_out: bfloat16 [1024, 1024], P('tp'), may hold values from -0.1875 to 0.1875
- cache_k: bfloat16 [2112, 128, 1024], P('seq', None, 'tp'), may hold values from -4000 to 4000
- cache_v: bfloat16 [2112, 128, 1024], P('seq', None, 'tp'), may hold values from -6 to 6
- moe_gain: float32 [1024], replicated, may hold values from 0.1 to 1.9
- router: float32 [1024, 32], replicated, may hold values from -0.1875 to 0.1875
- w_gate_up: bfloat16 [64, 2, 1024, 1408], P('seq', None, None, 'tp'), may hold values from -0.1875 to 0.1875
- w_down: bfloat16 [64, 1408, 1024], P('seq', 'tp'), may hold values from -0.109375 to 0.109375
Outputs:
- out: bfloat16 [8192, 1024], P('seq', 'tp')
The draws below stay inside these ranges and needn't reach their ends.
Inputs may be any that keep to these rules, and one draw needn't show every extreme that they name: `page_table`: row r lists the pages of request r's cache in order, ceil(cache_len[r] / 128) of them, then -1; no page number appears twice in the table. `cache_len`: half of the requests have exactly 32768 cached tokens; the others have at most 384. `expert_ids`: A token names 2 different experts; among the 128 tokens of one device no expert is named more than 10 times, and on some device one expert is named exactly 10 times.
All inputs are finite; a program needn't handle non-finite values.
Results may differ from the reference program's by a relative error of at most 0.0085.
Values may be sent and summed in bfloat16 or wider, within the bound.
No kernel may reach another device: no remote copies, remote signals or barrier semaphores. Data moves between devices by JAX's collectives and lax.ppermute only.
A program may use at most 128 MiB of HBM per device.

```python
import math
import jax
import jax.numpy as jnp
import numpy as np
from jax import lax

D = 1024
HEADS = 16
DH = 64
EXPERTS = 32
FF = 2816
TOP = 2
PAGE = 128
MAXP = 256
SPAN_DEVS = 4
TOK_DEV = 128
TOKENS = 8192
SPAN = 512
REQS = 16
PAGES = 2112
CAP = 10
FSPLIT = 2
FFS = 1408
N_SEQ = 64


def query_matrix(key):
    noise = jnp.clip(jax.random.normal(jax.random.fold_in(key, 71), (D, HEADS * DH), jnp.float32), -6.0, 6.0)
    return noise * (3.0 * D ** (-0.5))


def draw_w_query(key, part):
    return query_matrix(key).astype(jnp.bfloat16)


def draw_cache_k(key, part):
    base = jnp.clip(jax.random.normal(jax.random.fold_in(key, 5), (PAGES, PAGE, HEADS * DH), jnp.float32), -6.0, 6.0)
    return base.astype(jnp.bfloat16)


def draw_hidden(key, part):
    noise = jnp.clip(jax.random.normal(jax.random.fold_in(key, 21), (TOKENS, D), jnp.float32), -6.0, 6.0)
    columns = jnp.exp(jax.random.uniform(jax.random.fold_in(key, 22), (1, D), jnp.float32, math.log(0.5), math.log(2.0)))
    values = noise * columns
    return values.astype(jnp.bfloat16)


def request_lengths(key):
    longs = jax.random.permutation(jax.random.fold_in(key, 31), REQS) < REQS // 2
    shorts = jax.random.randint(jax.random.fold_in(key, 32), (REQS,), PAGE + 1, 3 * PAGE + 1)
    return jnp.where(longs, MAXP * PAGE, shorts).astype(jnp.int32)


def draw_cache_len(key, part):
    return request_lengths(key)


def draw_page_table(key, part):
    lengths = request_lengths(key)
    needed = (lengths + PAGE - 1) // PAGE
    starts = jnp.cumsum(needed) - needed
    order = jnp.concatenate([jnp.array([PAGES - 1], jnp.int32), jax.random.permutation(jax.random.fold_in(key, 33), PAGES - 1).astype(jnp.int32)])
    position = starts[:, None] + jnp.arange(MAXP)[None, :]
    table = order[jnp.minimum(position, PAGES - 1)]
    return jnp.where(jnp.arange(MAXP)[None, :] < needed[:, None], table, -1).astype(jnp.int32)


def steps_of(key, dims, shards, least, top_value):
    factor_of, own = 1.0, jax.random.fold_in(key, 6)
    for dim, shards_of in shards:
        steps = jnp.exp(jax.random.uniform(jax.random.fold_in(own, dim), (shards_of,), jnp.float32, least / len(shards), top_value / len(shards)))
        factor_of = factor_of * jnp.repeat(steps, dims[dim] // shards_of).reshape([-1 if axis == dim else 1 for axis in range(len(dims))])
    return factor_of


def shared_out(key, own, number, rows, count, top, bound, slope):
    ranking = jax.random.permutation(key, count)
    heavy_load, common = load_shares(count, rows * top, bound, slope, True), load_shares(count, rows * top, bound, slope, False)
    places = jnp.arange(count)

    def named(sizes, rotation):
        used = int((sizes > 0).sum())
        fixed = max(1, used // 4)
        shifted = fixed + (places - fixed + rotation * (used - fixed)) % max(1, count - fixed)
        return jnp.zeros((count,), jnp.int32).at[ranking[jnp.where(places < fixed, places, shifted)]].set(jnp.asarray(sizes, jnp.int32))

    sizes = jnp.where(number % 4 == 0, named(heavy_load, number // 4), named(common, number - number // 4 - 1))
    mixed = jax.random.permutation(jax.random.fold_in(own, 3), count)
    donor, taker = mixed[0:count // 2 * 2:2], mixed[1:count // 2 * 2:2]
    margin = jnp.minimum(sizes[donor] - 1, bound - sizes[taker]) // 2
    margin = jnp.where((donor == ranking[0]) | (taker == ranking[0]) | (sizes[taker] == 0), 0, jnp.maximum(margin, 0))
    shifted = jax.random.randint(jax.random.fold_in(own, 4), (count // 2,), 0, 1 << 20) % (margin + 1)
    sizes = sizes.at[donor].add(-shifted).at[taker].add(shifted)
    items = jnp.searchsorted(jnp.cumsum(sizes), jnp.arange(rows * top), side="right").astype(jnp.int32)
    grid = items.reshape(top, rows).T
    grid = grid[jax.random.permutation(jax.random.fold_in(own, 1), rows)]
    rotation = jax.random.randint(jax.random.fold_in(own, 2), (rows, 1), 0, top)
    return jnp.take_along_axis(grid, (jnp.arange(top)[None, :] + rotation) % top, axis=1)


def load_shares(count, total, reach, skew, full):
    loads = [(1 << 20) // math.isqrt(rank ** skew) + 1 for rank in range(1, count + 1)]
    largest = reach if full else min(reach, max(-(-total // count), total * loads[0] // sum(loads)))
    least = 1 if total - largest >= count - 1 else 0
    given, surplus = [largest] + [least] * (count - 1), total - largest - least * (count - 1)
    while surplus > 0:
        candidates = [i for i in range(1, count) if given[i] < largest] or [i for i in range(1, count) if given[i] < reach]
        pool, remaining = sum([loads[i] for i in candidates]), surplus
        for i in candidates:
            addition = min(reach - given[i], max(1, remaining * loads[i] // pool), surplus)
            given[i] = given[i] + addition
            surplus = surplus - addition
    return np.array(given)


def centred(key, dims, deviation, limit, shards=(), kind=jnp.bfloat16):
    factor_of = steps_of(key, dims, shards, -0.22, 0.18) if shards else 1.0
    values = jax.random.normal(key, dims, jnp.float32) * deviation * factor_of
    return jnp.minimum(jnp.maximum(values, -limit), limit).astype(kind)


def setup_inputs(seed: int = 0) -> dict:
    arg_keys = jax.random.split(jax.random.key(seed), 15)
    hidden = draw_hidden(jax.random.fold_in(arg_keys[14], 71), 0)
    page_table = draw_page_table(jax.random.fold_in(arg_keys[14], 71), 0)
    cache_len = draw_cache_len(jax.random.fold_in(arg_keys[14], 71), 0)
    expert_ids_keys = jax.random.split(jax.random.fold_in(arg_keys[3], 1), TOKENS // TOK_DEV)
    expert_ids_turns = jax.random.permutation(jax.random.fold_in(arg_keys[3], 3), TOKENS // TOK_DEV)
    expert_ids = jax.vmap(lambda own, number: shared_out(jax.random.fold_in(arg_keys[3], 2), own, number, TOK_DEV, EXPERTS, TOP, CAP, 2))(expert_ids_keys, expert_ids_turns).reshape((TOKENS, TOP))
    w_query = draw_w_query(jax.random.fold_in(arg_keys[14], 71), 0)
    w_key = centred(arg_keys[5], (D, HEADS * DH), D ** -0.5, 0.1875, ((1, 4),))
    w_value = centred(arg_keys[6], (D, HEADS * DH), D ** -0.5, 0.1875, ((1, 4),))
    w_out = centred(arg_keys[7], (HEADS * DH, D), (HEADS * DH) ** -0.5, 0.1875, ((0, 4),))
    cache_k = draw_cache_k(jax.random.fold_in(arg_keys[14], 71), 0)
    cache_v = centred(arg_keys[9], (PAGES, PAGE, HEADS * DH), 1.0, 6.0, ((0, 64), (2, 4)))
    moe_gain = jnp.clip(1.0 + 0.18 * jax.random.normal(arg_keys[10], (D,), jnp.float32), 0.1, 1.9)
    router = centred(arg_keys[11], (D, EXPERTS), D ** -0.5, 0.1875, (), jnp.float32)
    w_gate_up = centred(arg_keys[12], (EXPERTS * FSPLIT, 2, D, FFS), D ** -0.5, 0.1875, ((0, 64), (3, 4)))
    w_down = centred(arg_keys[13], (EXPERTS * FSPLIT, FFS, D), FF ** -0.5, 0.109375, ((0, 64), (1, 4)))
    return {"hidden": hidden, "page_table": page_table, "cache_len": cache_len, "expert_ids": expert_ids, "w_query": w_query, "w_key": w_key, "w_value": w_value, "w_out": w_out, "cache_k": cache_k, "cache_v": cache_v, "moe_gain": moe_gain, "router": router, "w_gate_up": w_gate_up, "w_down": w_down}


NEGATIVE = -1e+30

def rms_rows(values):
    return values * lax.rsqrt(lax.optimization_barrier(jnp.mean(values * values, axis=-1, keepdims=True)) + 1e-06)

def online_update(state, queries, keys, values, mask):
    m_old, l_old, accum = state
    scores = jnp.einsum('nhd,khd->hnk', queries.astype(jnp.float32), keys.astype(jnp.float32)) * DH ** (-0.5)
    scores = jnp.where(mask[None], scores, NEGATIVE)
    m_new = jnp.maximum(m_old, lax.optimization_barrier(jnp.max(scores, axis=-1)).T)
    probs = jnp.where(mask[None], jnp.exp(scores - m_new.T[:, :, None]), 0.0)
    factor = jnp.exp(m_old - m_new)
    l_new = l_old * factor + lax.optimization_barrier(jnp.sum(probs, axis=-1)).T
    rounded = lax.optimization_barrier(probs.astype(jnp.bfloat16))
    weighted = jnp.einsum('hnk,khd->nhd', rounded.astype(jnp.float32), values.astype(jnp.float32))
    return (m_new, l_new, accum * factor[:, :, None] + weighted)

def reference(hidden, page_table, cache_len, expert_ids, w_query, w_key, w_value, w_out, cache_k, cache_v, moe_gain, router, w_gate_up, w_down):
    normed = rms_rows(hidden.astype(jnp.float32)).astype(jnp.bfloat16)
    queries = jnp.dot(normed, w_query, preferred_element_type=jnp.float32).astype(jnp.bfloat16)
    new_keys = jnp.dot(normed, w_key, preferred_element_type=jnp.float32).astype(jnp.bfloat16)
    new_values = jnp.dot(normed, w_value, preferred_element_type=jnp.float32).astype(jnp.bfloat16)
    query_heads = queries.reshape(TOKENS, HEADS, DH)
    key_heads = new_keys.reshape(TOKENS, HEADS, DH)
    value_heads = new_values.reshape(TOKENS, HEADS, DH)

    def attend(request):
        start = request * SPAN
        rows = lax.dynamic_slice_in_dim(query_heads, start, SPAN, 0)
        state = (jnp.full((SPAN, HEADS), NEGATIVE, jnp.float32), jnp.zeros((SPAN, HEADS), jnp.float32), jnp.zeros((SPAN, HEADS, DH), jnp.float32))

        def page_step(current, order):
            page = page_table[request, order]
            index = jnp.maximum(page, 0)
            keys = lax.dynamic_index_in_dim(cache_k, index, 0, keepdims=False).reshape(PAGE, HEADS, DH)
            values = lax.dynamic_index_in_dim(cache_v, index, 0, keepdims=False).reshape(PAGE, HEADS, DH)
            positions = order * PAGE + jnp.arange(PAGE, dtype=jnp.int32)
            valid = (page >= 0) & (positions < cache_len[request])
            mask = jnp.broadcast_to(valid[None, :], (SPAN, PAGE))
            return (online_update(current, rows, keys, values, mask), None)
        state, _ = lax.scan(page_step, state, jnp.arange(MAXP, dtype=jnp.int32))
        for block in range(SPAN_DEVS):
            keys = lax.dynamic_slice_in_dim(key_heads, start + block * TOK_DEV, TOK_DEV, 0)
            values = lax.dynamic_slice_in_dim(value_heads, start + block * TOK_DEV, TOK_DEV, 0)
            mask = (block * TOK_DEV + jnp.arange(TOK_DEV, dtype=jnp.int32))[None, :] <= jnp.arange(SPAN, dtype=jnp.int32)[:, None]
            state = online_update(state, rows, keys, values, mask)
        return state[2] / state[1][:, :, None]
    attended = lax.map(attend, jnp.arange(REQS, dtype=jnp.int32))
    attention = attended.reshape(TOKENS, HEADS * DH).astype(jnp.bfloat16)
    mid = hidden.astype(jnp.float32) + jnp.dot(attention, w_out, preferred_element_type=jnp.float32)
    moe_in = (rms_rows(mid) * moe_gain).astype(jnp.bfloat16)
    logits = jnp.dot(moe_in.astype(jnp.float32), router, precision=lax.Precision.HIGHEST)
    chosen = jax.nn.sigmoid(jnp.take_along_axis(logits, expert_ids, axis=1))
    gates = chosen / lax.optimization_barrier(jnp.sum(chosen, axis=1, keepdims=True))
    blocks = expert_ids.reshape(N_SEQ, TOK_DEV * TOP)
    onehot = (blocks[:, :, None] == jnp.arange(EXPERTS, dtype=jnp.int32)[None, None, :]).astype(jnp.int32)
    ranks = lax.optimization_barrier(jnp.sum((jnp.cumsum(onehot, axis=1) - 1) * onehot, axis=2))
    flat = (blocks * N_SEQ + jnp.arange(N_SEQ, dtype=jnp.int32)[:, None]) * CAP + ranks
    token_of = jnp.repeat(jnp.arange(TOKENS, dtype=jnp.int32), TOP)
    table = jnp.full((EXPERTS * N_SEQ * CAP,), TOKENS, jnp.int32).at[flat.reshape(-1)].set(token_of)
    padded = jnp.concatenate([moe_in, jnp.zeros((1, D), jnp.bfloat16)], axis=0)
    buffer = padded[table].reshape(EXPERTS, N_SEQ * CAP, D)
    gate_up = w_gate_up.reshape(EXPERTS, FSPLIT, 2, D, FFS).transpose(0, 2, 3, 1, 4).reshape(EXPERTS, 2, D, FF)
    down = w_down.reshape(EXPERTS, FF, D)

    def run_expert(expert):
        rows = buffer[expert]
        gate = jnp.dot(rows, gate_up[expert, 0], preferred_element_type=jnp.float32)
        upper = jnp.dot(rows, gate_up[expert, 1], preferred_element_type=jnp.float32)
        inner = (jax.nn.gelu(gate, approximate=True) * upper).astype(jnp.bfloat16)
        return jnp.dot(inner, down[expert], preferred_element_type=jnp.float32)
    results = lax.map(run_expert, jnp.arange(EXPERTS, dtype=jnp.int32)).reshape(EXPERTS * N_SEQ * CAP, D)
    picked = results[flat.reshape(-1)].reshape(TOKENS, TOP, D)
    mixture = lax.optimization_barrier(jnp.sum(gates[:, :, None] * picked, axis=1))
    return (mid + mixture).astype(jnp.bfloat16)
```

```python
import jax
import jax.numpy as jnp
from jax import lax
from jax.sharding import PartitionSpec as P

DH = 64
EXPERTS = 32
TOP = 2
PAGE = 128
MAXP = 256
SPAN_DEVS = 4
CAP = 10


NEGATIVE = -1e30


def passed_along(value, axis, steps):
    count = lax.axis_size(axis)
    pairs = [(source, (source + steps) % count) for source in range(count)]
    return lax.ppermute(value, axis, pairs)


def rms_rows(values):
    return values * lax.rsqrt(jnp.mean(values * values, axis=-1, keepdims=True) + 1e-06)


def online_update(state, queries, keys, values, mask):
    m_old, l_old, accum = state
    scale = queries.shape[2] ** (-0.5)
    scores = jnp.einsum("nhd,khd->hnk", queries, keys, preferred_element_type=jnp.float32) * scale
    scores = jnp.where(mask[None], scores, NEGATIVE)
    m_new = jnp.maximum(m_old, jnp.max(scores, axis=-1).T)
    probs = jnp.where(mask[None], jnp.exp(scores - m_new.T[:, :, None]), 0.0)
    factor = jnp.exp(m_old - m_new)
    l_new = l_old * factor + jnp.sum(probs, axis=-1).T
    weighted = jnp.einsum(
        "hnk,khd->nhd", probs.astype(jnp.bfloat16), values, preferred_element_type=jnp.float32
    )
    return (m_new, l_new, accum * factor[:, :, None] + weighted)


def shards(
    hidden,
    page_table,
    cache_len,
    expert_ids,
    w_query,
    w_key,
    w_value,
    w_out,
    cache_k,
    cache_v,
    moe_gain,
    router,
    w_gate_up,
    w_down,
):
    tok_rows = hidden.shape[0]
    span_rows = tok_rows * SPAN_DEVS
    seq_count = lax.axis_size("seq")
    seq_index = lax.axis_index("seq")
    local_heads = w_query.shape[1] // DH
    request_total = page_table.shape[0]
    normed = rms_rows(hidden.astype(jnp.float32)).astype(jnp.bfloat16)
    queries = jnp.dot(normed, w_query, preferred_element_type=jnp.float32).astype(jnp.bfloat16)
    new_keys = (
        jnp.dot(normed, w_key, preferred_element_type=jnp.float32)
        .astype(jnp.bfloat16)
        .reshape(tok_rows, local_heads, DH)
    )
    new_values = (
        jnp.dot(normed, w_value, preferred_element_type=jnp.float32)
        .astype(jnp.bfloat16)
        .reshape(tok_rows, local_heads, DH)
    )
    page_count = cache_k.shape[0]
    page_ids = seq_index * page_count + jnp.arange(page_count, dtype=jnp.int32)
    listing = page_table.reshape(-1)
    matches = listing[None, :] == page_ids[:, None]
    entry_index = jnp.arange(listing.shape[0], dtype=jnp.int32)
    found = jnp.sum(jnp.where(matches, entry_index[None, :] + 1, 0), axis=1) - 1
    page_owner = jnp.where(found >= 0, found // MAXP, -1)
    page_order = jnp.where(found >= 0, found % MAXP, 0)
    page_limit = jnp.where(found >= 0, cache_len[jnp.maximum(page_owner, 0)], 0)
    own_request = seq_index * tok_rows // span_rows
    own_offset = seq_index * tok_rows % span_rows
    slot_range = jnp.arange(PAGE, dtype=jnp.int32)
    page_valid = (found >= 0)[:, None] & (
        page_order[:, None] * PAGE + slot_range[None, :] < page_limit[:, None]
    )
    span_positions = jnp.arange(span_rows, dtype=jnp.int32)
    fresh_mask = span_positions[:, None] >= own_offset + jnp.arange(tok_rows, dtype=jnp.int32)[None, :]
    mask = jnp.concatenate(
        [
            jnp.broadcast_to(page_valid[:, None, :], (page_count, span_rows, PAGE)),
            fresh_mask[None],
        ],
        axis=0,
    )
    owners = jnp.concatenate([page_owner, own_request[None]], axis=0)
    keys = jnp.concatenate(
        [cache_k.reshape(page_count, PAGE, local_heads, DH), new_keys[None]], axis=0
    )
    values = jnp.concatenate(
        [cache_v.reshape(page_count, PAGE, local_heads, DH), new_values[None]], axis=0
    )
    everyone = lax.all_gather(queries, "seq", axis=0, tiled=True).reshape(
        request_total, span_rows, local_heads, DH
    )
    rows = everyone[jnp.maximum(owners, 0)]
    scores = jnp.einsum("bqhd,bkhd->bhqk", rows, keys, preferred_element_type=jnp.float32) * (
        DH ** (-0.5)
    )
    scores = jnp.where(mask[:, None], scores, NEGATIVE)
    m_block = jnp.max(scores, axis=-1)
    probs = jnp.where(mask[:, None], jnp.exp(scores - m_block[..., None]), 0.0)
    l_block = jnp.sum(probs, axis=-1)
    acc_block = jnp.einsum(
        "bhqk,bkhd->bqhd", probs.astype(jnp.bfloat16), values, preferred_element_type=jnp.float32
    )
    onehot = owners[:, None] == jnp.arange(request_total, dtype=jnp.int32)[None, :]
    m_local = jnp.max(jnp.where(onehot[:, :, None, None], m_block[:, None], NEGATIVE), axis=0)
    m_global = lax.pmax(m_local, "seq")
    factor = jnp.exp(m_block - m_global[jnp.maximum(owners, 0)])
    scaled_acc = acc_block * jnp.transpose(factor, (0, 2, 1))[..., None]
    scaled_l = jnp.transpose(l_block * factor, (0, 2, 1))
    packed_state = jnp.concatenate(
        [scaled_acc.reshape(owners.shape[0], span_rows, -1), scaled_l], axis=2
    )
    state_width = packed_state.shape[2]
    folded_state = jnp.einsum(
        "br,bx->rx",
        onehot.astype(jnp.float32),
        packed_state.reshape(owners.shape[0], -1),
        precision=lax.Precision.HIGHEST,
    ).reshape(request_total * span_rows, state_width)
    own_state = lax.psum_scatter(folded_state, "seq", scatter_dimension=0, tiled=True)
    acc_fin = own_state[:, : local_heads * DH].reshape(tok_rows, local_heads, DH)
    l_fin = own_state[:, local_heads * DH :]
    attention = (acc_fin / l_fin[:, :, None]).reshape(tok_rows, -1).astype(jnp.bfloat16)
    head_terms = jnp.dot(attention, w_out, preferred_element_type=jnp.float32)
    mid = hidden.astype(jnp.float32) + lax.psum(head_terms.astype(jnp.bfloat16), "tp").astype(
        jnp.float32
    )
    moe_in = (rms_rows(mid) * moe_gain).astype(jnp.bfloat16)
    logits = jnp.dot(moe_in.astype(jnp.float32), router, precision=lax.Precision.HIGHEST)
    chosen = jax.nn.sigmoid(jnp.take_along_axis(logits, expert_ids, axis=1))
    gates = chosen / jnp.sum(chosen, axis=1, keepdims=True)
    flat_ids = expert_ids.reshape(-1)
    onehot = (flat_ids[:, None] == jnp.arange(EXPERTS, dtype=jnp.int32)[None, :]).astype(jnp.int32)
    ranks = jnp.sum((jnp.cumsum(onehot, axis=0) - 1) * onehot, axis=1)
    target = (flat_ids * CAP + ranks).reshape(tok_rows, TOP)
    hits = target[:, :, None] == jnp.arange(EXPERTS * CAP, dtype=jnp.int32)[None, None, :]
    placing = jnp.any(hits, axis=1).astype(jnp.bfloat16)
    combining = jnp.sum(jnp.where(hits, gates[:, :, None], 0.0), axis=1)
    packed = jnp.einsum("te,td->ed", placing, moe_in, preferred_element_type=jnp.float32).astype(
        jnp.bfloat16
    )
    width = moe_in.shape[1]
    splits = max(1, seq_count // EXPERTS)
    per_device = w_gate_up.shape[0]
    outgoing = jnp.repeat(packed.reshape(EXPERTS, CAP, width), splits, axis=0).reshape(
        seq_count, per_device, CAP, width
    )
    received = lax.all_to_all(outgoing, "seq", split_axis=0, concat_axis=0, tiled=True)
    count = received.shape[2]
    rows = received[:, 0].reshape(-1, width)
    gate = jnp.dot(rows, w_gate_up[0, 0], preferred_element_type=jnp.float32)
    upper = jnp.dot(rows, w_gate_up[0, 1], preferred_element_type=jnp.float32)
    inner = (jax.nn.gelu(gate, approximate=True) * upper).astype(jnp.bfloat16)
    results = [
        jnp.dot(inner, w_down[0], preferred_element_type=jnp.float32).reshape(
            seq_count, count, width
        )
    ]
    produced = jnp.stack(results, axis=1)
    returned = lax.all_to_all(
        produced.astype(jnp.bfloat16), "seq", split_axis=0, concat_axis=0, tiled=True
    ).astype(produced.dtype)
    columns = returned.shape[3]
    folded = jnp.sum(returned.reshape(EXPERTS, splits, CAP, columns), axis=1).reshape(
        EXPERTS * CAP, columns
    )
    mixture = jnp.dot(combining, folded, precision=lax.Precision.HIGHEST)
    tp_width = width // lax.axis_size("tp")
    mid_part = lax.dynamic_slice_in_dim(mid, lax.axis_index("tp") * tp_width, tp_width, 1)
    moe_part = lax.psum_scatter(
        mixture.astype(jnp.bfloat16), "tp", scatter_dimension=1, tiled=True
    ).astype(jnp.float32)
    return (mid_part + moe_part).astype(jnp.bfloat16)


def solution(mesh):
    in_specs = (
        P("seq", None),
        P(),
        P(),
        P("seq", None),
        P(None, "tp"),
        P(None, "tp"),
        P(None, "tp"),
        P("tp", None),
        P("seq", None, "tp"),
        P("seq", None, "tp"),
        P(),
        P(),
        P("seq", None, None, "tp"),
        P("seq", "tp", None),
    )
    out_specs = P("seq", "tp")
    return jax.shard_map(shards, mesh=mesh, in_specs=in_specs, out_specs=out_specs, check_vma=False)
```

```python
import jax
import jax.numpy as jnp
from jax import lax
from jax.sharding import PartitionSpec as P

DH = 64
EXPERTS = 32
TOP = 2
PAGE = 128
MAXP = 256
SPAN_DEVS = 4
CAP = 10


NEGATIVE = -1e30


def passed_along(value, axis, steps):
    count = lax.axis_size(axis)
    pairs = [(source, (source + steps) % count) for source in range(count)]
    return lax.ppermute(value, axis, pairs)


def rms_rows(values):
    return values * lax.rsqrt(jnp.mean(values * values, axis=-1, keepdims=True) + 1e-06)


def online_update(state, queries, keys, values, mask):
    m_old, l_old, accum = state
    scale = queries.shape[2] ** (-0.5)
    scores = jnp.einsum("nhd,khd->hnk", queries, keys, preferred_element_type=jnp.float32) * scale
    scores = jnp.where(mask[None], scores, NEGATIVE)
    m_new = jnp.maximum(m_old, jnp.max(scores, axis=-1).T)
    probs = jnp.where(mask[None], jnp.exp(scores - m_new.T[:, :, None]), 0.0)
    factor = jnp.exp(m_old - m_new)
    l_new = l_old * factor + jnp.sum(probs, axis=-1).T
    weighted = jnp.einsum(
        "hnk,khd->nhd", probs.astype(jnp.bfloat16), values, preferred_element_type=jnp.float32
    )
    return (m_new, l_new, accum * factor[:, :, None] + weighted)


def shards(
    hidden,
    page_table,
    cache_len,
    expert_ids,
    w_query,
    w_key,
    w_value,
    w_out,
    cache_k,
    cache_v,
    moe_gain,
    router,
    w_gate_up,
    w_down,
):
    tok_rows = hidden.shape[0]
    span_rows = tok_rows * SPAN_DEVS
    seq_count = lax.axis_size("seq")
    seq_index = lax.axis_index("seq")
    local_heads = w_query.shape[1] // DH
    request_total = page_table.shape[0]
    normed = rms_rows(hidden.astype(jnp.float32)).astype(jnp.bfloat16)
    queries = jnp.dot(normed, w_query, preferred_element_type=jnp.float32).astype(jnp.bfloat16)
    new_keys = (
        jnp.dot(normed, w_key, preferred_element_type=jnp.float32)
        .astype(jnp.bfloat16)
        .reshape(tok_rows, local_heads, DH)
    )
    new_values = (
        jnp.dot(normed, w_value, preferred_element_type=jnp.float32)
        .astype(jnp.bfloat16)
        .reshape(tok_rows, local_heads, DH)
    )
    page_count = cache_k.shape[0]
    page_ids = seq_index * page_count + jnp.arange(page_count, dtype=jnp.int32)
    listing = page_table.reshape(-1)
    matches = listing[None, :] == page_ids[:, None]
    entry_index = jnp.arange(listing.shape[0], dtype=jnp.int32)
    found = jnp.sum(jnp.where(matches, entry_index[None, :] + 1, 0), axis=1) - 1
    page_owner = jnp.where(found >= 0, found // MAXP, -1)
    page_order = jnp.where(found >= 0, found % MAXP, 0)
    page_limit = jnp.where(found >= 0, cache_len[jnp.maximum(page_owner, 0)], 0)
    own_request = seq_index * tok_rows // span_rows
    own_offset = seq_index * tok_rows % span_rows
    slot_range = jnp.arange(PAGE, dtype=jnp.int32)
    page_valid = (found >= 0)[:, None] & (
        page_order[:, None] * PAGE + slot_range[None, :] < page_limit[:, None]
    )
    span_positions = jnp.arange(span_rows, dtype=jnp.int32)
    fresh_mask = span_positions[:, None] >= own_offset + jnp.arange(tok_rows, dtype=jnp.int32)[None, :]
    mask = jnp.concatenate(
        [
            jnp.broadcast_to(page_valid[:, None, :], (page_count, span_rows, PAGE)),
            fresh_mask[None],
        ],
        axis=0,
    )
    owners = jnp.concatenate([page_owner, own_request[None]], axis=0)
    keys = jnp.concatenate(
        [cache_k.reshape(page_count, PAGE, local_heads, DH), new_keys[None]], axis=0
    )
    values = jnp.concatenate(
        [cache_v.reshape(page_count, PAGE, local_heads, DH), new_values[None]], axis=0
    )
    everyone = lax.all_gather(queries, "seq", axis=0, tiled=True).reshape(
        request_total, span_rows, local_heads, DH
    )
    rows = everyone[jnp.maximum(owners, 0)]
    scores = jnp.einsum("bqhd,bkhd->bhqk", rows, keys, preferred_element_type=jnp.float32) * (
        DH ** (-0.5)
    )
    scores = jnp.where(mask[:, None], scores, NEGATIVE)
    m_block = jnp.max(scores, axis=-1)
    probs = jnp.where(mask[:, None], jnp.exp(scores - m_block[..., None]), 0.0)
    l_block = jnp.sum(probs, axis=-1)
    acc_block = jnp.einsum(
        "bhqk,bkhd->bhqd", probs.astype(jnp.bfloat16), values, preferred_element_type=jnp.float32
    )
    onehot = owners[:, None] == jnp.arange(request_total, dtype=jnp.int32)[None, :]
    m_local = jnp.max(jnp.where(onehot[:, :, None, None], m_block[:, None], NEGATIVE), axis=0)
    factor = jnp.exp(m_block - m_local[jnp.maximum(owners, 0)])
    weights = onehot.astype(jnp.float32)
    acc_req = jnp.einsum(
        "br,bhqd->rhqd",
        weights,
        acc_block * factor[..., None],
        precision=lax.Precision.HIGHEST,
    )
    l_req = jnp.einsum("br,bhq->rhq", weights, l_block * factor, precision=lax.Precision.HIGHEST)
    quarters = span_rows // tok_rows
    acc_req = jnp.transpose(
        acc_req.reshape(request_total, local_heads, quarters, tok_rows, DH), (0, 2, 1, 3, 4)
    )
    stats = jnp.stack([m_local, l_req], axis=-1)
    stats = jnp.transpose(
        stats.reshape(request_total, local_heads, quarters, tok_rows, 2), (0, 2, 1, 3, 4)
    )
    bit_count = seq_count.bit_length() - 1
    acc_req = acc_req.reshape((2,) * bit_count + acc_req.shape[2:])
    stats = stats.reshape((2,) * bit_count + stats.shape[2:])
    remaining = list(range(bit_count - 1, -1, -1))
    for bit in ([0, 1, 3, 2, 4, 5] if bit_count == 6 else list(range(bit_count))):
        axis = remaining.index(bit)
        remaining.pop(axis)
        own_bit = (seq_index >> bit) & 1
        keep_acc = lax.dynamic_index_in_dim(acc_req, own_bit, axis, keepdims=False)
        send_acc = lax.dynamic_index_in_dim(acc_req, 1 - own_bit, axis, keepdims=False)
        keep_stats = lax.dynamic_index_in_dim(stats, own_bit, axis, keepdims=False)
        send_stats = lax.dynamic_index_in_dim(stats, 1 - own_bit, axis, keepdims=False)
        pairs = [(source, source ^ (1 << bit)) for source in range(seq_count)]
        got_acc = lax.ppermute(send_acc.astype(jnp.bfloat16), "seq", pairs).astype(jnp.float32)
        got_stats = lax.ppermute(send_stats, "seq", pairs)
        m_new = jnp.maximum(keep_stats[..., 0], got_stats[..., 0])
        keep_factor = jnp.exp(keep_stats[..., 0] - m_new)
        got_factor = jnp.exp(got_stats[..., 0] - m_new)
        l_new = keep_stats[..., 1] * keep_factor + got_stats[..., 1] * got_factor
        acc_req = keep_acc * keep_factor[..., None] + got_acc * got_factor[..., None]
        stats = jnp.stack([m_new, l_new], axis=-1)
    attention = jnp.transpose(acc_req / stats[..., 1:2], (1, 0, 2)).reshape(tok_rows, -1)
    attention = attention.astype(jnp.bfloat16)
    tp_count = lax.axis_size("tp")
    tp_index = lax.axis_index("tp")

    def tp_gather(value, axis):
        pieces = [value] + [
            lax.ppermute(value, "tp", [(i, (i + k) % tp_count) for i in range(tp_count)])
            for k in range(1, tp_count)
        ]
        stacked = jnp.stack(pieces, axis=0)
        ordered = jnp.take(stacked, (tp_index - jnp.arange(tp_count)) % tp_count, axis=0)
        return jnp.concatenate([ordered[j] for j in range(tp_count)], axis=axis)

    full_attention = tp_gather(attention, 1)
    full_w_out = tp_gather(w_out, 0)
    mid = hidden.astype(jnp.float32) + jnp.dot(
        full_attention, full_w_out, preferred_element_type=jnp.float32
    )
    moe_in = (rms_rows(mid) * moe_gain).astype(jnp.bfloat16)
    logits = jnp.dot(moe_in.astype(jnp.float32), router, precision=lax.Precision.HIGHEST)
    chosen = jax.nn.sigmoid(jnp.take_along_axis(logits, expert_ids, axis=1))
    gates = chosen / jnp.sum(chosen, axis=1, keepdims=True)
    flat_ids = expert_ids.reshape(-1)
    onehot = (flat_ids[:, None] == jnp.arange(EXPERTS, dtype=jnp.int32)[None, :]).astype(jnp.int32)
    ranks = jnp.sum((jnp.cumsum(onehot, axis=0) - 1) * onehot, axis=1)
    target = (flat_ids * CAP + ranks).reshape(tok_rows, TOP)
    hits = target[:, :, None] == jnp.arange(EXPERTS * CAP, dtype=jnp.int32)[None, None, :]
    placing = jnp.any(hits, axis=1).astype(jnp.bfloat16)
    combining = jnp.sum(jnp.where(hits, gates[:, :, None], 0.0), axis=1)
    packed = jnp.einsum("te,td->ed", placing, moe_in, preferred_element_type=jnp.float32).astype(
        jnp.bfloat16
    )
    width = moe_in.shape[1]
    splits = max(1, seq_count // EXPERTS)
    per_device = w_gate_up.shape[0]
    outgoing = jnp.repeat(packed.reshape(EXPERTS, CAP, width), splits, axis=0).reshape(
        seq_count, per_device, CAP, width
    )
    received = lax.all_to_all(outgoing, "seq", split_axis=0, concat_axis=0, tiled=True)
    count = received.shape[2]
    rows = received[:, 0].reshape(-1, width)
    gate = jnp.dot(rows, w_gate_up[0, 0], preferred_element_type=jnp.float32)
    upper = jnp.dot(rows, w_gate_up[0, 1], preferred_element_type=jnp.float32)
    inner = (jax.nn.gelu(gate, approximate=True) * upper).astype(jnp.bfloat16)
    results = [
        jnp.dot(inner, w_down[0], preferred_element_type=jnp.float32).reshape(
            seq_count, count, width
        )
    ]
    produced = jnp.stack(results, axis=1)
    returned = lax.all_to_all(
        produced.astype(jnp.bfloat16), "seq", split_axis=0, concat_axis=0, tiled=True
    ).astype(produced.dtype)
    columns = returned.shape[3]
    folded = jnp.sum(returned.reshape(EXPERTS, splits, CAP, columns), axis=1).reshape(
        EXPERTS * CAP, columns
    )
    mixture = jnp.dot(combining, folded, precision=lax.Precision.HIGHEST)
    tp_width = width // lax.axis_size("tp")
    mid_part = lax.dynamic_slice_in_dim(mid, lax.axis_index("tp") * tp_width, tp_width, 1)
    moe_part = lax.psum_scatter(
        mixture.astype(jnp.bfloat16), "tp", scatter_dimension=1, tiled=True
    ).astype(jnp.float32)
    return (mid_part + moe_part).astype(jnp.bfloat16)


def solution(mesh):
    in_specs = (
        P("seq", None),
        P(),
        P(),
        P("seq", None),
        P(None, "tp"),
        P(None, "tp"),
        P(None, "tp"),
        P("tp", None),
        P("seq", None, "tp"),
        P("seq", None, "tp"),
        P(),
        P(),
        P("seq", None, None, "tp"),
        P("seq", "tp", None),
    )
    out_specs = P("seq", "tp")
    return jax.shard_map(shards, mesh=mesh, in_specs=in_specs, out_specs=out_specs, check_vma=False)
```

```python
import jax
import jax.numpy as jnp
from jax import lax
from jax.sharding import PartitionSpec as P
from jax.experimental import pallas as pl
from jax.experimental.pallas import tpu as pltpu

DH = 64
EXPERTS = 32
TOP = 2
PAGE = 128
MAXP = 256
SPAN_DEVS = 4
CAP = 10


NEGATIVE = -1e30


def passed_along(value, axis, steps):
    count = lax.axis_size(axis)
    pairs = [(source, (source + steps) % count) for source in range(count)]
    return lax.ppermute(value, axis, pairs)


def rms_rows(values):
    return values * lax.rsqrt(jnp.mean(values * values, axis=-1, keepdims=True) + 1e-06)


def online_update(state, queries, keys, values, mask):
    m_old, l_old, accum = state
    scale = queries.shape[2] ** (-0.5)
    scores = jnp.einsum("nhd,khd->hnk", queries, keys, preferred_element_type=jnp.float32) * scale
    scores = jnp.where(mask[None], scores, NEGATIVE)
    m_new = jnp.maximum(m_old, jnp.max(scores, axis=-1).T)
    probs = jnp.where(mask[None], jnp.exp(scores - m_new.T[:, :, None]), 0.0)
    factor = jnp.exp(m_old - m_new)
    l_new = l_old * factor + jnp.sum(probs, axis=-1).T
    weighted = jnp.einsum(
        "hnk,khd->nhd", probs.astype(jnp.bfloat16), values, preferred_element_type=jnp.float32
    )
    return (m_new, l_new, accum * factor[:, :, None] + weighted)


def attend_kernel(
    own_ref, page_ref, limit_ref, offset_ref, fresh_ref,
    q_ref, k_ref, v_ref, nk_ref, nv_ref, acc_ref, m_ref, l_ref,
):
    step = pl.program_id(0)
    owner = own_ref[step]
    first = (step == 0) | (own_ref[jnp.maximum(step - 1, 0)] != owner)

    @pl.when(first)
    def _():
        acc_ref[...] = jnp.zeros(acc_ref.shape, acc_ref.dtype)
        m_ref[...] = jnp.full(m_ref.shape, NEGATIVE, m_ref.dtype)
        l_ref[...] = jnp.zeros(l_ref.shape, l_ref.dtype)

    is_fresh = fresh_ref[step] == 1
    keys = jnp.where(is_fresh, nk_ref[0], k_ref[0])
    vals = jnp.where(is_fresh, nv_ref[0], v_ref[0])
    rows, cols = q_ref.shape[1], keys.shape[0]
    q_pos = lax.broadcasted_iota(jnp.int32, (rows, cols), 0)
    k_pos = lax.broadcasted_iota(jnp.int32, (rows, cols), 1)
    valid = (k_pos < limit_ref[step]) & (q_pos >= offset_ref[step] + k_pos)
    for h in range(m_ref.shape[1]):
        lanes = slice(h * DH, (h + 1) * DH)
        s = lax.dot_general(
            q_ref[0, :, lanes], keys[:, lanes], (((1,), (1,)), ((), ())),
            preferred_element_type=jnp.float32,
        ) * (DH ** (-0.5))
        s = jnp.where(valid, s, NEGATIVE)
        m_prev = m_ref[0, h]
        m_cur = jnp.maximum(m_prev, jnp.max(s, axis=1, keepdims=True))
        p = jnp.where(valid, jnp.exp(s - m_cur), 0.0)
        alpha = jnp.exp(m_prev - m_cur)
        l_ref[0, h] = alpha * l_ref[0, h] + jnp.sum(p, axis=1, keepdims=True)
        pv = jnp.dot(p.astype(jnp.bfloat16), vals[:, lanes], preferred_element_type=jnp.float32)
        acc_ref[0, :, lanes] = alpha * acc_ref[0, :, lanes] + pv
        m_ref[0, h] = m_cur


def local_attention(
    owner, page, limit, offset, fresh, everyone, cache_k, cache_v, new_k, new_v, heads, requests
):
    span_rows, width = everyone.shape[1], everyone.shape[2]
    page_rows = cache_k.shape[1]
    blocks = owner.shape[0]
    by_owner = lambda b, own, pg, lim, off, fr: (own[b], 0, 0)
    by_page = lambda b, own, pg, lim, off, fr: (pg[b], 0, 0)
    fixed = lambda b, own, pg, lim, off, fr: (0, 0, 0)
    stat_map = lambda b, own, pg, lim, off, fr: (own[b], 0, 0, 0)
    grid_spec = pltpu.PrefetchScalarGridSpec(
        num_scalar_prefetch=5,
        grid=(blocks,),
        in_specs=[
            pl.BlockSpec((1, span_rows, width), by_owner),
            pl.BlockSpec((1, page_rows, width), by_page),
            pl.BlockSpec((1, page_rows, width), by_page),
            pl.BlockSpec((1, page_rows, width), fixed),
            pl.BlockSpec((1, page_rows, width), fixed),
        ],
        out_specs=[
            pl.BlockSpec((1, span_rows, width), by_owner),
            pl.BlockSpec((1, heads, span_rows, 1), stat_map),
            pl.BlockSpec((1, heads, span_rows, 1), stat_map),
        ],
    )
    return pl.pallas_call(
        attend_kernel,
        grid_spec=grid_spec,
        out_shape=[
            jax.ShapeDtypeStruct((requests, span_rows, width), jnp.float32),
            jax.ShapeDtypeStruct((requests, heads, span_rows, 1), jnp.float32),
            jax.ShapeDtypeStruct((requests, heads, span_rows, 1), jnp.float32),
        ],
        compiler_params=pltpu.CompilerParams(dimension_semantics=("arbitrary",)),
    )(owner, page, limit, offset, fresh, everyone, cache_k, cache_v, new_k, new_v)


def shards(
    hidden,
    page_table,
    cache_len,
    expert_ids,
    w_query,
    w_key,
    w_value,
    w_out,
    cache_k,
    cache_v,
    moe_gain,
    router,
    w_gate_up,
    w_down,
):
    tok_rows = hidden.shape[0]
    span_rows = tok_rows * SPAN_DEVS
    seq_count = lax.axis_size("seq")
    seq_index = lax.axis_index("seq")
    local_heads = w_query.shape[1] // DH
    request_total = page_table.shape[0]
    normed = rms_rows(hidden.astype(jnp.float32)).astype(jnp.bfloat16)
    queries = jnp.dot(normed, w_query, preferred_element_type=jnp.float32).astype(jnp.bfloat16)
    new_keys = (
        jnp.dot(normed, w_key, preferred_element_type=jnp.float32)
        .astype(jnp.bfloat16)
        .reshape(tok_rows, local_heads, DH)
    )
    new_values = (
        jnp.dot(normed, w_value, preferred_element_type=jnp.float32)
        .astype(jnp.bfloat16)
        .reshape(tok_rows, local_heads, DH)
    )
    page_count = cache_k.shape[0]
    page_ids = seq_index * page_count + jnp.arange(page_count, dtype=jnp.int32)
    listing = page_table.reshape(-1)
    matches = listing[None, :] == page_ids[:, None]
    entry_index = jnp.arange(listing.shape[0], dtype=jnp.int32)
    found = jnp.sum(jnp.where(matches, entry_index[None, :] + 1, 0), axis=1) - 1
    page_owner = jnp.where(found >= 0, found // MAXP, -1)
    page_order = jnp.where(found >= 0, found % MAXP, 0)
    page_limit = jnp.where(found >= 0, cache_len[jnp.maximum(page_owner, 0)], 0)
    own_request = seq_index * tok_rows // span_rows
    own_offset = seq_index * tok_rows % span_rows
    slot_range = jnp.arange(PAGE, dtype=jnp.int32)
    page_valid = (found >= 0)[:, None] & (
        page_order[:, None] * PAGE + slot_range[None, :] < page_limit[:, None]
    )
    block_total = page_count + 1
    owners = jnp.concatenate([jnp.maximum(page_owner, 0), own_request[None]], axis=0)
    key_limits = jnp.concatenate(
        [jnp.clip(page_limit - page_order * PAGE, 0, PAGE), jnp.full((1,), PAGE, jnp.int32)], axis=0
    )
    query_offsets = jnp.concatenate(
        [jnp.full((page_count,), -span_rows - PAGE, jnp.int32), own_offset[None]], axis=0
    )
    block_order = jnp.argsort(owners, stable=True).astype(jnp.int32)
    sorted_owner = owners[block_order]
    sorted_limit = key_limits[block_order]
    sorted_offset = query_offsets[block_order]
    sorted_fresh = (block_order == page_count).astype(jnp.int32)
    sorted_page = jnp.minimum(block_order, page_count - 1)
    everyone = lax.all_gather(queries, "seq", axis=0, tiled=True).reshape(
        request_total, span_rows, local_heads * DH
    )
    width_heads = local_heads * DH
    acc_out, m_out, l_out = local_attention(
        sorted_owner,
        sorted_page,
        sorted_limit,
        sorted_offset,
        sorted_fresh,
        everyone,
        cache_k,
        cache_v,
        new_keys.reshape(1, tok_rows, width_heads),
        new_values.reshape(1, tok_rows, width_heads),
        local_heads,
        request_total,
    )
    visited = jnp.any(
        sorted_owner[:, None] == jnp.arange(request_total, dtype=jnp.int32)[None, :], axis=0
    )
    acc_req = jnp.where(visited[:, None, None], acc_out, 0.0)
    m_req = jnp.where(visited[:, None, None, None], m_out, NEGATIVE)
    l_req = jnp.where(visited[:, None, None, None], l_out, 0.0)
    quarters = span_rows // tok_rows
    stats = jnp.stack([m_req[..., 0], l_req[..., 0]], axis=-1)
    stats = jnp.transpose(
        stats.reshape(request_total, local_heads, quarters, tok_rows, 2), (0, 2, 3, 1, 4)
    )
    bit_count = seq_count.bit_length() - 1
    acc_req = acc_req.reshape((2,) * bit_count + (tok_rows, width_heads))
    stats = stats.reshape((2,) * bit_count + stats.shape[2:])
    remaining = list(range(bit_count - 1, -1, -1))
    for bit in ([0, 1, 3, 2, 4, 5] if bit_count == 6 else list(range(bit_count))):
        axis = remaining.index(bit)
        remaining.pop(axis)
        own_bit = (seq_index >> bit) & 1
        keep_acc = lax.dynamic_index_in_dim(acc_req, own_bit, axis, keepdims=False)
        send_acc = lax.dynamic_index_in_dim(acc_req, 1 - own_bit, axis, keepdims=False)
        keep_stats = lax.dynamic_index_in_dim(stats, own_bit, axis, keepdims=False)
        send_stats = lax.dynamic_index_in_dim(stats, 1 - own_bit, axis, keepdims=False)
        pairs = [(source, source ^ (1 << bit)) for source in range(seq_count)]
        got_acc = lax.ppermute(send_acc.astype(jnp.bfloat16), "seq", pairs).astype(jnp.float32)
        got_stats = lax.ppermute(send_stats, "seq", pairs)
        m_new = jnp.maximum(keep_stats[..., 0], got_stats[..., 0])
        keep_factor = jnp.exp(keep_stats[..., 0] - m_new)
        got_factor = jnp.exp(got_stats[..., 0] - m_new)
        l_new = keep_stats[..., 1] * keep_factor + got_stats[..., 1] * got_factor
        split_shape = keep_acc.shape[:-1] + (local_heads, DH)
        acc_req = (
            keep_acc.reshape(split_shape) * keep_factor[..., None]
            + got_acc.reshape(split_shape) * got_factor[..., None]
        ).reshape(keep_acc.shape)
        stats = jnp.stack([m_new, l_new], axis=-1)
    attention = (
        acc_req.reshape(tok_rows, local_heads, DH) / stats[..., 1][..., None]
    ).reshape(tok_rows, -1)
    attention = attention.astype(jnp.bfloat16)
    tp_count = lax.axis_size("tp")
    tp_index = lax.axis_index("tp")

    def tp_gather(value, axis):
        pieces = [value] + [
            lax.ppermute(value, "tp", [(i, (i + k) % tp_count) for i in range(tp_count)])
            for k in range(1, tp_count)
        ]
        stacked = jnp.stack(pieces, axis=0)
        ordered = jnp.take(stacked, (tp_index - jnp.arange(tp_count)) % tp_count, axis=0)
        return jnp.concatenate([ordered[j] for j in range(tp_count)], axis=axis)

    full_attention = tp_gather(attention, 1)
    full_w_out = tp_gather(w_out, 0)
    mid = hidden.astype(jnp.float32) + jnp.dot(
        full_attention, full_w_out, preferred_element_type=jnp.float32
    )
    moe_in = (rms_rows(mid) * moe_gain).astype(jnp.bfloat16)
    logits = jnp.dot(moe_in.astype(jnp.float32), router, precision=lax.Precision.HIGHEST)
    chosen = jax.nn.sigmoid(jnp.take_along_axis(logits, expert_ids, axis=1))
    gates = chosen / jnp.sum(chosen, axis=1, keepdims=True)
    flat_ids = expert_ids.reshape(-1)
    onehot = (flat_ids[:, None] == jnp.arange(EXPERTS, dtype=jnp.int32)[None, :]).astype(jnp.int32)
    ranks = jnp.sum((jnp.cumsum(onehot, axis=0) - 1) * onehot, axis=1)
    target = (flat_ids * CAP + ranks).reshape(tok_rows, TOP)
    hits = target[:, :, None] == jnp.arange(EXPERTS * CAP, dtype=jnp.int32)[None, None, :]
    placing = jnp.any(hits, axis=1).astype(jnp.bfloat16)
    combining = jnp.sum(jnp.where(hits, gates[:, :, None], 0.0), axis=1)
    packed = jnp.einsum("te,td->ed", placing, moe_in, preferred_element_type=jnp.float32).astype(
        jnp.bfloat16
    )
    width = moe_in.shape[1]
    splits = max(1, seq_count // EXPERTS)
    per_device = w_gate_up.shape[0]
    outgoing = jnp.repeat(packed.reshape(EXPERTS, CAP, width), splits, axis=0).reshape(
        seq_count, per_device, CAP, width
    )
    received = lax.all_to_all(outgoing, "seq", split_axis=0, concat_axis=0, tiled=True)
    count = received.shape[2]
    rows = received[:, 0].reshape(-1, width)
    gate = jnp.dot(rows, w_gate_up[0, 0], preferred_element_type=jnp.float32)
    upper = jnp.dot(rows, w_gate_up[0, 1], preferred_element_type=jnp.float32)
    inner = (jax.nn.gelu(gate, approximate=True) * upper).astype(jnp.bfloat16)
    results = [
        jnp.dot(inner, w_down[0], preferred_element_type=jnp.float32).reshape(
            seq_count, count, width
        )
    ]
    produced = jnp.stack(results, axis=1)
    returned = lax.all_to_all(
        produced.astype(jnp.bfloat16), "seq", split_axis=0, concat_axis=0, tiled=True
    ).astype(produced.dtype)
    columns = returned.shape[3]
    folded = jnp.sum(returned.reshape(EXPERTS, splits, CAP, columns), axis=1).reshape(
        EXPERTS * CAP, columns
    )
    mixture = jnp.dot(combining, folded, precision=lax.Precision.HIGHEST)
    tp_width = width // lax.axis_size("tp")
    mid_part = lax.dynamic_slice_in_dim(mid, lax.axis_index("tp") * tp_width, tp_width, 1)
    moe_part = lax.psum_scatter(
        mixture.astype(jnp.bfloat16), "tp", scatter_dimension=1, tiled=True
    ).astype(jnp.float32)
    return (mid_part + moe_part).astype(jnp.bfloat16)


def solution(mesh):
    in_specs = (
        P("seq", None),
        P(),
        P(),
        P("seq", None),
        P(None, "tp"),
        P(None, "tp"),
        P(None, "tp"),
        P("tp", None),
        P("seq", None, "tp"),
        P("seq", None, "tp"),
        P(),
        P(),
        P("seq", None, None, "tp"),
        P("seq", "tp", None),
    )
    out_specs = P("seq", "tp")
    return jax.shard_map(shards, mesh=mesh, in_specs=in_specs, out_specs=out_specs, check_vma=False)
```

```python
import jax
import jax.numpy as jnp
from jax import lax
from jax.sharding import PartitionSpec as P
from jax.experimental import pallas as pl
from jax.experimental.pallas import tpu as pltpu

DH = 64
EXPERTS = 32
TOP = 2
PAGE = 128
MAXP = 256
SPAN_DEVS = 4
CAP = 10


NEGATIVE = -1e30


def passed_along(value, axis, steps):
    count = lax.axis_size(axis)
    pairs = [(source, (source + steps) % count) for source in range(count)]
    return lax.ppermute(value, axis, pairs)


def rms_rows(values):
    return values * lax.rsqrt(jnp.mean(values * values, axis=-1, keepdims=True) + 1e-06)


def online_update(state, queries, keys, values, mask):
    m_old, l_old, accum = state
    scale = queries.shape[2] ** (-0.5)
    scores = jnp.einsum("nhd,khd->hnk", queries, keys, preferred_element_type=jnp.float32) * scale
    scores = jnp.where(mask[None], scores, NEGATIVE)
    m_new = jnp.maximum(m_old, jnp.max(scores, axis=-1).T)
    probs = jnp.where(mask[None], jnp.exp(scores - m_new.T[:, :, None]), 0.0)
    factor = jnp.exp(m_old - m_new)
    l_new = l_old * factor + jnp.sum(probs, axis=-1).T
    weighted = jnp.einsum(
        "hnk,khd->nhd", probs.astype(jnp.bfloat16), values, preferred_element_type=jnp.float32
    )
    return (m_new, l_new, accum * factor[:, :, None] + weighted)


def attend_kernel(
    own_ref, page_ref, limit_ref, offset_ref, fresh_ref,
    q_ref, k_ref, v_ref, nk_ref, nv_ref, acc_ref, stat_ref,
):
    step = pl.program_id(0)
    owner = own_ref[step]
    first = (step == 0) | (own_ref[jnp.maximum(step - 1, 0)] != owner)
    heads = acc_ref.shape[1]

    @pl.when(first)
    def _():
        acc_ref[...] = jnp.zeros(acc_ref.shape, acc_ref.dtype)
        stat_ref[0, :heads, :] = jnp.full((heads, stat_ref.shape[2]), NEGATIVE, jnp.float32)
        stat_ref[0, heads:, :] = jnp.zeros((heads, stat_ref.shape[2]), jnp.float32)

    is_fresh = fresh_ref[step] == 1
    keys = jnp.where(is_fresh, nk_ref[0], k_ref[0])
    vals = jnp.where(is_fresh, nv_ref[0], v_ref[0])
    rows, cols = keys.shape[0], q_ref.shape[1]
    k_pos = lax.broadcasted_iota(jnp.int32, (rows, cols), 0)
    q_pos = lax.broadcasted_iota(jnp.int32, (rows, cols), 1)
    valid = (k_pos < limit_ref[step]) & (q_pos >= offset_ref[step] + k_pos)
    for h in range(heads):
        lanes = slice(h * DH, (h + 1) * DH)
        s = lax.dot_general(
            keys[:, lanes], q_ref[0, :, lanes], (((1,), (1,)), ((), ())),
            preferred_element_type=jnp.float32,
        ) * (DH ** (-0.5))
        s = jnp.where(valid, s, NEGATIVE)
        m_prev = stat_ref[0, h : h + 1, :]
        m_cur = jnp.maximum(m_prev, jnp.max(s, axis=0, keepdims=True))
        p = jnp.where(valid, jnp.exp(s - m_cur), 0.0)
        alpha = jnp.exp(m_prev - m_cur)
        stat_ref[0, heads + h : heads + h + 1, :] = alpha * stat_ref[
            0, heads + h : heads + h + 1, :
        ] + jnp.sum(p, axis=0, keepdims=True)
        pv = lax.dot_general(
            vals[:, lanes], p.astype(jnp.bfloat16), (((0,), (0,)), ((), ())),
            preferred_element_type=jnp.float32,
        )
        acc_ref[0, h] = alpha * acc_ref[0, h] + pv
        stat_ref[0, h : h + 1, :] = m_cur


def local_attention(
    owner, page, limit, offset, fresh, everyone, cache_k, cache_v, new_k, new_v, heads, requests
):
    span_rows, width = everyone.shape[1], everyone.shape[2]
    page_rows = cache_k.shape[1]
    blocks = owner.shape[0]
    by_owner = lambda b, own, pg, lim, off, fr: (own[b], 0, 0)
    by_page = lambda b, own, pg, lim, off, fr: (pg[b], 0, 0)
    fixed = lambda b, own, pg, lim, off, fr: (0, 0, 0)
    acc_map = lambda b, own, pg, lim, off, fr: (own[b], 0, 0, 0)
    grid_spec = pltpu.PrefetchScalarGridSpec(
        num_scalar_prefetch=5,
        grid=(blocks,),
        in_specs=[
            pl.BlockSpec((1, span_rows, width), by_owner),
            pl.BlockSpec((1, page_rows, width), by_page),
            pl.BlockSpec((1, page_rows, width), by_page),
            pl.BlockSpec((1, page_rows, width), fixed),
            pl.BlockSpec((1, page_rows, width), fixed),
        ],
        out_specs=[
            pl.BlockSpec((1, heads, DH, span_rows), acc_map),
            pl.BlockSpec((1, 2 * heads, span_rows), by_owner),
        ],
    )
    return pl.pallas_call(
        attend_kernel,
        grid_spec=grid_spec,
        out_shape=[
            jax.ShapeDtypeStruct((requests, heads, DH, span_rows), jnp.float32),
            jax.ShapeDtypeStruct((requests, 2 * heads, span_rows), jnp.float32),
        ],
        compiler_params=pltpu.CompilerParams(dimension_semantics=("arbitrary",)),
    )(owner, page, limit, offset, fresh, everyone, cache_k, cache_v, new_k, new_v)


def shards(
    hidden,
    page_table,
    cache_len,
    expert_ids,
    w_query,
    w_key,
    w_value,
    w_out,
    cache_k,
    cache_v,
    moe_gain,
    router,
    w_gate_up,
    w_down,
):
    tok_rows = hidden.shape[0]
    span_rows = tok_rows * SPAN_DEVS
    seq_count = lax.axis_size("seq")
    seq_index = lax.axis_index("seq")
    local_heads = w_query.shape[1] // DH
    request_total = page_table.shape[0]
    normed = rms_rows(hidden.astype(jnp.float32)).astype(jnp.bfloat16)
    queries = jnp.dot(normed, w_query, preferred_element_type=jnp.float32).astype(jnp.bfloat16)
    new_keys = (
        jnp.dot(normed, w_key, preferred_element_type=jnp.float32)
        .astype(jnp.bfloat16)
        .reshape(tok_rows, local_heads, DH)
    )
    new_values = (
        jnp.dot(normed, w_value, preferred_element_type=jnp.float32)
        .astype(jnp.bfloat16)
        .reshape(tok_rows, local_heads, DH)
    )
    page_count = cache_k.shape[0]
    page_ids = seq_index * page_count + jnp.arange(page_count, dtype=jnp.int32)
    listing = page_table.reshape(-1)
    matches = listing[None, :] == page_ids[:, None]
    entry_index = jnp.arange(listing.shape[0], dtype=jnp.int32)
    found = jnp.sum(jnp.where(matches, entry_index[None, :] + 1, 0), axis=1) - 1
    page_owner = jnp.where(found >= 0, found // MAXP, -1)
    page_order = jnp.where(found >= 0, found % MAXP, 0)
    page_limit = jnp.where(found >= 0, cache_len[jnp.maximum(page_owner, 0)], 0)
    own_request = seq_index * tok_rows // span_rows
    own_offset = seq_index * tok_rows % span_rows
    slot_range = jnp.arange(PAGE, dtype=jnp.int32)
    page_valid = (found >= 0)[:, None] & (
        page_order[:, None] * PAGE + slot_range[None, :] < page_limit[:, None]
    )
    block_total = page_count + 1
    owners = jnp.concatenate([jnp.maximum(page_owner, 0), own_request[None]], axis=0)
    key_limits = jnp.concatenate(
        [jnp.clip(page_limit - page_order * PAGE, 0, PAGE), jnp.full((1,), PAGE, jnp.int32)], axis=0
    )
    query_offsets = jnp.concatenate(
        [jnp.full((page_count,), -span_rows - PAGE, jnp.int32), own_offset[None]], axis=0
    )
    block_order = jnp.argsort(owners, stable=True).astype(jnp.int32)
    sorted_owner = owners[block_order]
    sorted_limit = key_limits[block_order]
    sorted_offset = query_offsets[block_order]
    sorted_fresh = (block_order == page_count).astype(jnp.int32)
    sorted_page = jnp.minimum(block_order, page_count - 1)
    everyone = lax.all_gather(queries, "seq", axis=0, tiled=True).reshape(
        request_total, span_rows, local_heads * DH
    )
    width_heads = local_heads * DH
    acc_out, stat_out = local_attention(
        sorted_owner,
        sorted_page,
        sorted_limit,
        sorted_offset,
        sorted_fresh,
        everyone,
        cache_k,
        cache_v,
        new_keys.reshape(1, tok_rows, width_heads),
        new_values.reshape(1, tok_rows, width_heads),
        local_heads,
        request_total,
    )
    visited = jnp.any(
        sorted_owner[:, None] == jnp.arange(request_total, dtype=jnp.int32)[None, :], axis=0
    )
    stat_init = jnp.where(jnp.arange(2 * local_heads) < local_heads, NEGATIVE, 0.0)
    acc_req = jnp.where(visited[:, None, None, None], acc_out, 0.0)
    stats = jnp.where(visited[:, None, None], stat_out, stat_init[None, :, None])
    quarters = span_rows // tok_rows
    quarter_bits = quarters.bit_length() - 1
    request_bits = request_total.bit_length() - 1
    acc_req = acc_req.reshape(
        (2,) * request_bits + (local_heads, DH) + (2,) * quarter_bits + (tok_rows,)
    )
    stats = stats.reshape((2,) * request_bits + (2 * local_heads,) + (2,) * quarter_bits + (tok_rows,))
    bit_names = [quarter_bits + k for k in range(request_bits - 1, -1, -1)]
    bit_names += list(range(quarter_bits - 1, -1, -1))
    acc_names = bit_names[:request_bits] + ["h", "d"] + bit_names[request_bits:] + ["q"]
    stat_names = bit_names[:request_bits] + ["s"] + bit_names[request_bits:] + ["q"]
    bit_count = request_bits + quarter_bits
    for bit in ([0, 1, 3, 2, 4, 5] if bit_count == 6 else list(range(bit_count))):
        acc_axis = acc_names.index(bit)
        stat_axis = stat_names.index(bit)
        acc_names.pop(acc_axis)
        stat_names.pop(stat_axis)
        own_bit = (seq_index >> bit) & 1
        keep_acc = lax.dynamic_index_in_dim(acc_req, own_bit, acc_axis, keepdims=False)
        send_acc = lax.dynamic_index_in_dim(acc_req, 1 - own_bit, acc_axis, keepdims=False)
        keep_stats = lax.dynamic_index_in_dim(stats, own_bit, stat_axis, keepdims=False)
        send_stats = lax.dynamic_index_in_dim(stats, 1 - own_bit, stat_axis, keepdims=False)
        pairs = [(source, source ^ (1 << bit)) for source in range(seq_count)]
        got_acc = lax.ppermute(send_acc.astype(jnp.bfloat16), "seq", pairs).astype(jnp.float32)
        got_stats = lax.ppermute(send_stats, "seq", pairs)
        s_axis = stat_names.index("s")
        keep_m = lax.slice_in_dim(keep_stats, 0, local_heads, axis=s_axis)
        keep_l = lax.slice_in_dim(keep_stats, local_heads, 2 * local_heads, axis=s_axis)
        got_m = lax.slice_in_dim(got_stats, 0, local_heads, axis=s_axis)
        got_l = lax.slice_in_dim(got_stats, local_heads, 2 * local_heads, axis=s_axis)
        m_new = jnp.maximum(keep_m, got_m)
        keep_factor = jnp.exp(keep_m - m_new)
        got_factor = jnp.exp(got_m - m_new)
        l_new = keep_l * keep_factor + got_l * got_factor
        d_axis = acc_names.index("d")
        acc_req = keep_acc * jnp.expand_dims(keep_factor, d_axis) + got_acc * jnp.expand_dims(
            got_factor, d_axis
        )
        stats = jnp.concatenate([m_new, l_new], axis=s_axis)
    attention = acc_req / stats[local_heads:][:, None, :]
    attention = jnp.transpose(attention, (2, 0, 1)).reshape(tok_rows, -1).astype(jnp.bfloat16)
    tp_count = lax.axis_size("tp")
    tp_index = lax.axis_index("tp")

    def tp_gather(value, axis):
        pieces = [value] + [
            lax.ppermute(value, "tp", [(i, (i + k) % tp_count) for i in range(tp_count)])
            for k in range(1, tp_count)
        ]
        stacked = jnp.stack(pieces, axis=0)
        ordered = jnp.take(stacked, (tp_index - jnp.arange(tp_count)) % tp_count, axis=0)
        return jnp.concatenate([ordered[j] for j in range(tp_count)], axis=axis)

    full_attention = tp_gather(attention, 1)
    full_w_out = tp_gather(w_out, 0)
    mid = hidden.astype(jnp.float32) + jnp.dot(
        full_attention, full_w_out, preferred_element_type=jnp.float32
    )
    moe_in = (rms_rows(mid) * moe_gain).astype(jnp.bfloat16)
    logits = jnp.dot(moe_in.astype(jnp.float32), router, precision=lax.Precision.HIGHEST)
    chosen = jax.nn.sigmoid(jnp.take_along_axis(logits, expert_ids, axis=1))
    gates = chosen / jnp.sum(chosen, axis=1, keepdims=True)
    flat_ids = expert_ids.reshape(-1)
    onehot = (flat_ids[:, None] == jnp.arange(EXPERTS, dtype=jnp.int32)[None, :]).astype(jnp.int32)
    ranks = jnp.sum((jnp.cumsum(onehot, axis=0) - 1) * onehot, axis=1)
    target = (flat_ids * CAP + ranks).reshape(tok_rows, TOP)
    hits = target[:, :, None] == jnp.arange(EXPERTS * CAP, dtype=jnp.int32)[None, None, :]
    placing = jnp.any(hits, axis=1).astype(jnp.bfloat16)
    combining = jnp.sum(jnp.where(hits, gates[:, :, None], 0.0), axis=1)
    packed = jnp.einsum("te,td->ed", placing, moe_in, preferred_element_type=jnp.float32).astype(
        jnp.bfloat16
    )
    width = moe_in.shape[1]
    splits = max(1, seq_count // EXPERTS)
    per_device = w_gate_up.shape[0]
    outgoing = jnp.repeat(packed.reshape(EXPERTS, CAP, width), splits, axis=0).reshape(
        seq_count, per_device, CAP, width
    )
    received = lax.all_to_all(outgoing, "seq", split_axis=0, concat_axis=0, tiled=True)
    count = received.shape[2]
    rows = received[:, 0].reshape(-1, width)
    gate = jnp.dot(rows, w_gate_up[0, 0], preferred_element_type=jnp.float32)
    upper = jnp.dot(rows, w_gate_up[0, 1], preferred_element_type=jnp.float32)
    inner = (jax.nn.gelu(gate, approximate=True) * upper).astype(jnp.bfloat16)
    results = [
        jnp.dot(inner, w_down[0], preferred_element_type=jnp.float32).reshape(
            seq_count, count, width
        )
    ]
    produced = jnp.stack(results, axis=1)
    returned = lax.all_to_all(
        produced.astype(jnp.bfloat16), "seq", split_axis=0, concat_axis=0, tiled=True
    ).astype(produced.dtype)
    columns = returned.shape[3]
    folded = jnp.sum(returned.reshape(EXPERTS, splits, CAP, columns), axis=1).reshape(
        EXPERTS * CAP, columns
    )
    mixture = jnp.dot(combining, folded, precision=lax.Precision.HIGHEST)
    tp_width = width // lax.axis_size("tp")
    mid_part = lax.dynamic_slice_in_dim(mid, lax.axis_index("tp") * tp_width, tp_width, 1)
    moe_part = lax.psum_scatter(
        mixture.astype(jnp.bfloat16), "tp", scatter_dimension=1, tiled=True
    ).astype(jnp.float32)
    return (mid_part + moe_part).astype(jnp.bfloat16)


def solution(mesh):
    in_specs = (
        P("seq", None),
        P(),
        P(),
        P("seq", None),
        P(None, "tp"),
        P(None, "tp"),
        P(None, "tp"),
        P("tp", None),
        P("seq", None, "tp"),
        P("seq", None, "tp"),
        P(),
        P(),
        P("seq", None, None, "tp"),
        P("seq", "tp", None),
    )
    out_specs = P("seq", "tp")
    return jax.shard_map(shards, mesh=mesh, in_specs=in_specs, out_specs=out_specs, check_vma=False)
```

```python
import jax
import jax.numpy as jnp
from jax import lax
from jax.sharding import PartitionSpec as P
from jax.experimental import pallas as pl
from jax.experimental.pallas import tpu as pltpu

DH = 64
EXPERTS = 32
TOP = 2
PAGE = 128
MAXP = 256
SPAN_DEVS = 4
CAP = 10


NEGATIVE = -1e30


def passed_along(value, axis, steps):
    count = lax.axis_size(axis)
    pairs = [(source, (source + steps) % count) for source in range(count)]
    return lax.ppermute(value, axis, pairs)


def rms_rows(values):
    return values * lax.rsqrt(jnp.mean(values * values, axis=-1, keepdims=True) + 1e-06)


def online_update(state, queries, keys, values, mask):
    m_old, l_old, accum = state
    scale = queries.shape[2] ** (-0.5)
    scores = jnp.einsum("nhd,khd->hnk", queries, keys, preferred_element_type=jnp.float32) * scale
    scores = jnp.where(mask[None], scores, NEGATIVE)
    m_new = jnp.maximum(m_old, jnp.max(scores, axis=-1).T)
    probs = jnp.where(mask[None], jnp.exp(scores - m_new.T[:, :, None]), 0.0)
    factor = jnp.exp(m_old - m_new)
    l_new = l_old * factor + jnp.sum(probs, axis=-1).T
    weighted = jnp.einsum(
        "hnk,khd->nhd", probs.astype(jnp.bfloat16), values, preferred_element_type=jnp.float32
    )
    return (m_new, l_new, accum * factor[:, :, None] + weighted)


def attend_kernel(
    own_ref, page_ref, limit_ref, offset_ref, fresh_ref,
    q_ref, k_ref, v_ref, nk_ref, nv_ref, acc_ref, stat_ref,
):
    step = pl.program_id(0)
    owner = own_ref[step]
    first = (step == 0) | (own_ref[jnp.maximum(step - 1, 0)] != owner)
    heads = acc_ref.shape[1]

    @pl.when(first)
    def _():
        acc_ref[...] = jnp.zeros(acc_ref.shape, acc_ref.dtype)
        stat_ref[0, :heads, :] = jnp.full((heads, stat_ref.shape[2]), NEGATIVE, jnp.float32)
        stat_ref[0, heads:, :] = jnp.zeros((heads, stat_ref.shape[2]), jnp.float32)

    is_fresh = fresh_ref[step] == 1
    keys = jnp.where(is_fresh, nk_ref[0], k_ref[0])
    vals = jnp.where(is_fresh, nv_ref[0], v_ref[0])
    rows, cols = keys.shape[0], q_ref.shape[1]
    k_pos = lax.broadcasted_iota(jnp.int32, (rows, cols), 0)
    q_pos = lax.broadcasted_iota(jnp.int32, (rows, cols), 1)
    valid = (k_pos < limit_ref[step]) & (q_pos >= offset_ref[step] + k_pos)
    for h in range(heads):
        lanes = slice(h * DH, (h + 1) * DH)
        s = lax.dot_general(
            keys[:, lanes], q_ref[0, :, lanes], (((1,), (1,)), ((), ())),
            preferred_element_type=jnp.float32,
        ) * (DH ** (-0.5))
        s = jnp.where(valid, s, NEGATIVE)
        m_prev = stat_ref[0, h : h + 1, :]
        m_cur = jnp.maximum(m_prev, jnp.max(s, axis=0, keepdims=True))
        p = jnp.where(valid, jnp.exp(s - m_cur), 0.0)
        alpha = jnp.exp(m_prev - m_cur)
        stat_ref[0, heads + h : heads + h + 1, :] = alpha * stat_ref[
            0, heads + h : heads + h + 1, :
        ] + jnp.sum(p, axis=0, keepdims=True)
        pv = lax.dot_general(
            vals[:, lanes], p.astype(jnp.bfloat16), (((0,), (0,)), ((), ())),
            preferred_element_type=jnp.float32,
        )
        acc_ref[0, h] = alpha * acc_ref[0, h] + pv
        stat_ref[0, h : h + 1, :] = m_cur


def local_attention(
    owner, page, limit, offset, fresh, everyone, cache_k, cache_v, new_k, new_v, heads, requests
):
    span_rows, width = everyone.shape[1], everyone.shape[2]
    page_rows = cache_k.shape[1]
    blocks = owner.shape[0]
    by_owner = lambda b, own, pg, lim, off, fr: (own[b], 0, 0)
    by_page = lambda b, own, pg, lim, off, fr: (pg[b], 0, 0)
    fixed = lambda b, own, pg, lim, off, fr: (0, 0, 0)
    acc_map = lambda b, own, pg, lim, off, fr: (own[b], 0, 0, 0)
    grid_spec = pltpu.PrefetchScalarGridSpec(
        num_scalar_prefetch=5,
        grid=(blocks,),
        in_specs=[
            pl.BlockSpec((1, span_rows, width), by_owner),
            pl.BlockSpec((1, page_rows, width), by_page),
            pl.BlockSpec((1, page_rows, width), by_page),
            pl.BlockSpec((1, page_rows, width), fixed),
            pl.BlockSpec((1, page_rows, width), fixed),
        ],
        out_specs=[
            pl.BlockSpec((1, heads, DH, span_rows), acc_map),
            pl.BlockSpec((1, 2 * heads, span_rows), by_owner),
        ],
    )
    return pl.pallas_call(
        attend_kernel,
        grid_spec=grid_spec,
        out_shape=[
            jax.ShapeDtypeStruct((requests, heads, DH, span_rows), jnp.float32),
            jax.ShapeDtypeStruct((requests, 2 * heads, span_rows), jnp.float32),
        ],
        compiler_params=pltpu.CompilerParams(dimension_semantics=("arbitrary",)),
    )(owner, page, limit, offset, fresh, everyone, cache_k, cache_v, new_k, new_v)


def shards(
    hidden,
    page_table,
    cache_len,
    expert_ids,
    w_query,
    w_key,
    w_value,
    w_out,
    cache_k,
    cache_v,
    moe_gain,
    router,
    w_gate_up,
    w_down,
):
    tok_rows = hidden.shape[0]
    span_rows = tok_rows * SPAN_DEVS
    seq_count = lax.axis_size("seq")
    seq_index = lax.axis_index("seq")
    local_heads = w_query.shape[1] // DH
    request_total = page_table.shape[0]
    normed = rms_rows(hidden.astype(jnp.float32)).astype(jnp.bfloat16)
    queries = jnp.dot(normed, w_query, preferred_element_type=jnp.float32).astype(jnp.bfloat16)
    new_keys = (
        jnp.dot(normed, w_key, preferred_element_type=jnp.float32)
        .astype(jnp.bfloat16)
        .reshape(tok_rows, local_heads, DH)
    )
    new_values = (
        jnp.dot(normed, w_value, preferred_element_type=jnp.float32)
        .astype(jnp.bfloat16)
        .reshape(tok_rows, local_heads, DH)
    )
    page_count = cache_k.shape[0]
    page_ids = seq_index * page_count + jnp.arange(page_count, dtype=jnp.int32)
    listing = page_table.reshape(-1)
    matches = listing[None, :] == page_ids[:, None]
    entry_index = jnp.arange(listing.shape[0], dtype=jnp.int32)
    found = jnp.sum(jnp.where(matches, entry_index[None, :] + 1, 0), axis=1) - 1
    page_owner = jnp.where(found >= 0, found // MAXP, -1)
    page_order = jnp.where(found >= 0, found % MAXP, 0)
    page_limit = jnp.where(found >= 0, cache_len[jnp.maximum(page_owner, 0)], 0)
    own_request = seq_index * tok_rows // span_rows
    own_offset = seq_index * tok_rows % span_rows
    slot_range = jnp.arange(PAGE, dtype=jnp.int32)
    page_valid = (found >= 0)[:, None] & (
        page_order[:, None] * PAGE + slot_range[None, :] < page_limit[:, None]
    )
    block_total = page_count + 1
    owners = jnp.concatenate([jnp.maximum(page_owner, 0), own_request[None]], axis=0)
    key_limits = jnp.concatenate(
        [jnp.clip(page_limit - page_order * PAGE, 0, PAGE), jnp.full((1,), PAGE, jnp.int32)], axis=0
    )
    query_offsets = jnp.concatenate(
        [jnp.full((page_count,), -span_rows - PAGE, jnp.int32), own_offset[None]], axis=0
    )
    block_order = jnp.argsort(owners, stable=True).astype(jnp.int32)
    sorted_owner = owners[block_order]
    sorted_limit = key_limits[block_order]
    sorted_offset = query_offsets[block_order]
    sorted_fresh = (block_order == page_count).astype(jnp.int32)
    sorted_page = jnp.minimum(block_order, page_count - 1)
    everyone = lax.all_gather(queries, "seq", axis=0, tiled=True).reshape(
        request_total, span_rows, local_heads * DH
    )
    width_heads = local_heads * DH
    acc_out, stat_out = local_attention(
        sorted_owner,
        sorted_page,
        sorted_limit,
        sorted_offset,
        sorted_fresh,
        everyone,
        cache_k,
        cache_v,
        new_keys.reshape(1, tok_rows, width_heads),
        new_values.reshape(1, tok_rows, width_heads),
        local_heads,
        request_total,
    )
    visited = jnp.any(
        sorted_owner[:, None] == jnp.arange(request_total, dtype=jnp.int32)[None, :], axis=0
    )
    stat_init = jnp.where(jnp.arange(2 * local_heads) < local_heads, NEGATIVE, 0.0)
    acc_req = jnp.where(visited[:, None, None, None], acc_out, 0.0)
    stats = jnp.where(visited[:, None, None], stat_out, stat_init[None, :, None])
    quarters = span_rows // tok_rows
    quarter_bits = quarters.bit_length() - 1
    request_bits = request_total.bit_length() - 1
    acc_req = acc_req.reshape(
        (2,) * request_bits + (local_heads, DH) + (2,) * quarter_bits + (tok_rows,)
    )
    stats = stats.reshape((2,) * request_bits + (2 * local_heads,) + (2,) * quarter_bits + (tok_rows,))
    bit_names = [quarter_bits + k for k in range(request_bits - 1, -1, -1)]
    bit_names += list(range(quarter_bits - 1, -1, -1))
    acc_names = bit_names[:request_bits] + ["h", "d"] + bit_names[request_bits:] + ["q"]
    stat_names = bit_names[:request_bits] + ["s"] + bit_names[request_bits:] + ["q"]
    bit_count = request_bits + quarter_bits
    for bit in ([0, 1, 3, 2, 4, 5] if bit_count == 6 else list(range(bit_count))):
        acc_axis = acc_names.index(bit)
        stat_axis = stat_names.index(bit)
        acc_names.pop(acc_axis)
        stat_names.pop(stat_axis)
        own_bit = (seq_index >> bit) & 1
        keep_acc = lax.dynamic_index_in_dim(acc_req, own_bit, acc_axis, keepdims=False)
        send_acc = lax.dynamic_index_in_dim(acc_req, 1 - own_bit, acc_axis, keepdims=False)
        keep_stats = lax.dynamic_index_in_dim(stats, own_bit, stat_axis, keepdims=False)
        send_stats = lax.dynamic_index_in_dim(stats, 1 - own_bit, stat_axis, keepdims=False)
        pairs = [(source, source ^ (1 << bit)) for source in range(seq_count)]
        got_acc = lax.ppermute(send_acc.astype(jnp.bfloat16), "seq", pairs).astype(jnp.float32)
        got_stats = lax.ppermute(send_stats, "seq", pairs)
        s_axis = stat_names.index("s")
        keep_m = lax.slice_in_dim(keep_stats, 0, local_heads, axis=s_axis)
        keep_l = lax.slice_in_dim(keep_stats, local_heads, 2 * local_heads, axis=s_axis)
        got_m = lax.slice_in_dim(got_stats, 0, local_heads, axis=s_axis)
        got_l = lax.slice_in_dim(got_stats, local_heads, 2 * local_heads, axis=s_axis)
        m_new = jnp.maximum(keep_m, got_m)
        keep_factor = jnp.exp(keep_m - m_new)
        got_factor = jnp.exp(got_m - m_new)
        l_new = keep_l * keep_factor + got_l * got_factor
        d_axis = acc_names.index("d")
        acc_req = keep_acc * jnp.expand_dims(keep_factor, d_axis) + got_acc * jnp.expand_dims(
            got_factor, d_axis
        )
        stats = jnp.concatenate([m_new, l_new], axis=s_axis)
    attention = acc_req / stats[local_heads:][:, None, :]
    attention = jnp.transpose(attention, (2, 0, 1)).reshape(tok_rows, -1).astype(jnp.bfloat16)
    tp_count = lax.axis_size("tp")
    tp_index = lax.axis_index("tp")

    def tp_gather(value, axis):
        pieces = [value] + [
            lax.ppermute(value, "tp", [(i, (i + k) % tp_count) for i in range(tp_count)])
            for k in range(1, tp_count)
        ]
        stacked = jnp.stack(pieces, axis=0)
        ordered = jnp.take(stacked, (tp_index - jnp.arange(tp_count)) % tp_count, axis=0)
        return jnp.concatenate([ordered[j] for j in range(tp_count)], axis=axis)

    full_attention = tp_gather(attention, 1)
    full_w_out = tp_gather(w_out, 0)
    mid = hidden.astype(jnp.float32) + jnp.dot(
        full_attention, full_w_out, preferred_element_type=jnp.float32
    )
    moe_in = (rms_rows(mid) * moe_gain).astype(jnp.bfloat16)
    logits = jnp.dot(moe_in.astype(jnp.float32), router, precision=lax.Precision.HIGHEST)
    chosen = jax.nn.sigmoid(jnp.take_along_axis(logits, expert_ids, axis=1))
    gates = chosen / jnp.sum(chosen, axis=1, keepdims=True)
    flat_ids = expert_ids.reshape(-1)
    onehot = (flat_ids[:, None] == jnp.arange(EXPERTS, dtype=jnp.int32)[None, :]).astype(jnp.int32)
    ranks = jnp.sum((jnp.cumsum(onehot, axis=0) - 1) * onehot, axis=1)
    target = (flat_ids * CAP + ranks).reshape(tok_rows, TOP)
    hits = target[:, :, None] == jnp.arange(EXPERTS * CAP, dtype=jnp.int32)[None, None, :]
    placing = jnp.any(hits, axis=1).astype(jnp.bfloat16)
    combining = jnp.sum(jnp.where(hits, gates[:, :, None], 0.0), axis=1)
    width = moe_in.shape[1]
    tp_width = width // tp_count
    moe_cols = lax.dynamic_slice_in_dim(moe_in, tp_index * tp_width, tp_width, 1)
    packed = jnp.einsum(
        "te,td->ed", placing, moe_cols, preferred_element_type=jnp.float32
    ).astype(jnp.bfloat16)
    splits = max(1, seq_count // EXPERTS)
    per_device = w_gate_up.shape[0]
    outgoing = jnp.repeat(packed.reshape(EXPERTS, CAP, tp_width), splits, axis=0).reshape(
        seq_count, per_device, CAP, tp_width
    )
    received = lax.all_to_all(outgoing, "seq", split_axis=0, concat_axis=0, tiled=True)
    count = received.shape[2]
    rows = tp_gather(received[:, 0].reshape(-1, tp_width), 1)
    gate = jnp.dot(rows, w_gate_up[0, 0], preferred_element_type=jnp.float32)
    upper = jnp.dot(rows, w_gate_up[0, 1], preferred_element_type=jnp.float32)
    inner = (jax.nn.gelu(gate, approximate=True) * upper).astype(jnp.bfloat16)
    results = jnp.dot(inner, w_down[0], preferred_element_type=jnp.float32).astype(jnp.bfloat16)
    share = lax.dynamic_slice_in_dim(results, tp_index * tp_width, tp_width, 1).astype(
        jnp.float32
    )
    for k in range(1, tp_count):
        target_cols = lax.dynamic_slice_in_dim(
            results, ((tp_index + k) % tp_count) * tp_width, tp_width, 1
        )
        share = share + lax.ppermute(
            target_cols, "tp", [(i, (i + k) % tp_count) for i in range(tp_count)]
        ).astype(jnp.float32)
    produced = share.reshape(seq_count, 1, count, tp_width)
    returned = lax.all_to_all(
        produced.astype(jnp.bfloat16), "seq", split_axis=0, concat_axis=0, tiled=True
    ).astype(jnp.float32)
    folded = jnp.sum(returned.reshape(EXPERTS, splits, CAP, tp_width), axis=1).reshape(
        EXPERTS * CAP, tp_width
    )
    mixture = jnp.dot(combining, folded, precision=lax.Precision.HIGHEST)
    mid_part = lax.dynamic_slice_in_dim(mid, tp_index * tp_width, tp_width, 1)
    return (mid_part + mixture).astype(jnp.bfloat16)

def solution(mesh):
    in_specs = (
        P("seq", None),
        P(),
        P(),
        P("seq", None),
        P(None, "tp"),
        P(None, "tp"),
        P(None, "tp"),
        P("tp", None),
        P("seq", None, "tp"),
        P("seq", None, "tp"),
        P(),
        P(),
        P("seq", None, None, "tp"),
        P("seq", "tp", None),
    )
    out_specs = P("seq", "tp")
    return jax.shard_map(shards, mesh=mesh, in_specs=in_specs, out_specs=out_specs, check_vma=False)
```

```python
import jax
import jax.numpy as jnp
from jax import lax
from jax.sharding import PartitionSpec as P
from jax.experimental import pallas as pl
from jax.experimental.pallas import tpu as pltpu

DH = 64
EXPERTS = 32
TOP = 2
PAGE = 128
MAXP = 256
SPAN_DEVS = 4
CAP = 10


NEGATIVE = -1e30


def passed_along(value, axis, steps):
    count = lax.axis_size(axis)
    pairs = [(source, (source + steps) % count) for source in range(count)]
    return lax.ppermute(value, axis, pairs)


def rms_rows(values):
    return values * lax.rsqrt(jnp.mean(values * values, axis=-1, keepdims=True) + 1e-06)


def online_update(state, queries, keys, values, mask):
    m_old, l_old, accum = state
    scale = queries.shape[2] ** (-0.5)
    scores = jnp.einsum("nhd,khd->hnk", queries, keys, preferred_element_type=jnp.float32) * scale
    scores = jnp.where(mask[None], scores, NEGATIVE)
    m_new = jnp.maximum(m_old, jnp.max(scores, axis=-1).T)
    probs = jnp.where(mask[None], jnp.exp(scores - m_new.T[:, :, None]), 0.0)
    factor = jnp.exp(m_old - m_new)
    l_new = l_old * factor + jnp.sum(probs, axis=-1).T
    weighted = jnp.einsum(
        "hnk,khd->nhd", probs.astype(jnp.bfloat16), values, preferred_element_type=jnp.float32
    )
    return (m_new, l_new, accum * factor[:, :, None] + weighted)


def attend_kernel(
    own_ref, page_ref, limit_ref, offset_ref, fresh_ref,
    q_ref, k_ref, v_ref, nk_ref, nv_ref, acc_ref, stat_ref,
):
    step = pl.program_id(0)
    owner = own_ref[step]
    first = (step == 0) | (own_ref[jnp.maximum(step - 1, 0)] != owner)
    heads = acc_ref.shape[2]

    @pl.when(first)
    def _():
        acc_ref[...] = jnp.zeros(acc_ref.shape, acc_ref.dtype)
        stat_ref[:, :, :heads, :] = jnp.full(
            stat_ref.shape[:2] + (heads, stat_ref.shape[3]), NEGATIVE, jnp.float32
        )
        stat_ref[:, :, heads:, :] = jnp.zeros(
            stat_ref.shape[:2] + (heads, stat_ref.shape[3]), jnp.float32
        )

    is_fresh = fresh_ref[step] == 1
    keys = jnp.where(is_fresh, nk_ref[0], k_ref[0])
    vals = jnp.where(is_fresh, nv_ref[0], v_ref[0])
    rows, cols = keys.shape[0], q_ref.shape[1]
    quarters, piece = acc_ref.shape[0], acc_ref.shape[4]
    k_pos = lax.broadcasted_iota(jnp.int32, (rows, cols), 0)
    q_pos = lax.broadcasted_iota(jnp.int32, (rows, cols), 1)
    valid = (k_pos < limit_ref[step]) & (q_pos >= offset_ref[step] + k_pos)

    def joined(read):
        return jnp.concatenate([read(c) for c in range(quarters)], axis=1)

    for h in range(heads):
        lanes = slice(h * DH, (h + 1) * DH)
        s = lax.dot_general(
            keys[:, lanes], q_ref[0, :, lanes], (((1,), (1,)), ((), ())),
            preferred_element_type=jnp.float32,
        ) * (DH ** (-0.5))
        s = jnp.where(valid, s, NEGATIVE)
        m_prev = joined(lambda c: stat_ref[c, 0, h : h + 1, :])
        l_prev = joined(lambda c: stat_ref[c, 0, heads + h : heads + h + 1, :])
        acc_prev = joined(lambda c: acc_ref[c, 0, h])
        m_cur = jnp.maximum(m_prev, jnp.max(s, axis=0, keepdims=True))
        p = jnp.where(valid, jnp.exp(s - m_cur), 0.0)
        alpha = jnp.exp(m_prev - m_cur)
        l_cur = alpha * l_prev + jnp.sum(p, axis=0, keepdims=True)
        pv = lax.dot_general(
            vals[:, lanes], p.astype(jnp.bfloat16), (((0,), (0,)), ((), ())),
            preferred_element_type=jnp.float32,
        )
        acc_cur = alpha * acc_prev + pv
        for c in range(quarters):
            cut = slice(c * piece, (c + 1) * piece)
            acc_ref[c, 0, h] = acc_cur[:, cut]
            stat_ref[c, 0, h : h + 1, :] = m_cur[:, cut]
            stat_ref[c, 0, heads + h : heads + h + 1, :] = l_cur[:, cut]


def local_attention(
    owner, page, limit, offset, fresh, everyone, cache_k, cache_v, new_k, new_v, heads, requests,
    piece,
):
    span_rows, width = everyone.shape[1], everyone.shape[2]
    page_rows = cache_k.shape[1]
    blocks = owner.shape[0]
    by_owner = lambda b, own, pg, lim, off, fr: (own[b], 0, 0)
    by_page = lambda b, own, pg, lim, off, fr: (pg[b], 0, 0)
    fixed = lambda b, own, pg, lim, off, fr: (0, 0, 0)
    acc_map = lambda b, own, pg, lim, off, fr: (0, own[b], 0, 0, 0)
    stat_map = lambda b, own, pg, lim, off, fr: (0, own[b], 0, 0)
    quarters = span_rows // piece
    grid_spec = pltpu.PrefetchScalarGridSpec(
        num_scalar_prefetch=5,
        grid=(blocks,),
        in_specs=[
            pl.BlockSpec((1, span_rows, width), by_owner),
            pl.BlockSpec((1, page_rows, width), by_page),
            pl.BlockSpec((1, page_rows, width), by_page),
            pl.BlockSpec((1, page_rows, width), fixed),
            pl.BlockSpec((1, page_rows, width), fixed),
        ],
        out_specs=[
            pl.BlockSpec((quarters, 1, heads, DH, piece), acc_map),
            pl.BlockSpec((quarters, 1, 2 * heads, piece), stat_map),
        ],
    )
    return pl.pallas_call(
        attend_kernel,
        grid_spec=grid_spec,
        out_shape=[
            jax.ShapeDtypeStruct((quarters, requests, heads, DH, piece), jnp.float32),
            jax.ShapeDtypeStruct((quarters, requests, 2 * heads, piece), jnp.float32),
        ],
        compiler_params=pltpu.CompilerParams(dimension_semantics=("arbitrary",)),
    )(owner, page, limit, offset, fresh, everyone, cache_k, cache_v, new_k, new_v)


def shards(
    hidden,
    page_table,
    cache_len,
    expert_ids,
    w_query,
    w_key,
    w_value,
    w_out,
    cache_k,
    cache_v,
    moe_gain,
    router,
    w_gate_up,
    w_down,
):
    tok_rows = hidden.shape[0]
    span_rows = tok_rows * SPAN_DEVS
    seq_count = lax.axis_size("seq")
    seq_index = lax.axis_index("seq")
    local_heads = w_query.shape[1] // DH
    request_total = page_table.shape[0]
    normed = rms_rows(hidden.astype(jnp.float32)).astype(jnp.bfloat16)
    queries = jnp.dot(normed, w_query, preferred_element_type=jnp.float32).astype(jnp.bfloat16)
    new_keys = (
        jnp.dot(normed, w_key, preferred_element_type=jnp.float32)
        .astype(jnp.bfloat16)
        .reshape(tok_rows, local_heads, DH)
    )
    new_values = (
        jnp.dot(normed, w_value, preferred_element_type=jnp.float32)
        .astype(jnp.bfloat16)
        .reshape(tok_rows, local_heads, DH)
    )
    page_count = cache_k.shape[0]
    page_ids = seq_index * page_count + jnp.arange(page_count, dtype=jnp.int32)
    listing = page_table.reshape(-1)
    matches = listing[None, :] == page_ids[:, None]
    entry_index = jnp.arange(listing.shape[0], dtype=jnp.int32)
    found = jnp.sum(jnp.where(matches, entry_index[None, :] + 1, 0), axis=1) - 1
    page_owner = jnp.where(found >= 0, found // MAXP, -1)
    page_order = jnp.where(found >= 0, found % MAXP, 0)
    page_limit = jnp.where(found >= 0, cache_len[jnp.maximum(page_owner, 0)], 0)
    own_request = seq_index * tok_rows // span_rows
    own_offset = seq_index * tok_rows % span_rows
    slot_range = jnp.arange(PAGE, dtype=jnp.int32)
    page_valid = (found >= 0)[:, None] & (
        page_order[:, None] * PAGE + slot_range[None, :] < page_limit[:, None]
    )
    block_total = page_count + 1
    owners = jnp.concatenate([jnp.maximum(page_owner, 0), own_request[None]], axis=0)
    key_limits = jnp.concatenate(
        [jnp.clip(page_limit - page_order * PAGE, 0, PAGE), jnp.full((1,), PAGE, jnp.int32)], axis=0
    )
    query_offsets = jnp.concatenate(
        [jnp.full((page_count,), -span_rows - PAGE, jnp.int32), own_offset[None]], axis=0
    )
    block_order = jnp.argsort(owners, stable=True).astype(jnp.int32)
    sorted_owner = owners[block_order]
    sorted_limit = key_limits[block_order]
    sorted_offset = query_offsets[block_order]
    sorted_fresh = (block_order == page_count).astype(jnp.int32)
    sorted_page = jnp.minimum(block_order, page_count - 1)
    everyone = lax.all_gather(queries, "seq", axis=0, tiled=True).reshape(
        request_total, span_rows, local_heads * DH
    )
    width_heads = local_heads * DH
    acc_out, stat_out = local_attention(
        sorted_owner,
        sorted_page,
        sorted_limit,
        sorted_offset,
        sorted_fresh,
        everyone,
        cache_k,
        cache_v,
        new_keys.reshape(1, tok_rows, width_heads),
        new_values.reshape(1, tok_rows, width_heads),
        local_heads,
        request_total,
        tok_rows,
    )
    visited = jnp.any(
        sorted_owner[:, None] == jnp.arange(request_total, dtype=jnp.int32)[None, :], axis=0
    )
    stat_init = jnp.where(jnp.arange(2 * local_heads) < local_heads, NEGATIVE, 0.0)
    acc_req = jnp.where(visited[None, :, None, None, None], acc_out, 0.0)
    stats = jnp.where(visited[None, :, None, None], stat_out, stat_init[None, None, :, None])
    quarters = span_rows // tok_rows
    quarter_bits = quarters.bit_length() - 1
    request_bits = request_total.bit_length() - 1
    acc_req = acc_req.reshape((2,) * (quarter_bits + request_bits) + (local_heads, DH, tok_rows))
    stats = stats.reshape((2,) * (quarter_bits + request_bits) + (2 * local_heads, tok_rows))
    bit_names = list(range(quarter_bits - 1, -1, -1))
    bit_names += [quarter_bits + k for k in range(request_bits - 1, -1, -1)]
    acc_names = bit_names + ["h", "d", "q"]
    stat_names = bit_names + ["s", "q"]
    bit_count = request_bits + quarter_bits
    for bit in ([0, 1, 3, 2, 4, 5] if bit_count == 6 else list(range(bit_count))):
        acc_axis = acc_names.index(bit)
        stat_axis = stat_names.index(bit)
        acc_names.pop(acc_axis)
        stat_names.pop(stat_axis)
        own_bit = (seq_index >> bit) & 1
        keep_acc = lax.dynamic_index_in_dim(acc_req, own_bit, acc_axis, keepdims=False)
        send_acc = lax.dynamic_index_in_dim(acc_req, 1 - own_bit, acc_axis, keepdims=False)
        keep_stats = lax.dynamic_index_in_dim(stats, own_bit, stat_axis, keepdims=False)
        send_stats = lax.dynamic_index_in_dim(stats, 1 - own_bit, stat_axis, keepdims=False)
        pairs = [(source, source ^ (1 << bit)) for source in range(seq_count)]
        got_acc = lax.ppermute(send_acc.astype(jnp.bfloat16), "seq", pairs).astype(jnp.float32)
        got_stats = lax.ppermute(send_stats, "seq", pairs)
        s_axis = stat_names.index("s")
        keep_m = lax.slice_in_dim(keep_stats, 0, local_heads, axis=s_axis)
        keep_l = lax.slice_in_dim(keep_stats, local_heads, 2 * local_heads, axis=s_axis)
        got_m = lax.slice_in_dim(got_stats, 0, local_heads, axis=s_axis)
        got_l = lax.slice_in_dim(got_stats, local_heads, 2 * local_heads, axis=s_axis)
        m_new = jnp.maximum(keep_m, got_m)
        keep_factor = jnp.exp(keep_m - m_new)
        got_factor = jnp.exp(got_m - m_new)
        l_new = keep_l * keep_factor + got_l * got_factor
        d_axis = acc_names.index("d")
        acc_req = keep_acc * jnp.expand_dims(keep_factor, d_axis) + got_acc * jnp.expand_dims(
            got_factor, d_axis
        )
        stats = jnp.concatenate([m_new, l_new], axis=s_axis)
    attention = acc_req / stats[local_heads:][:, None, :]
    attention = jnp.transpose(attention, (2, 0, 1)).reshape(tok_rows, -1).astype(jnp.bfloat16)
    tp_count = lax.axis_size("tp")
    tp_index = lax.axis_index("tp")

    def tp_gather(value, axis):
        pieces = [value] + [
            lax.ppermute(value, "tp", [(i, (i + k) % tp_count) for i in range(tp_count)])
            for k in range(1, tp_count)
        ]
        stacked = jnp.stack(pieces, axis=0)
        ordered = jnp.take(stacked, (tp_index - jnp.arange(tp_count)) % tp_count, axis=0)
        return jnp.concatenate([ordered[j] for j in range(tp_count)], axis=axis)

    full_attention = tp_gather(attention, 1)
    full_w_out = tp_gather(w_out, 0)
    mid = hidden.astype(jnp.float32) + jnp.dot(
        full_attention, full_w_out, preferred_element_type=jnp.float32
    )
    moe_in = (rms_rows(mid) * moe_gain).astype(jnp.bfloat16)
    logits = jnp.dot(moe_in.astype(jnp.float32), router, precision=lax.Precision.HIGHEST)
    chosen = jax.nn.sigmoid(jnp.take_along_axis(logits, expert_ids, axis=1))
    gates = chosen / jnp.sum(chosen, axis=1, keepdims=True)
    flat_ids = expert_ids.reshape(-1)
    onehot = (flat_ids[:, None] == jnp.arange(EXPERTS, dtype=jnp.int32)[None, :]).astype(jnp.int32)
    ranks = jnp.sum((jnp.cumsum(onehot, axis=0) - 1) * onehot, axis=1)
    target = (flat_ids * CAP + ranks).reshape(tok_rows, TOP)
    hits = target[:, :, None] == jnp.arange(EXPERTS * CAP, dtype=jnp.int32)[None, None, :]
    placing = jnp.any(hits, axis=1).astype(jnp.bfloat16)
    combining = jnp.sum(jnp.where(hits, gates[:, :, None], 0.0), axis=1)
    width = moe_in.shape[1]
    tp_width = width // tp_count
    moe_cols = lax.dynamic_slice_in_dim(moe_in, tp_index * tp_width, tp_width, 1)
    packed = jnp.einsum(
        "te,td->ed", placing, moe_cols, preferred_element_type=jnp.float32
    ).astype(jnp.bfloat16)
    splits = max(1, seq_count // EXPERTS)
    per_device = w_gate_up.shape[0]
    outgoing = jnp.repeat(packed.reshape(EXPERTS, CAP, tp_width), splits, axis=0).reshape(
        seq_count, per_device, CAP, tp_width
    )
    received = lax.all_to_all(outgoing, "seq", split_axis=0, concat_axis=0, tiled=True)
    count = received.shape[2]
    rows = tp_gather(received[:, 0].reshape(-1, tp_width), 1)
    gate = jnp.dot(rows, w_gate_up[0, 0], preferred_element_type=jnp.float32)
    upper = jnp.dot(rows, w_gate_up[0, 1], preferred_element_type=jnp.float32)
    inner = (jax.nn.gelu(gate, approximate=True) * upper).astype(jnp.bfloat16)
    results = jnp.dot(inner, w_down[0], preferred_element_type=jnp.float32).astype(jnp.bfloat16)
    share = lax.dynamic_slice_in_dim(results, tp_index * tp_width, tp_width, 1).astype(
        jnp.float32
    )
    for k in range(1, tp_count):
        target_cols = lax.dynamic_slice_in_dim(
            results, ((tp_index + k) % tp_count) * tp_width, tp_width, 1
        )
        share = share + lax.ppermute(
            target_cols, "tp", [(i, (i + k) % tp_count) for i in range(tp_count)]
        ).astype(jnp.float32)
    produced = share.reshape(seq_count, 1, count, tp_width)
    returned = lax.all_to_all(
        produced.astype(jnp.bfloat16), "seq", split_axis=0, concat_axis=0, tiled=True
    ).astype(jnp.float32)
    folded = jnp.sum(returned.reshape(EXPERTS, splits, CAP, tp_width), axis=1).reshape(
        EXPERTS * CAP, tp_width
    )
    mixture = jnp.dot(combining, folded, precision=lax.Precision.HIGHEST)
    mid_part = lax.dynamic_slice_in_dim(mid, tp_index * tp_width, tp_width, 1)
    return (mid_part + mixture).astype(jnp.bfloat16)

def solution(mesh):
    in_specs = (
        P("seq", None),
        P(),
        P(),
        P("seq", None),
        P(None, "tp"),
        P(None, "tp"),
        P(None, "tp"),
        P("tp", None),
        P("seq", None, "tp"),
        P("seq", None, "tp"),
        P(),
        P(),
        P("seq", None, None, "tp"),
        P("seq", "tp", None),
    )
    out_specs = P("seq", "tp")
    return jax.shard_map(shards, mesh=mesh, in_specs=in_specs, out_specs=out_specs, check_vma=False)
```

```python
import jax
import jax.numpy as jnp
from jax import lax
from jax.sharding import PartitionSpec as P
from jax.experimental import pallas as pl
from jax.experimental.pallas import tpu as pltpu

DH = 64
EXPERTS = 32
TOP = 2
PAGE = 128
MAXP = 256
SPAN_DEVS = 4
CAP = 10


NEGATIVE = -1e30


def passed_along(value, axis, steps):
    count = lax.axis_size(axis)
    pairs = [(source, (source + steps) % count) for source in range(count)]
    return lax.ppermute(value, axis, pairs)


def rms_rows(values):
    return values * lax.rsqrt(jnp.mean(values * values, axis=-1, keepdims=True) + 1e-06)


def online_update(state, queries, keys, values, mask):
    m_old, l_old, accum = state
    scale = queries.shape[2] ** (-0.5)
    scores = jnp.einsum("nhd,khd->hnk", queries, keys, preferred_element_type=jnp.float32) * scale
    scores = jnp.where(mask[None], scores, NEGATIVE)
    m_new = jnp.maximum(m_old, jnp.max(scores, axis=-1).T)
    probs = jnp.where(mask[None], jnp.exp(scores - m_new.T[:, :, None]), 0.0)
    factor = jnp.exp(m_old - m_new)
    l_new = l_old * factor + jnp.sum(probs, axis=-1).T
    weighted = jnp.einsum(
        "hnk,khd->nhd", probs.astype(jnp.bfloat16), values, preferred_element_type=jnp.float32
    )
    return (m_new, l_new, accum * factor[:, :, None] + weighted)


def attend_kernel(
    own_ref, page_ref, limit_ref, offset_ref, fresh_ref,
    q_ref, k_ref, v_ref, nk_ref, nv_ref, acc_ref, stat_ref,
):
    step = pl.program_id(0)
    owner = own_ref[step]
    first = (step == 0) | (own_ref[jnp.maximum(step - 1, 0)] != owner)
    heads = acc_ref.shape[2]

    @pl.when(first)
    def _():
        acc_ref[...] = jnp.zeros(acc_ref.shape, acc_ref.dtype)
        stat_ref[:, :, :heads, :] = jnp.full(
            stat_ref.shape[:2] + (heads, stat_ref.shape[3]), NEGATIVE, jnp.float32
        )
        stat_ref[:, :, heads:, :] = jnp.zeros(
            stat_ref.shape[:2] + (heads, stat_ref.shape[3]), jnp.float32
        )

    is_fresh = fresh_ref[step] == 1
    keys = jnp.where(is_fresh, nk_ref[0], k_ref[0])
    vals = jnp.where(is_fresh, nv_ref[0], v_ref[0])
    rows, cols = keys.shape[0], q_ref.shape[1]
    quarters, piece = acc_ref.shape[0], acc_ref.shape[4]
    k_pos = lax.broadcasted_iota(jnp.int32, (rows, cols), 0)
    q_pos = lax.broadcasted_iota(jnp.int32, (rows, cols), 1)
    valid = (k_pos < limit_ref[step]) & (q_pos >= offset_ref[step] + k_pos)

    def joined(read):
        return jnp.concatenate([read(c) for c in range(quarters)], axis=1)

    for h in range(heads):
        lanes = slice(h * DH, (h + 1) * DH)
        s = lax.dot_general(
            keys[:, lanes], q_ref[0, :, lanes], (((1,), (1,)), ((), ())),
            preferred_element_type=jnp.float32,
        ) * (DH ** (-0.5))
        s = jnp.where(valid, s, NEGATIVE)
        m_prev = joined(lambda c: stat_ref[c, 0, h : h + 1, :])
        l_prev = joined(lambda c: stat_ref[c, 0, heads + h : heads + h + 1, :])
        acc_prev = joined(lambda c: acc_ref[c, 0, h])
        m_cur = jnp.maximum(m_prev, jnp.max(s, axis=0, keepdims=True))
        p = jnp.where(valid, jnp.exp(s - m_cur), 0.0)
        alpha = jnp.exp(m_prev - m_cur)
        l_cur = alpha * l_prev + jnp.sum(p, axis=0, keepdims=True)
        pv = lax.dot_general(
            vals[:, lanes], p.astype(jnp.bfloat16), (((0,), (0,)), ((), ())),
            preferred_element_type=jnp.float32,
        )
        acc_cur = alpha * acc_prev + pv
        for c in range(quarters):
            cut = slice(c * piece, (c + 1) * piece)
            acc_ref[c, 0, h] = acc_cur[:, cut]
            stat_ref[c, 0, h : h + 1, :] = m_cur[:, cut]
            stat_ref[c, 0, heads + h : heads + h + 1, :] = l_cur[:, cut]


def local_attention(
    owner, page, limit, offset, fresh, everyone, cache_k, cache_v, new_k, new_v, heads, requests,
    piece,
):
    span_rows, width = everyone.shape[1], everyone.shape[2]
    page_rows = cache_k.shape[1]
    blocks = owner.shape[0]
    by_owner = lambda b, own, pg, lim, off, fr: (own[b], 0, 0)
    by_page = lambda b, own, pg, lim, off, fr: (pg[b], 0, 0)
    fixed = lambda b, own, pg, lim, off, fr: (0, 0, 0)
    acc_map = lambda b, own, pg, lim, off, fr: (0, own[b], 0, 0, 0)
    stat_map = lambda b, own, pg, lim, off, fr: (0, own[b], 0, 0)
    quarters = span_rows // piece
    grid_spec = pltpu.PrefetchScalarGridSpec(
        num_scalar_prefetch=5,
        grid=(blocks,),
        in_specs=[
            pl.BlockSpec((1, span_rows, width), by_owner),
            pl.BlockSpec((1, page_rows, width), by_page),
            pl.BlockSpec((1, page_rows, width), by_page),
            pl.BlockSpec((1, page_rows, width), fixed),
            pl.BlockSpec((1, page_rows, width), fixed),
        ],
        out_specs=[
            pl.BlockSpec((quarters, 1, heads, DH, piece), acc_map),
            pl.BlockSpec((quarters, 1, 2 * heads, piece), stat_map),
        ],
    )
    return pl.pallas_call(
        attend_kernel,
        grid_spec=grid_spec,
        out_shape=[
            jax.ShapeDtypeStruct((quarters, requests, heads, DH, piece), jnp.float32),
            jax.ShapeDtypeStruct((quarters, requests, 2 * heads, piece), jnp.float32),
        ],
        compiler_params=pltpu.CompilerParams(dimension_semantics=("arbitrary",)),
    )(owner, page, limit, offset, fresh, everyone, cache_k, cache_v, new_k, new_v)


def shards(
    hidden,
    page_table,
    cache_len,
    expert_ids,
    w_query,
    w_key,
    w_value,
    w_out,
    cache_k,
    cache_v,
    moe_gain,
    router,
    w_gate_up,
    w_down,
):
    tok_rows = hidden.shape[0]
    span_rows = tok_rows * SPAN_DEVS
    seq_count = lax.axis_size("seq")
    seq_index = lax.axis_index("seq")
    local_heads = w_query.shape[1] // DH
    request_total = page_table.shape[0]
    normed = rms_rows(hidden.astype(jnp.float32)).astype(jnp.bfloat16)
    queries = jnp.dot(normed, w_query, preferred_element_type=jnp.float32).astype(jnp.bfloat16)
    new_keys = (
        jnp.dot(normed, w_key, preferred_element_type=jnp.float32)
        .astype(jnp.bfloat16)
        .reshape(tok_rows, local_heads, DH)
    )
    new_values = (
        jnp.dot(normed, w_value, preferred_element_type=jnp.float32)
        .astype(jnp.bfloat16)
        .reshape(tok_rows, local_heads, DH)
    )
    page_count = cache_k.shape[0]
    page_ids = seq_index * page_count + jnp.arange(page_count, dtype=jnp.int32)
    listing = page_table.reshape(-1)
    matches = listing[None, :] == page_ids[:, None]
    entry_index = jnp.arange(listing.shape[0], dtype=jnp.int32)
    found = jnp.sum(jnp.where(matches, entry_index[None, :] + 1, 0), axis=1) - 1
    page_owner = jnp.where(found >= 0, found // MAXP, -1)
    page_order = jnp.where(found >= 0, found % MAXP, 0)
    page_limit = jnp.where(found >= 0, cache_len[jnp.maximum(page_owner, 0)], 0)
    own_request = seq_index * tok_rows // span_rows
    own_offset = seq_index * tok_rows % span_rows
    slot_range = jnp.arange(PAGE, dtype=jnp.int32)
    page_valid = (found >= 0)[:, None] & (
        page_order[:, None] * PAGE + slot_range[None, :] < page_limit[:, None]
    )
    block_total = page_count + 1
    owners = jnp.concatenate([jnp.maximum(page_owner, 0), own_request[None]], axis=0)
    key_limits = jnp.concatenate(
        [jnp.clip(page_limit - page_order * PAGE, 0, PAGE), jnp.full((1,), PAGE, jnp.int32)], axis=0
    )
    query_offsets = jnp.concatenate(
        [jnp.full((page_count,), -span_rows - PAGE, jnp.int32), own_offset[None]], axis=0
    )
    block_order = jnp.argsort(owners, stable=True).astype(jnp.int32)
    sorted_owner = owners[block_order]
    sorted_limit = key_limits[block_order]
    sorted_offset = query_offsets[block_order]
    sorted_fresh = (block_order == page_count).astype(jnp.int32)
    sorted_page = jnp.minimum(block_order, page_count - 1)
    gathered = queries
    held_bits = []
    gather_count = seq_count.bit_length() - 1
    for bit in ([5, 4, 2, 3, 1, 0] if gather_count == 6 else list(range(gather_count - 1, -1, -1))):
        pairs = [(source, source ^ (1 << bit)) for source in range(seq_count)]
        got = lax.ppermute(gathered, "seq", pairs)
        low_side = ((seq_index >> bit) & 1) == 0
        position = sum(1 for held in held_bits if held > bit)
        gathered = jnp.stack(
            [jnp.where(low_side, gathered, got), jnp.where(low_side, got, gathered)], axis=position
        )
        held_bits.insert(position, bit)
    everyone = gathered.reshape(request_total, span_rows, local_heads * DH)
    width_heads = local_heads * DH
    acc_out, stat_out = local_attention(
        sorted_owner,
        sorted_page,
        sorted_limit,
        sorted_offset,
        sorted_fresh,
        everyone,
        cache_k,
        cache_v,
        new_keys.reshape(1, tok_rows, width_heads),
        new_values.reshape(1, tok_rows, width_heads),
        local_heads,
        request_total,
        tok_rows,
    )
    visited = jnp.any(
        sorted_owner[:, None] == jnp.arange(request_total, dtype=jnp.int32)[None, :], axis=0
    )
    stat_init = jnp.where(jnp.arange(2 * local_heads) < local_heads, NEGATIVE, 0.0)
    acc_req = jnp.where(visited[None, :, None, None, None], acc_out, 0.0)
    stats = jnp.where(visited[None, :, None, None], stat_out, stat_init[None, None, :, None])
    quarters = span_rows // tok_rows
    quarter_bits = quarters.bit_length() - 1
    request_bits = request_total.bit_length() - 1
    acc_req = acc_req.reshape((2,) * (quarter_bits + request_bits) + (local_heads, DH, tok_rows))
    stats = stats.reshape((2,) * (quarter_bits + request_bits) + (2 * local_heads, tok_rows))
    bit_names = list(range(quarter_bits - 1, -1, -1))
    bit_names += [quarter_bits + k for k in range(request_bits - 1, -1, -1)]
    acc_names = bit_names + ["h", "d", "q"]
    stat_names = bit_names + ["s", "q"]
    bit_count = request_bits + quarter_bits
    for bit in ([0, 1, 3, 2, 4, 5] if bit_count == 6 else list(range(bit_count))):
        acc_axis = acc_names.index(bit)
        stat_axis = stat_names.index(bit)
        acc_names.pop(acc_axis)
        stat_names.pop(stat_axis)
        own_bit = (seq_index >> bit) & 1
        keep_acc = lax.dynamic_index_in_dim(acc_req, own_bit, acc_axis, keepdims=False)
        send_acc = lax.dynamic_index_in_dim(acc_req, 1 - own_bit, acc_axis, keepdims=False)
        keep_stats = lax.dynamic_index_in_dim(stats, own_bit, stat_axis, keepdims=False)
        send_stats = lax.dynamic_index_in_dim(stats, 1 - own_bit, stat_axis, keepdims=False)
        pairs = [(source, source ^ (1 << bit)) for source in range(seq_count)]
        got_acc = lax.ppermute(send_acc.astype(jnp.bfloat16), "seq", pairs).astype(jnp.float32)
        got_stats = lax.ppermute(send_stats, "seq", pairs)
        s_axis = stat_names.index("s")
        keep_m = lax.slice_in_dim(keep_stats, 0, local_heads, axis=s_axis)
        keep_l = lax.slice_in_dim(keep_stats, local_heads, 2 * local_heads, axis=s_axis)
        got_m = lax.slice_in_dim(got_stats, 0, local_heads, axis=s_axis)
        got_l = lax.slice_in_dim(got_stats, local_heads, 2 * local_heads, axis=s_axis)
        m_new = jnp.maximum(keep_m, got_m)
        keep_factor = jnp.exp(keep_m - m_new)
        got_factor = jnp.exp(got_m - m_new)
        l_new = keep_l * keep_factor + got_l * got_factor
        d_axis = acc_names.index("d")
        acc_req = keep_acc * jnp.expand_dims(keep_factor, d_axis) + got_acc * jnp.expand_dims(
            got_factor, d_axis
        )
        stats = jnp.concatenate([m_new, l_new], axis=s_axis)
    attention = acc_req / stats[local_heads:][:, None, :]
    attention = jnp.transpose(attention, (2, 0, 1)).reshape(tok_rows, -1).astype(jnp.bfloat16)
    tp_count = lax.axis_size("tp")
    tp_index = lax.axis_index("tp")

    def tp_gather(value, axis):
        pieces = [value] + [
            lax.ppermute(value, "tp", [(i, (i + k) % tp_count) for i in range(tp_count)])
            for k in range(1, tp_count)
        ]
        stacked = jnp.stack(pieces, axis=0)
        ordered = jnp.take(stacked, (tp_index - jnp.arange(tp_count)) % tp_count, axis=0)
        return jnp.concatenate([ordered[j] for j in range(tp_count)], axis=axis)

    full_attention = tp_gather(attention, 1)
    full_w_out = tp_gather(w_out, 0)
    mid = hidden.astype(jnp.float32) + jnp.dot(
        full_attention, full_w_out, preferred_element_type=jnp.float32
    )
    moe_in = (rms_rows(mid) * moe_gain).astype(jnp.bfloat16)
    logits = jnp.dot(moe_in.astype(jnp.float32), router, precision=lax.Precision.HIGHEST)
    chosen = jax.nn.sigmoid(jnp.take_along_axis(logits, expert_ids, axis=1))
    gates = chosen / jnp.sum(chosen, axis=1, keepdims=True)
    flat_ids = expert_ids.reshape(-1)
    onehot = (flat_ids[:, None] == jnp.arange(EXPERTS, dtype=jnp.int32)[None, :]).astype(jnp.int32)
    ranks = jnp.sum((jnp.cumsum(onehot, axis=0) - 1) * onehot, axis=1)
    target = (flat_ids * CAP + ranks).reshape(tok_rows, TOP)
    hits = target[:, :, None] == jnp.arange(EXPERTS * CAP, dtype=jnp.int32)[None, None, :]
    placing = jnp.any(hits, axis=1).astype(jnp.bfloat16)
    combining = jnp.sum(jnp.where(hits, gates[:, :, None], 0.0), axis=1)
    width = moe_in.shape[1]
    tp_width = width // tp_count
    moe_cols = lax.dynamic_slice_in_dim(moe_in, tp_index * tp_width, tp_width, 1)
    packed = jnp.einsum(
        "te,td->ed", placing, moe_cols, preferred_element_type=jnp.float32
    ).astype(jnp.bfloat16)
    splits = max(1, seq_count // EXPERTS)
    per_device = w_gate_up.shape[0]
    outgoing = jnp.repeat(packed.reshape(EXPERTS, CAP, tp_width), splits, axis=0).reshape(
        seq_count, per_device, CAP, tp_width
    )
    received = lax.all_to_all(outgoing, "seq", split_axis=0, concat_axis=0, tiled=True)
    count = received.shape[2]
    rows = tp_gather(received[:, 0].reshape(-1, tp_width), 1)
    gate = jnp.dot(rows, w_gate_up[0, 0], preferred_element_type=jnp.float32)
    upper = jnp.dot(rows, w_gate_up[0, 1], preferred_element_type=jnp.float32)
    inner = (jax.nn.gelu(gate, approximate=True) * upper).astype(jnp.bfloat16)
    results = jnp.dot(inner, w_down[0], preferred_element_type=jnp.float32).astype(jnp.bfloat16)
    share = lax.dynamic_slice_in_dim(results, tp_index * tp_width, tp_width, 1).astype(
        jnp.float32
    )
    for k in range(1, tp_count):
        target_cols = lax.dynamic_slice_in_dim(
            results, ((tp_index + k) % tp_count) * tp_width, tp_width, 1
        )
        share = share + lax.ppermute(
            target_cols, "tp", [(i, (i + k) % tp_count) for i in range(tp_count)]
        ).astype(jnp.float32)
    produced = share.reshape(seq_count, 1, count, tp_width)
    returned = lax.all_to_all(
        produced.astype(jnp.bfloat16), "seq", split_axis=0, concat_axis=0, tiled=True
    ).astype(jnp.float32)
    folded = jnp.sum(returned.reshape(EXPERTS, splits, CAP, tp_width), axis=1).reshape(
        EXPERTS * CAP, tp_width
    )
    mixture = jnp.dot(combining, folded, precision=lax.Precision.HIGHEST)
    mid_part = lax.dynamic_slice_in_dim(mid, tp_index * tp_width, tp_width, 1)
    return (mid_part + mixture).astype(jnp.bfloat16)

def solution(mesh):
    in_specs = (
        P("seq", None),
        P(),
        P(),
        P("seq", None),
        P(None, "tp"),
        P(None, "tp"),
        P(None, "tp"),
        P("tp", None),
        P("seq", None, "tp"),
        P("seq", None, "tp"),
        P(),
        P(),
        P("seq", None, None, "tp"),
        P("seq", "tp", None),
    )
    out_specs = P("seq", "tp")
    return jax.shard_map(shards, mesh=mesh, in_specs=in_specs, out_specs=out_specs, check_vma=False)
```

```python
import jax
import jax.numpy as jnp
from jax import lax
from jax.sharding import PartitionSpec as P
from jax.experimental import pallas as pl
from jax.experimental.pallas import tpu as pltpu

DH = 64
EXPERTS = 32
TOP = 2
PAGE = 128
MAXP = 256
SPAN_DEVS = 4
CAP = 10


NEGATIVE = -1e30


def passed_along(value, axis, steps):
    count = lax.axis_size(axis)
    pairs = [(source, (source + steps) % count) for source in range(count)]
    return lax.ppermute(value, axis, pairs)


def rms_rows(values):
    return values * lax.rsqrt(jnp.mean(values * values, axis=-1, keepdims=True) + 1e-06)


def online_update(state, queries, keys, values, mask):
    m_old, l_old, accum = state
    scale = queries.shape[2] ** (-0.5)
    scores = jnp.einsum("nhd,khd->hnk", queries, keys, preferred_element_type=jnp.float32) * scale
    scores = jnp.where(mask[None], scores, NEGATIVE)
    m_new = jnp.maximum(m_old, jnp.max(scores, axis=-1).T)
    probs = jnp.where(mask[None], jnp.exp(scores - m_new.T[:, :, None]), 0.0)
    factor = jnp.exp(m_old - m_new)
    l_new = l_old * factor + jnp.sum(probs, axis=-1).T
    weighted = jnp.einsum(
        "hnk,khd->nhd", probs.astype(jnp.bfloat16), values, preferred_element_type=jnp.float32
    )
    return (m_new, l_new, accum * factor[:, :, None] + weighted)


def attend_kernel(
    own_ref, page_ref, limit_ref, offset_ref, fresh_ref,
    q_ref, k_ref, v_ref, nk_ref, nv_ref, acc_ref, stat_ref,
):
    step = pl.program_id(0)
    owner = own_ref[step]
    first = (step == 0) | (own_ref[jnp.maximum(step - 1, 0)] != owner)
    heads = acc_ref.shape[2]

    @pl.when(first)
    def _():
        acc_ref[...] = jnp.zeros(acc_ref.shape, acc_ref.dtype)
        stat_ref[:, :, :heads, :] = jnp.full(
            stat_ref.shape[:2] + (heads, stat_ref.shape[3]), NEGATIVE, jnp.float32
        )
        stat_ref[:, :, heads:, :] = jnp.zeros(
            stat_ref.shape[:2] + (heads, stat_ref.shape[3]), jnp.float32
        )

    is_fresh = fresh_ref[step] == 1
    keys = jnp.where(is_fresh, nk_ref[0], k_ref[0])
    vals = jnp.where(is_fresh, nv_ref[0], v_ref[0])
    quarters, piece = acc_ref.shape[0], acc_ref.shape[4]
    rows, cols = keys.shape[0], quarters * piece
    k_pos = lax.broadcasted_iota(jnp.int32, (rows, cols), 0)
    q_pos = lax.broadcasted_iota(jnp.int32, (rows, cols), 1)
    valid = (k_pos < limit_ref[step]) & (q_pos >= offset_ref[step] + k_pos)

    def joined(read):
        return jnp.concatenate([read(c) for c in range(quarters)], axis=1)

    for h in range(heads):
        lanes = slice(h * DH, (h + 1) * DH)
        q_cols = jnp.concatenate([q_ref[0, c, h] for c in range(quarters)], axis=1)
        s = jnp.dot(keys[:, lanes], q_cols, preferred_element_type=jnp.float32) * (DH ** (-0.5))
        s = jnp.where(valid, s, NEGATIVE)
        m_prev = joined(lambda c: stat_ref[c, 0, h : h + 1, :])
        l_prev = joined(lambda c: stat_ref[c, 0, heads + h : heads + h + 1, :])
        acc_prev = joined(lambda c: acc_ref[c, 0, h])
        m_cur = jnp.maximum(m_prev, jnp.max(s, axis=0, keepdims=True))
        p = jnp.where(valid, jnp.exp(s - m_cur), 0.0)
        alpha = jnp.exp(m_prev - m_cur)
        l_cur = alpha * l_prev + jnp.sum(p, axis=0, keepdims=True)
        pv = jnp.dot(vals[lanes, :], p.astype(jnp.bfloat16), preferred_element_type=jnp.float32)
        acc_cur = alpha * acc_prev + pv
        for c in range(quarters):
            cut = slice(c * piece, (c + 1) * piece)
            acc_ref[c, 0, h] = acc_cur[:, cut]
            stat_ref[c, 0, h : h + 1, :] = m_cur[:, cut]
            stat_ref[c, 0, heads + h : heads + h + 1, :] = l_cur[:, cut]


def local_attention(
    owner, page, limit, offset, fresh, everyone, cache_k, cache_v, new_k, new_v, heads, requests,
    piece,
):
    span_rows, width = everyone.shape[1] * everyone.shape[4], cache_k.shape[2]
    page_rows = cache_k.shape[1]
    blocks = owner.shape[0]
    by_owner = lambda b, own, pg, lim, off, fr: (own[b], 0, 0)
    by_page = lambda b, own, pg, lim, off, fr: (pg[b], 0, 0)
    fixed = lambda b, own, pg, lim, off, fr: (0, 0, 0)
    acc_map = lambda b, own, pg, lim, off, fr: (0, own[b], 0, 0, 0)
    stat_map = lambda b, own, pg, lim, off, fr: (0, own[b], 0, 0)
    quarters = span_rows // piece
    grid_spec = pltpu.PrefetchScalarGridSpec(
        num_scalar_prefetch=5,
        grid=(blocks,),
        in_specs=[
            pl.BlockSpec((1,) + everyone.shape[1:], lambda b, own, pg, lim, off, fr: (own[b], 0, 0, 0, 0)),
            pl.BlockSpec((1, page_rows, width), by_page),
            pl.BlockSpec((1, width, page_rows), by_page),
            pl.BlockSpec((1, page_rows, width), fixed),
            pl.BlockSpec((1, width, page_rows), fixed),
        ],
        out_specs=[
            pl.BlockSpec((quarters, 1, heads, DH, piece), acc_map),
            pl.BlockSpec((quarters, 1, 2 * heads, piece), stat_map),
        ],
    )
    return pl.pallas_call(
        attend_kernel,
        grid_spec=grid_spec,
        out_shape=[
            jax.ShapeDtypeStruct((quarters, requests, heads, DH, piece), jnp.float32),
            jax.ShapeDtypeStruct((quarters, requests, 2 * heads, piece), jnp.float32),
        ],
        compiler_params=pltpu.CompilerParams(dimension_semantics=("arbitrary",)),
    )(owner, page, limit, offset, fresh, everyone, cache_k, cache_v, new_k, new_v)


def shards(
    hidden,
    page_table,
    cache_len,
    expert_ids,
    w_query,
    w_key,
    w_value,
    w_out,
    cache_k,
    cache_v,
    moe_gain,
    router,
    w_gate_up,
    w_down,
):
    tok_rows = hidden.shape[0]
    span_rows = tok_rows * SPAN_DEVS
    seq_count = lax.axis_size("seq")
    seq_index = lax.axis_index("seq")
    local_heads = w_query.shape[1] // DH
    request_total = page_table.shape[0]
    normed = rms_rows(hidden.astype(jnp.float32)).astype(jnp.bfloat16)
    queries = jnp.dot(normed, w_query, preferred_element_type=jnp.float32).astype(jnp.bfloat16)
    new_keys = (
        jnp.dot(normed, w_key, preferred_element_type=jnp.float32)
        .astype(jnp.bfloat16)
        .reshape(tok_rows, local_heads, DH)
    )
    new_values = (
        jnp.dot(normed, w_value, preferred_element_type=jnp.float32)
        .astype(jnp.bfloat16)
        .reshape(tok_rows, local_heads, DH)
    )
    page_count = cache_k.shape[0]
    page_ids = seq_index * page_count + jnp.arange(page_count, dtype=jnp.int32)
    listing = page_table.reshape(-1)
    matches = listing[None, :] == page_ids[:, None]
    entry_index = jnp.arange(listing.shape[0], dtype=jnp.int32)
    found = jnp.sum(jnp.where(matches, entry_index[None, :] + 1, 0), axis=1) - 1
    page_owner = jnp.where(found >= 0, found // MAXP, -1)
    page_order = jnp.where(found >= 0, found % MAXP, 0)
    page_limit = jnp.where(found >= 0, cache_len[jnp.maximum(page_owner, 0)], 0)
    own_request = seq_index * tok_rows // span_rows
    own_offset = seq_index * tok_rows % span_rows
    slot_range = jnp.arange(PAGE, dtype=jnp.int32)
    page_valid = (found >= 0)[:, None] & (
        page_order[:, None] * PAGE + slot_range[None, :] < page_limit[:, None]
    )
    block_total = page_count + 1
    owners = jnp.concatenate([jnp.maximum(page_owner, 0), own_request[None]], axis=0)
    key_limits = jnp.concatenate(
        [jnp.clip(page_limit - page_order * PAGE, 0, PAGE), jnp.full((1,), PAGE, jnp.int32)], axis=0
    )
    query_offsets = jnp.concatenate(
        [jnp.full((page_count,), -span_rows - PAGE, jnp.int32), own_offset[None]], axis=0
    )
    block_order = jnp.argsort(owners, stable=True).astype(jnp.int32)
    sorted_owner = owners[block_order]
    sorted_limit = key_limits[block_order]
    sorted_offset = query_offsets[block_order]
    sorted_fresh = (block_order == page_count).astype(jnp.int32)
    sorted_page = jnp.minimum(block_order, page_count - 1)
    gathered = jnp.transpose(queries.reshape(tok_rows, local_heads, DH), (1, 2, 0))
    held_bits = []
    gather_count = seq_count.bit_length() - 1
    for bit in ([5, 4, 2, 3, 1, 0] if gather_count == 6 else list(range(gather_count - 1, -1, -1))):
        pairs = [(source, source ^ (1 << bit)) for source in range(seq_count)]
        got = lax.ppermute(gathered, "seq", pairs)
        low_side = ((seq_index >> bit) & 1) == 0
        position = sum(1 for held in held_bits if held > bit)
        gathered = jnp.stack(
            [jnp.where(low_side, gathered, got), jnp.where(low_side, got, gathered)], axis=position
        )
        held_bits.insert(position, bit)
    everyone = gathered.reshape(
        request_total, span_rows // tok_rows, local_heads, DH, tok_rows
    )
    width_heads = local_heads * DH
    acc_out, stat_out = local_attention(
        sorted_owner,
        sorted_page,
        sorted_limit,
        sorted_offset,
        sorted_fresh,
        everyone,
        cache_k,
        jnp.swapaxes(cache_v, 1, 2),
        new_keys.reshape(1, tok_rows, width_heads),
        new_values.reshape(tok_rows, width_heads).T[None],
        local_heads,
        request_total,
        tok_rows,
    )
    visited = jnp.any(
        sorted_owner[:, None] == jnp.arange(request_total, dtype=jnp.int32)[None, :], axis=0
    )
    stat_init = jnp.where(jnp.arange(2 * local_heads) < local_heads, NEGATIVE, 0.0)
    acc_req = jnp.where(visited[None, :, None, None, None], acc_out, 0.0)
    stats = jnp.where(visited[None, :, None, None], stat_out, stat_init[None, None, :, None])
    quarters = span_rows // tok_rows
    quarter_bits = quarters.bit_length() - 1
    request_bits = request_total.bit_length() - 1
    acc_req = acc_req.reshape((2,) * (quarter_bits + request_bits) + (local_heads, DH, tok_rows))
    stats = stats.reshape((2,) * (quarter_bits + request_bits) + (2 * local_heads, tok_rows))
    bit_names = list(range(quarter_bits - 1, -1, -1))
    bit_names += [quarter_bits + k for k in range(request_bits - 1, -1, -1)]
    acc_names = bit_names + ["h", "d", "q"]
    stat_names = bit_names + ["s", "q"]
    bit_count = request_bits + quarter_bits
    for bit in ([0, 1, 3, 2, 4, 5] if bit_count == 6 else list(range(bit_count))):
        acc_axis = acc_names.index(bit)
        stat_axis = stat_names.index(bit)
        acc_names.pop(acc_axis)
        stat_names.pop(stat_axis)
        own_bit = (seq_index >> bit) & 1
        keep_acc = lax.dynamic_index_in_dim(acc_req, own_bit, acc_axis, keepdims=False)
        send_acc = lax.dynamic_index_in_dim(acc_req, 1 - own_bit, acc_axis, keepdims=False)
        keep_stats = lax.dynamic_index_in_dim(stats, own_bit, stat_axis, keepdims=False)
        send_stats = lax.dynamic_index_in_dim(stats, 1 - own_bit, stat_axis, keepdims=False)
        pairs = [(source, source ^ (1 << bit)) for source in range(seq_count)]
        got_acc = lax.ppermute(send_acc.astype(jnp.bfloat16), "seq", pairs).astype(jnp.float32)
        got_stats = lax.ppermute(send_stats, "seq", pairs)
        s_axis = stat_names.index("s")
        keep_m = lax.slice_in_dim(keep_stats, 0, local_heads, axis=s_axis)
        keep_l = lax.slice_in_dim(keep_stats, local_heads, 2 * local_heads, axis=s_axis)
        got_m = lax.slice_in_dim(got_stats, 0, local_heads, axis=s_axis)
        got_l = lax.slice_in_dim(got_stats, local_heads, 2 * local_heads, axis=s_axis)
        m_new = jnp.maximum(keep_m, got_m)
        keep_factor = jnp.exp(keep_m - m_new)
        got_factor = jnp.exp(got_m - m_new)
        l_new = keep_l * keep_factor + got_l * got_factor
        d_axis = acc_names.index("d")
        acc_req = keep_acc * jnp.expand_dims(keep_factor, d_axis) + got_acc * jnp.expand_dims(
            got_factor, d_axis
        )
        stats = jnp.concatenate([m_new, l_new], axis=s_axis)
    attention = acc_req / stats[local_heads:][:, None, :]
    attention = jnp.transpose(attention, (2, 0, 1)).reshape(tok_rows, -1).astype(jnp.bfloat16)
    tp_count = lax.axis_size("tp")
    tp_index = lax.axis_index("tp")

    def tp_gather(value, axis):
        pieces = [value] + [
            lax.ppermute(value, "tp", [(i, (i + k) % tp_count) for i in range(tp_count)])
            for k in range(1, tp_count)
        ]
        stacked = jnp.stack(pieces, axis=0)
        ordered = jnp.take(stacked, (tp_index - jnp.arange(tp_count)) % tp_count, axis=0)
        return jnp.concatenate([ordered[j] for j in range(tp_count)], axis=axis)

    full_attention = tp_gather(attention, 1)
    full_w_out = tp_gather(w_out, 0)
    mid = hidden.astype(jnp.float32) + jnp.dot(
        full_attention, full_w_out, preferred_element_type=jnp.float32
    )
    moe_in = (rms_rows(mid) * moe_gain).astype(jnp.bfloat16)
    logits = jnp.dot(moe_in.astype(jnp.float32), router, precision=lax.Precision.HIGHEST)
    chosen = jax.nn.sigmoid(jnp.take_along_axis(logits, expert_ids, axis=1))
    gates = chosen / jnp.sum(chosen, axis=1, keepdims=True)
    flat_ids = expert_ids.reshape(-1)
    onehot = (flat_ids[:, None] == jnp.arange(EXPERTS, dtype=jnp.int32)[None, :]).astype(jnp.int32)
    ranks = jnp.sum((jnp.cumsum(onehot, axis=0) - 1) * onehot, axis=1)
    target = (flat_ids * CAP + ranks).reshape(tok_rows, TOP)
    hits = target[:, :, None] == jnp.arange(EXPERTS * CAP, dtype=jnp.int32)[None, None, :]
    placing = jnp.any(hits, axis=1).astype(jnp.bfloat16)
    combining = jnp.sum(jnp.where(hits, gates[:, :, None], 0.0), axis=1)
    width = moe_in.shape[1]
    tp_width = width // tp_count
    moe_cols = lax.dynamic_slice_in_dim(moe_in, tp_index * tp_width, tp_width, 1)
    packed = jnp.einsum(
        "te,td->ed", placing, moe_cols, preferred_element_type=jnp.float32
    ).astype(jnp.bfloat16)
    splits = max(1, seq_count // EXPERTS)
    per_device = w_gate_up.shape[0]
    outgoing = jnp.repeat(packed.reshape(EXPERTS, CAP, tp_width), splits, axis=0).reshape(
        seq_count, per_device, CAP, tp_width
    )
    received = lax.all_to_all(outgoing, "seq", split_axis=0, concat_axis=0, tiled=True)
    count = received.shape[2]
    rows = tp_gather(received[:, 0].reshape(-1, tp_width), 1)
    gate = jnp.dot(rows, w_gate_up[0, 0], preferred_element_type=jnp.float32)
    upper = jnp.dot(rows, w_gate_up[0, 1], preferred_element_type=jnp.float32)
    inner = (jax.nn.gelu(gate, approximate=True) * upper).astype(jnp.bfloat16)
    results = jnp.dot(inner, w_down[0], preferred_element_type=jnp.float32).astype(jnp.bfloat16)
    share = lax.dynamic_slice_in_dim(results, tp_index * tp_width, tp_width, 1).astype(
        jnp.float32
    )
    for k in range(1, tp_count):
        target_cols = lax.dynamic_slice_in_dim(
            results, ((tp_index + k) % tp_count) * tp_width, tp_width, 1
        )
        share = share + lax.ppermute(
            target_cols, "tp", [(i, (i + k) % tp_count) for i in range(tp_count)]
        ).astype(jnp.float32)
    produced = share.reshape(seq_count, 1, count, tp_width)
    returned = lax.all_to_all(
        produced.astype(jnp.bfloat16), "seq", split_axis=0, concat_axis=0, tiled=True
    ).astype(jnp.float32)
    folded = jnp.sum(returned.reshape(EXPERTS, splits, CAP, tp_width), axis=1).reshape(
        EXPERTS * CAP, tp_width
    )
    mixture = jnp.dot(combining, folded, precision=lax.Precision.HIGHEST)
    mid_part = lax.dynamic_slice_in_dim(mid, tp_index * tp_width, tp_width, 1)
    return (mid_part + mixture).astype(jnp.bfloat16)

def solution(mesh):
    in_specs = (
        P("seq", None),
        P(),
        P(),
        P("seq", None),
        P(None, "tp"),
        P(None, "tp"),
        P(None, "tp"),
        P("tp", None),
        P("seq", None, "tp"),
        P("seq", None, "tp"),
        P(),
        P(),
        P("seq", None, None, "tp"),
        P("seq", "tp", None),
    )
    out_specs = P("seq", "tp")
    return jax.shard_map(shards, mesh=mesh, in_specs=in_specs, out_specs=out_specs, check_vma=False)
```

```python
import jax
import jax.numpy as jnp
from jax import lax
from jax.sharding import PartitionSpec as P
from jax.experimental import pallas as pl
from jax.experimental.pallas import tpu as pltpu

DH = 64
EXPERTS = 32
TOP = 2
PAGE = 128
MAXP = 256
SPAN_DEVS = 4
CAP = 10


NEGATIVE = -1e30


def passed_along(value, axis, steps):
    count = lax.axis_size(axis)
    pairs = [(source, (source + steps) % count) for source in range(count)]
    return lax.ppermute(value, axis, pairs)


def rms_rows(values):
    return values * lax.rsqrt(jnp.mean(values * values, axis=-1, keepdims=True) + 1e-06)


def online_update(state, queries, keys, values, mask):
    m_old, l_old, accum = state
    scale = queries.shape[2] ** (-0.5)
    scores = jnp.einsum("nhd,khd->hnk", queries, keys, preferred_element_type=jnp.float32) * scale
    scores = jnp.where(mask[None], scores, NEGATIVE)
    m_new = jnp.maximum(m_old, jnp.max(scores, axis=-1).T)
    probs = jnp.where(mask[None], jnp.exp(scores - m_new.T[:, :, None]), 0.0)
    factor = jnp.exp(m_old - m_new)
    l_new = l_old * factor + jnp.sum(probs, axis=-1).T
    weighted = jnp.einsum(
        "hnk,khd->nhd", probs.astype(jnp.bfloat16), values, preferred_element_type=jnp.float32
    )
    return (m_new, l_new, accum * factor[:, :, None] + weighted)


def attend_kernel(
    own_ref, page_ref, limit_ref, offset_ref, fresh_ref,
    q_ref, k_ref, v_ref, nk_ref, nv_ref, acc_ref, stat_ref,
):
    step = pl.program_id(0)
    owner = own_ref[step]
    first = (step == 0) | (own_ref[jnp.maximum(step - 1, 0)] != owner)
    heads = acc_ref.shape[2]

    @pl.when(first)
    def _():
        acc_ref[...] = jnp.zeros(acc_ref.shape, acc_ref.dtype)
        stat_ref[:, :, :heads, :] = jnp.full(
            stat_ref.shape[:2] + (heads, stat_ref.shape[3]), NEGATIVE, jnp.float32
        )
        stat_ref[:, :, heads:, :] = jnp.zeros(
            stat_ref.shape[:2] + (heads, stat_ref.shape[3]), jnp.float32
        )

    is_fresh = fresh_ref[step] == 1
    keys = jnp.where(is_fresh, nk_ref[0], k_ref[0])
    vals = jnp.where(is_fresh, nv_ref[0], v_ref[0])
    rows, cols = keys.shape[0], q_ref.shape[1]
    quarters, piece = acc_ref.shape[0], acc_ref.shape[4]
    k_pos = lax.broadcasted_iota(jnp.int32, (rows, cols), 0)
    q_pos = lax.broadcasted_iota(jnp.int32, (rows, cols), 1)
    valid = (k_pos < limit_ref[step]) & (q_pos >= offset_ref[step] + k_pos)

    def joined(read):
        return jnp.concatenate([read(c) for c in range(quarters)], axis=1)

    for h in range(heads):
        lanes = slice(h * DH, (h + 1) * DH)
        s = lax.dot_general(
            keys[:, lanes], q_ref[0, :, lanes], (((1,), (1,)), ((), ())),
            preferred_element_type=jnp.float32,
        ) * (DH ** (-0.5))
        s = jnp.where(valid, s, NEGATIVE)
        m_prev = joined(lambda c: stat_ref[c, 0, h : h + 1, :])
        l_prev = joined(lambda c: stat_ref[c, 0, heads + h : heads + h + 1, :])
        acc_prev = joined(lambda c: acc_ref[c, 0, h])
        m_cur = jnp.maximum(m_prev, jnp.max(s, axis=0, keepdims=True))
        p = jnp.where(valid, jnp.exp(s - m_cur), 0.0)
        alpha = jnp.exp(m_prev - m_cur)
        l_cur = alpha * l_prev + jnp.sum(p, axis=0, keepdims=True)
        pv = lax.dot_general(
            vals[:, lanes], p.astype(jnp.bfloat16), (((0,), (0,)), ((), ())),
            preferred_element_type=jnp.float32,
        )
        acc_cur = alpha * acc_prev + pv
        for c in range(quarters):
            cut = slice(c * piece, (c + 1) * piece)
            acc_ref[c, 0, h] = acc_cur[:, cut]
            stat_ref[c, 0, h : h + 1, :] = m_cur[:, cut]
            stat_ref[c, 0, heads + h : heads + h + 1, :] = l_cur[:, cut]


def local_attention(
    owner, page, limit, offset, fresh, everyone, cache_k, cache_v, new_k, new_v, heads, requests,
    piece,
):
    span_rows, width = everyone.shape[1], everyone.shape[2]
    page_rows = cache_k.shape[1]
    blocks = owner.shape[0]
    by_owner = lambda b, own, pg, lim, off, fr: (own[b], 0, 0)
    by_page = lambda b, own, pg, lim, off, fr: (pg[b], 0, 0)
    fixed = lambda b, own, pg, lim, off, fr: (0, 0, 0)
    acc_map = lambda b, own, pg, lim, off, fr: (0, own[b], 0, 0, 0)
    stat_map = lambda b, own, pg, lim, off, fr: (0, own[b], 0, 0)
    quarters = span_rows // piece
    grid_spec = pltpu.PrefetchScalarGridSpec(
        num_scalar_prefetch=5,
        grid=(blocks,),
        in_specs=[
            pl.BlockSpec((1, span_rows, width), by_owner),
            pl.BlockSpec((1, page_rows, width), by_page),
            pl.BlockSpec((1, page_rows, width), by_page),
            pl.BlockSpec((1, page_rows, width), fixed),
            pl.BlockSpec((1, page_rows, width), fixed),
        ],
        out_specs=[
            pl.BlockSpec((quarters, 1, heads, DH, piece), acc_map),
            pl.BlockSpec((quarters, 1, 2 * heads, piece), stat_map),
        ],
    )
    return pl.pallas_call(
        attend_kernel,
        grid_spec=grid_spec,
        out_shape=[
            jax.ShapeDtypeStruct((quarters, requests, heads, DH, piece), jnp.float32),
            jax.ShapeDtypeStruct((quarters, requests, 2 * heads, piece), jnp.float32),
        ],
        compiler_params=pltpu.CompilerParams(dimension_semantics=("arbitrary",)),
    )(owner, page, limit, offset, fresh, everyone, cache_k, cache_v, new_k, new_v)


def shards(
    hidden,
    page_table,
    cache_len,
    expert_ids,
    w_query,
    w_key,
    w_value,
    w_out,
    cache_k,
    cache_v,
    moe_gain,
    router,
    w_gate_up,
    w_down,
):
    tok_rows = hidden.shape[0]
    span_rows = tok_rows * SPAN_DEVS
    seq_count = lax.axis_size("seq")
    seq_index = lax.axis_index("seq")
    local_heads = w_query.shape[1] // DH
    request_total = page_table.shape[0]
    normed = rms_rows(hidden.astype(jnp.float32)).astype(jnp.bfloat16)
    queries = jnp.dot(normed, w_query, preferred_element_type=jnp.float32).astype(jnp.bfloat16)
    new_keys = (
        jnp.dot(normed, w_key, preferred_element_type=jnp.float32)
        .astype(jnp.bfloat16)
        .reshape(tok_rows, local_heads, DH)
    )
    new_values = (
        jnp.dot(normed, w_value, preferred_element_type=jnp.float32)
        .astype(jnp.bfloat16)
        .reshape(tok_rows, local_heads, DH)
    )
    page_count = cache_k.shape[0]
    page_ids = seq_index * page_count + jnp.arange(page_count, dtype=jnp.int32)
    listing = page_table.reshape(-1)
    matches = listing[None, :] == page_ids[:, None]
    entry_index = jnp.arange(listing.shape[0], dtype=jnp.int32)
    found = jnp.sum(jnp.where(matches, entry_index[None, :] + 1, 0), axis=1) - 1
    page_owner = jnp.where(found >= 0, found // MAXP, -1)
    page_order = jnp.where(found >= 0, found % MAXP, 0)
    page_limit = jnp.where(found >= 0, cache_len[jnp.maximum(page_owner, 0)], 0)
    own_request = seq_index * tok_rows // span_rows
    own_offset = seq_index * tok_rows % span_rows
    slot_range = jnp.arange(PAGE, dtype=jnp.int32)
    page_valid = (found >= 0)[:, None] & (
        page_order[:, None] * PAGE + slot_range[None, :] < page_limit[:, None]
    )
    block_total = page_count + 1
    owners = jnp.concatenate([jnp.maximum(page_owner, 0), own_request[None]], axis=0)
    key_limits = jnp.concatenate(
        [jnp.clip(page_limit - page_order * PAGE, 0, PAGE), jnp.full((1,), PAGE, jnp.int32)], axis=0
    )
    query_offsets = jnp.concatenate(
        [jnp.full((page_count,), -span_rows - PAGE, jnp.int32), own_offset[None]], axis=0
    )
    block_order = jnp.argsort(owners, stable=True).astype(jnp.int32)
    sorted_owner = owners[block_order]
    sorted_limit = key_limits[block_order]
    sorted_offset = query_offsets[block_order]
    sorted_fresh = (block_order == page_count).astype(jnp.int32)
    sorted_page = jnp.minimum(block_order, page_count - 1)
    block_tables = (sorted_owner, sorted_page, sorted_limit, sorted_offset, sorted_fresh)
    fresh_kv = (
        new_keys.reshape(1, tok_rows, local_heads * DH),
        new_values.reshape(1, tok_rows, local_heads * DH),
    )
    gathered = queries
    held_bits = []
    gather_count = seq_count.bit_length() - 1
    for bit in ([5, 4, 2, 3, 1, 0] if gather_count == 6 else list(range(gather_count - 1, -1, -1))):
        pairs = [(source, source ^ (1 << bit)) for source in range(seq_count)]
        got = lax.ppermute(gathered, "seq", pairs)
        low_side = ((seq_index >> bit) & 1) == 0
        position = sum(1 for held in held_bits if held > bit)
        gathered = jnp.stack(
            [jnp.where(low_side, gathered, got), jnp.where(low_side, got, gathered)], axis=position
        )
        held_bits.insert(position, bit)
        if len(held_bits) == 1:
            gathered, block_tables, fresh_kv = lax.optimization_barrier(
                (gathered, block_tables, fresh_kv)
            )
    everyone = gathered.reshape(request_total, span_rows, local_heads * DH)
    width_heads = local_heads * DH
    sorted_owner, sorted_page, sorted_limit, sorted_offset, sorted_fresh = block_tables
    acc_out, stat_out = local_attention(
        sorted_owner,
        sorted_page,
        sorted_limit,
        sorted_offset,
        sorted_fresh,
        everyone,
        cache_k,
        cache_v,
        fresh_kv[0],
        fresh_kv[1],
        local_heads,
        request_total,
        tok_rows,
    )
    visited = jnp.any(
        sorted_owner[:, None] == jnp.arange(request_total, dtype=jnp.int32)[None, :], axis=0
    )
    stat_init = jnp.where(jnp.arange(2 * local_heads) < local_heads, NEGATIVE, 0.0)
    acc_req = jnp.where(visited[None, :, None, None, None], acc_out, 0.0)
    stats = jnp.where(visited[None, :, None, None], stat_out, stat_init[None, None, :, None])
    quarters = span_rows // tok_rows
    quarter_bits = quarters.bit_length() - 1
    request_bits = request_total.bit_length() - 1
    acc_req = acc_req.reshape((2,) * (quarter_bits + request_bits) + (local_heads, DH, tok_rows))
    stats = stats.reshape((2,) * (quarter_bits + request_bits) + (2 * local_heads, tok_rows))
    bit_names = list(range(quarter_bits - 1, -1, -1))
    bit_names += [quarter_bits + k for k in range(request_bits - 1, -1, -1)]
    acc_names = bit_names + ["h", "d", "q"]
    stat_names = bit_names + ["s", "q"]
    bit_count = request_bits + quarter_bits
    for bit in ([0, 1, 3, 2, 4, 5] if bit_count == 6 else list(range(bit_count))):
        acc_axis = acc_names.index(bit)
        stat_axis = stat_names.index(bit)
        acc_names.pop(acc_axis)
        stat_names.pop(stat_axis)
        own_bit = (seq_index >> bit) & 1
        keep_acc = lax.dynamic_index_in_dim(acc_req, own_bit, acc_axis, keepdims=False)
        send_acc = lax.dynamic_index_in_dim(acc_req, 1 - own_bit, acc_axis, keepdims=False)
        keep_stats = lax.dynamic_index_in_dim(stats, own_bit, stat_axis, keepdims=False)
        send_stats = lax.dynamic_index_in_dim(stats, 1 - own_bit, stat_axis, keepdims=False)
        pairs = [(source, source ^ (1 << bit)) for source in range(seq_count)]
        got_acc = lax.ppermute(send_acc.astype(jnp.bfloat16), "seq", pairs).astype(jnp.float32)
        got_stats = lax.ppermute(send_stats, "seq", pairs)
        s_axis = stat_names.index("s")
        keep_m = lax.slice_in_dim(keep_stats, 0, local_heads, axis=s_axis)
        keep_l = lax.slice_in_dim(keep_stats, local_heads, 2 * local_heads, axis=s_axis)
        got_m = lax.slice_in_dim(got_stats, 0, local_heads, axis=s_axis)
        got_l = lax.slice_in_dim(got_stats, local_heads, 2 * local_heads, axis=s_axis)
        m_new = jnp.maximum(keep_m, got_m)
        keep_factor = jnp.exp(keep_m - m_new)
        got_factor = jnp.exp(got_m - m_new)
        l_new = keep_l * keep_factor + got_l * got_factor
        d_axis = acc_names.index("d")
        acc_req = keep_acc * jnp.expand_dims(keep_factor, d_axis) + got_acc * jnp.expand_dims(
            got_factor, d_axis
        )
        stats = jnp.concatenate([m_new, l_new], axis=s_axis)
    attention = acc_req / stats[local_heads:][:, None, :]
    attention = jnp.transpose(attention, (2, 0, 1)).reshape(tok_rows, -1).astype(jnp.bfloat16)
    tp_count = lax.axis_size("tp")
    tp_index = lax.axis_index("tp")

    def tp_gather(value, axis):
        pieces = [value] + [
            lax.ppermute(value, "tp", [(i, (i + k) % tp_count) for i in range(tp_count)])
            for k in range(1, tp_count)
        ]
        stacked = jnp.stack(pieces, axis=0)
        ordered = jnp.take(stacked, (tp_index - jnp.arange(tp_count)) % tp_count, axis=0)
        return jnp.concatenate([ordered[j] for j in range(tp_count)], axis=axis)

    full_attention = tp_gather(attention, 1)
    full_w_out = tp_gather(w_out, 0)
    mid = hidden.astype(jnp.float32) + jnp.dot(
        full_attention, full_w_out, preferred_element_type=jnp.float32
    )
    moe_in = (rms_rows(mid) * moe_gain).astype(jnp.bfloat16)
    logits = jnp.dot(moe_in.astype(jnp.float32), router, precision=lax.Precision.HIGHEST)
    chosen = jax.nn.sigmoid(jnp.take_along_axis(logits, expert_ids, axis=1))
    gates = chosen / jnp.sum(chosen, axis=1, keepdims=True)
    flat_ids = expert_ids.reshape(-1)
    onehot = (flat_ids[:, None] == jnp.arange(EXPERTS, dtype=jnp.int32)[None, :]).astype(jnp.int32)
    ranks = jnp.sum((jnp.cumsum(onehot, axis=0) - 1) * onehot, axis=1)
    target = (flat_ids * CAP + ranks).reshape(tok_rows, TOP)
    hits = target[:, :, None] == jnp.arange(EXPERTS * CAP, dtype=jnp.int32)[None, None, :]
    placing = jnp.any(hits, axis=1).astype(jnp.bfloat16)
    combining = jnp.sum(jnp.where(hits, gates[:, :, None], 0.0), axis=1)
    width = moe_in.shape[1]
    tp_width = width // tp_count
    moe_cols = lax.dynamic_slice_in_dim(moe_in, tp_index * tp_width, tp_width, 1)
    packed = jnp.einsum(
        "te,td->ed", placing, moe_cols, preferred_element_type=jnp.float32
    ).astype(jnp.bfloat16)
    splits = max(1, seq_count // EXPERTS)
    per_device = w_gate_up.shape[0]
    outgoing = jnp.repeat(packed.reshape(EXPERTS, CAP, tp_width), splits, axis=0).reshape(
        seq_count, per_device, CAP, tp_width
    )
    received = lax.all_to_all(outgoing, "seq", split_axis=0, concat_axis=0, tiled=True)
    count = received.shape[2]
    rows = tp_gather(received[:, 0].reshape(-1, tp_width), 1)
    gate = jnp.dot(rows, w_gate_up[0, 0], preferred_element_type=jnp.float32)
    upper = jnp.dot(rows, w_gate_up[0, 1], preferred_element_type=jnp.float32)
    inner = (jax.nn.gelu(gate, approximate=True) * upper).astype(jnp.bfloat16)
    results = jnp.dot(inner, w_down[0], preferred_element_type=jnp.float32).astype(jnp.bfloat16)
    share = lax.dynamic_slice_in_dim(results, tp_index * tp_width, tp_width, 1).astype(
        jnp.float32
    )
    for k in range(1, tp_count):
        target_cols = lax.dynamic_slice_in_dim(
            results, ((tp_index + k) % tp_count) * tp_width, tp_width, 1
        )
        share = share + lax.ppermute(
            target_cols, "tp", [(i, (i + k) % tp_count) for i in range(tp_count)]
        ).astype(jnp.float32)
    produced = share.reshape(seq_count, 1, count, tp_width)
    returned = lax.all_to_all(
        produced.astype(jnp.bfloat16), "seq", split_axis=0, concat_axis=0, tiled=True
    ).astype(jnp.float32)
    folded = jnp.sum(returned.reshape(EXPERTS, splits, CAP, tp_width), axis=1).reshape(
        EXPERTS * CAP, tp_width
    )
    mixture = jnp.dot(combining, folded, precision=lax.Precision.HIGHEST)
    mid_part = lax.dynamic_slice_in_dim(mid, tp_index * tp_width, tp_width, 1)
    return (mid_part + mixture).astype(jnp.bfloat16)

def solution(mesh):
    in_specs = (
        P("seq", None),
        P(),
        P(),
        P("seq", None),
        P(None, "tp"),
        P(None, "tp"),
        P(None, "tp"),
        P("tp", None),
        P("seq", None, "tp"),
        P("seq", None, "tp"),
        P(),
        P(),
        P("seq", None, None, "tp"),
        P("seq", "tp", None),
    )
    out_specs = P("seq", "tp")
    return jax.shard_map(shards, mesh=mesh, in_specs=in_specs, out_specs=out_specs, check_vma=False)
```

```python
import jax
import jax.numpy as jnp
from jax import lax
from jax.sharding import PartitionSpec as P
from jax.experimental import pallas as pl
from jax.experimental.pallas import tpu as pltpu

DH = 64
EXPERTS = 32
TOP = 2
PAGE = 128
MAXP = 256
SPAN_DEVS = 4
CAP = 10


NEGATIVE = -1e30


def passed_along(value, axis, steps):
    count = lax.axis_size(axis)
    pairs = [(source, (source + steps) % count) for source in range(count)]
    return lax.ppermute(value, axis, pairs)


def rms_rows(values):
    return values * lax.rsqrt(jnp.mean(values * values, axis=-1, keepdims=True) + 1e-06)


def online_update(state, queries, keys, values, mask):
    m_old, l_old, accum = state
    scale = queries.shape[2] ** (-0.5)
    scores = jnp.einsum("nhd,khd->hnk", queries, keys, preferred_element_type=jnp.float32) * scale
    scores = jnp.where(mask[None], scores, NEGATIVE)
    m_new = jnp.maximum(m_old, jnp.max(scores, axis=-1).T)
    probs = jnp.where(mask[None], jnp.exp(scores - m_new.T[:, :, None]), 0.0)
    factor = jnp.exp(m_old - m_new)
    l_new = l_old * factor + jnp.sum(probs, axis=-1).T
    weighted = jnp.einsum(
        "hnk,khd->nhd", probs.astype(jnp.bfloat16), values, preferred_element_type=jnp.float32
    )
    return (m_new, l_new, accum * factor[:, :, None] + weighted)


def attend_kernel(
    own_ref, page_ref, limit_ref, offset_ref, fresh_ref,
    q_ref, k_ref, v_ref, nk_ref, nv_ref, acc_ref, stat_ref,
):
    step = pl.program_id(0)
    owner = own_ref[step]
    first = (step == 0) | (own_ref[jnp.maximum(step - 1, 0)] != owner)
    heads = acc_ref.shape[2]

    @pl.when(first)
    def _():
        acc_ref[...] = jnp.zeros(acc_ref.shape, acc_ref.dtype)
        stat_ref[:, :, :heads, :] = jnp.full(
            stat_ref.shape[:2] + (heads, stat_ref.shape[3]), NEGATIVE, jnp.float32
        )
        stat_ref[:, :, heads:, :] = jnp.zeros(
            stat_ref.shape[:2] + (heads, stat_ref.shape[3]), jnp.float32
        )

    is_fresh = fresh_ref[step] == 1
    keys = jnp.where(is_fresh, nk_ref[0], k_ref[0])
    vals = jnp.where(is_fresh, nv_ref[0], v_ref[0])
    rows, cols = keys.shape[0], q_ref.shape[1]
    quarters, piece = acc_ref.shape[0], acc_ref.shape[4]
    k_pos = lax.broadcasted_iota(jnp.int32, (rows, cols), 0)
    q_pos = lax.broadcasted_iota(jnp.int32, (rows, cols), 1)
    valid = (k_pos < limit_ref[step]) & (q_pos >= offset_ref[step] + k_pos)

    def joined(read):
        return jnp.concatenate([read(c) for c in range(quarters)], axis=1)

    for h in range(heads):
        lanes = slice(h * DH, (h + 1) * DH)
        s = lax.dot_general(
            keys[:, lanes], q_ref[0, :, lanes], (((1,), (1,)), ((), ())),
            preferred_element_type=jnp.float32,
        ) * (DH ** (-0.5))
        s = jnp.where(valid, s, NEGATIVE)
        m_prev = joined(lambda c: stat_ref[c, 0, h : h + 1, :])
        l_prev = joined(lambda c: stat_ref[c, 0, heads + h : heads + h + 1, :])
        acc_prev = joined(lambda c: acc_ref[c, 0, h])
        m_cur = jnp.maximum(m_prev, jnp.max(s, axis=0, keepdims=True))
        p = jnp.where(valid, jnp.exp(s - m_cur), 0.0)
        alpha = jnp.exp(m_prev - m_cur)
        l_cur = alpha * l_prev + jnp.sum(p, axis=0, keepdims=True)
        pv = lax.dot_general(
            vals[:, lanes], p.astype(jnp.bfloat16), (((0,), (0,)), ((), ())),
            preferred_element_type=jnp.float32,
        )
        acc_cur = alpha * acc_prev + pv
        for c in range(quarters):
            cut = slice(c * piece, (c + 1) * piece)
            acc_ref[c, 0, h] = acc_cur[:, cut]
            stat_ref[c, 0, h : h + 1, :] = m_cur[:, cut]
            stat_ref[c, 0, heads + h : heads + h + 1, :] = l_cur[:, cut]


def local_attention(
    owner, page, limit, offset, fresh, everyone, cache_k, cache_v, new_k, new_v, heads, requests,
    piece,
):
    span_rows, width = everyone.shape[1], everyone.shape[2]
    page_rows = cache_k.shape[1]
    blocks = owner.shape[0]
    by_owner = lambda b, own, pg, lim, off, fr: (own[b], 0, 0)
    by_page = lambda b, own, pg, lim, off, fr: (pg[b], 0, 0)
    fixed = lambda b, own, pg, lim, off, fr: (0, 0, 0)
    acc_map = lambda b, own, pg, lim, off, fr: (0, own[b], 0, 0, 0)
    stat_map = lambda b, own, pg, lim, off, fr: (0, own[b], 0, 0)
    quarters = span_rows // piece
    grid_spec = pltpu.PrefetchScalarGridSpec(
        num_scalar_prefetch=5,
        grid=(blocks,),
        in_specs=[
            pl.BlockSpec((1, span_rows, width), by_owner),
            pl.BlockSpec((1, page_rows, width), by_page),
            pl.BlockSpec((1, page_rows, width), by_page),
            pl.BlockSpec((1, page_rows, width), fixed),
            pl.BlockSpec((1, page_rows, width), fixed),
        ],
        out_specs=[
            pl.BlockSpec((quarters, 1, heads, DH, piece), acc_map),
            pl.BlockSpec((quarters, 1, 2 * heads, piece), stat_map),
        ],
    )
    return pl.pallas_call(
        attend_kernel,
        grid_spec=grid_spec,
        out_shape=[
            jax.ShapeDtypeStruct((quarters, requests, heads, DH, piece), jnp.float32),
            jax.ShapeDtypeStruct((quarters, requests, 2 * heads, piece), jnp.float32),
        ],
        compiler_params=pltpu.CompilerParams(dimension_semantics=("arbitrary",)),
    )(owner, page, limit, offset, fresh, everyone, cache_k, cache_v, new_k, new_v)


def shards(
    hidden,
    page_table,
    cache_len,
    expert_ids,
    w_query,
    w_key,
    w_value,
    w_out,
    cache_k,
    cache_v,
    moe_gain,
    router,
    w_gate_up,
    w_down,
):
    tok_rows = hidden.shape[0]
    span_rows = tok_rows * SPAN_DEVS
    seq_count = lax.axis_size("seq")
    seq_index = lax.axis_index("seq")
    local_heads = w_query.shape[1] // DH
    request_total = page_table.shape[0]
    normed = rms_rows(hidden.astype(jnp.float32)).astype(jnp.bfloat16)
    queries = jnp.dot(normed, w_query, preferred_element_type=jnp.float32).astype(jnp.bfloat16)
    new_keys = (
        jnp.dot(normed, w_key, preferred_element_type=jnp.float32)
        .astype(jnp.bfloat16)
        .reshape(tok_rows, local_heads, DH)
    )
    new_values = (
        jnp.dot(normed, w_value, preferred_element_type=jnp.float32)
        .astype(jnp.bfloat16)
        .reshape(tok_rows, local_heads, DH)
    )
    page_count = cache_k.shape[0]
    page_ids = seq_index * page_count + jnp.arange(page_count, dtype=jnp.int32)
    listing = page_table.reshape(-1)
    matches = listing[None, :] == page_ids[:, None]
    entry_index = jnp.arange(listing.shape[0], dtype=jnp.int32)
    found = jnp.sum(jnp.where(matches, entry_index[None, :] + 1, 0), axis=1) - 1
    page_owner = jnp.where(found >= 0, found // MAXP, -1)
    page_order = jnp.where(found >= 0, found % MAXP, 0)
    page_limit = jnp.where(found >= 0, cache_len[jnp.maximum(page_owner, 0)], 0)
    own_request = seq_index * tok_rows // span_rows
    own_offset = seq_index * tok_rows % span_rows
    slot_range = jnp.arange(PAGE, dtype=jnp.int32)
    page_valid = (found >= 0)[:, None] & (
        page_order[:, None] * PAGE + slot_range[None, :] < page_limit[:, None]
    )
    block_total = page_count + 1
    owners = jnp.concatenate([jnp.maximum(page_owner, 0), own_request[None]], axis=0)
    key_limits = jnp.concatenate(
        [jnp.clip(page_limit - page_order * PAGE, 0, PAGE), jnp.full((1,), PAGE, jnp.int32)], axis=0
    )
    query_offsets = jnp.concatenate(
        [jnp.full((page_count,), -span_rows - PAGE, jnp.int32), own_offset[None]], axis=0
    )
    block_order = jnp.argsort(owners, stable=True).astype(jnp.int32)
    sorted_owner = owners[block_order]
    sorted_limit = key_limits[block_order]
    sorted_offset = query_offsets[block_order]
    sorted_fresh = (block_order == page_count).astype(jnp.int32)
    sorted_page = jnp.minimum(block_order, page_count - 1)
    block_tables = (sorted_owner, sorted_page, sorted_limit, sorted_offset, sorted_fresh)
    fresh_kv = (
        new_keys.reshape(1, tok_rows, local_heads * DH),
        new_values.reshape(1, tok_rows, local_heads * DH),
    )
    gathered = queries
    held_bits = []
    gather_count = seq_count.bit_length() - 1
    for bit in ([5, 4, 2, 3, 1, 0] if gather_count == 6 else list(range(gather_count - 1, -1, -1))):
        pairs = [(source, source ^ (1 << bit)) for source in range(seq_count)]
        got = lax.ppermute(gathered, "seq", pairs)
        low_side = ((seq_index >> bit) & 1) == 0
        position = sum(1 for held in held_bits if held > bit)
        gathered = jnp.stack(
            [jnp.where(low_side, gathered, got), jnp.where(low_side, got, gathered)], axis=position
        )
        held_bits.insert(position, bit)
        if len(held_bits) == gather_count - 1:
            gathered, block_tables, fresh_kv = lax.optimization_barrier(
                (gathered, block_tables, fresh_kv)
            )
    everyone = gathered.reshape(request_total, span_rows, local_heads * DH)
    width_heads = local_heads * DH
    sorted_owner, sorted_page, sorted_limit, sorted_offset, sorted_fresh = block_tables
    acc_out, stat_out = local_attention(
        sorted_owner,
        sorted_page,
        sorted_limit,
        sorted_offset,
        sorted_fresh,
        everyone,
        cache_k,
        cache_v,
        fresh_kv[0],
        fresh_kv[1],
        local_heads,
        request_total,
        tok_rows,
    )
    visited = jnp.any(
        sorted_owner[:, None] == jnp.arange(request_total, dtype=jnp.int32)[None, :], axis=0
    )
    stat_init = jnp.where(jnp.arange(2 * local_heads) < local_heads, NEGATIVE, 0.0)
    acc_req = jnp.where(visited[None, :, None, None, None], acc_out, 0.0)
    stats = jnp.where(visited[None, :, None, None], stat_out, stat_init[None, None, :, None])
    quarters = span_rows // tok_rows
    quarter_bits = quarters.bit_length() - 1
    request_bits = request_total.bit_length() - 1
    acc_req = acc_req.reshape((2,) * (quarter_bits + request_bits) + (local_heads, DH, tok_rows))
    stats = stats.reshape((2,) * (quarter_bits + request_bits) + (2 * local_heads, tok_rows))
    bit_names = list(range(quarter_bits - 1, -1, -1))
    bit_names += [quarter_bits + k for k in range(request_bits - 1, -1, -1)]
    acc_names = bit_names + ["h", "d", "q"]
    stat_names = bit_names + ["s", "q"]
    bit_count = request_bits + quarter_bits
    for bit in ([0, 1, 3, 2, 4, 5] if bit_count == 6 else list(range(bit_count))):
        acc_axis = acc_names.index(bit)
        stat_axis = stat_names.index(bit)
        acc_names.pop(acc_axis)
        stat_names.pop(stat_axis)
        own_bit = (seq_index >> bit) & 1
        keep_acc = lax.dynamic_index_in_dim(acc_req, own_bit, acc_axis, keepdims=False)
        send_acc = lax.dynamic_index_in_dim(acc_req, 1 - own_bit, acc_axis, keepdims=False)
        keep_stats = lax.dynamic_index_in_dim(stats, own_bit, stat_axis, keepdims=False)
        send_stats = lax.dynamic_index_in_dim(stats, 1 - own_bit, stat_axis, keepdims=False)
        pairs = [(source, source ^ (1 << bit)) for source in range(seq_count)]
        got_acc = lax.ppermute(send_acc.astype(jnp.bfloat16), "seq", pairs).astype(jnp.float32)
        got_stats = lax.ppermute(send_stats, "seq", pairs)
        s_axis = stat_names.index("s")
        keep_m = lax.slice_in_dim(keep_stats, 0, local_heads, axis=s_axis)
        keep_l = lax.slice_in_dim(keep_stats, local_heads, 2 * local_heads, axis=s_axis)
        got_m = lax.slice_in_dim(got_stats, 0, local_heads, axis=s_axis)
        got_l = lax.slice_in_dim(got_stats, local_heads, 2 * local_heads, axis=s_axis)
        m_new = jnp.maximum(keep_m, got_m)
        keep_factor = jnp.exp(keep_m - m_new)
        got_factor = jnp.exp(got_m - m_new)
        l_new = keep_l * keep_factor + got_l * got_factor
        d_axis = acc_names.index("d")
        acc_req = keep_acc * jnp.expand_dims(keep_factor, d_axis) + got_acc * jnp.expand_dims(
            got_factor, d_axis
        )
        stats = jnp.concatenate([m_new, l_new], axis=s_axis)
    attention = acc_req / stats[local_heads:][:, None, :]
    attention = jnp.transpose(attention, (2, 0, 1)).reshape(tok_rows, -1).astype(jnp.bfloat16)
    tp_count = lax.axis_size("tp")
    tp_index = lax.axis_index("tp")

    def tp_gather(value, axis):
        pieces = [value] + [
            lax.ppermute(value, "tp", [(i, (i + k) % tp_count) for i in range(tp_count)])
            for k in range(1, tp_count)
        ]
        stacked = jnp.stack(pieces, axis=0)
        ordered = jnp.take(stacked, (tp_index - jnp.arange(tp_count)) % tp_count, axis=0)
        return jnp.concatenate([ordered[j] for j in range(tp_count)], axis=axis)

    full_attention = tp_gather(attention, 1)
    full_w_out = tp_gather(w_out, 0)
    mid = hidden.astype(jnp.float32) + jnp.dot(
        full_attention, full_w_out, preferred_element_type=jnp.float32
    )
    moe_in = (rms_rows(mid) * moe_gain).astype(jnp.bfloat16)
    logits = jnp.dot(moe_in.astype(jnp.float32), router, precision=lax.Precision.HIGHEST)
    chosen = jax.nn.sigmoid(jnp.take_along_axis(logits, expert_ids, axis=1))
    gates = chosen / jnp.sum(chosen, axis=1, keepdims=True)
    flat_ids = expert_ids.reshape(-1)
    onehot = (flat_ids[:, None] == jnp.arange(EXPERTS, dtype=jnp.int32)[None, :]).astype(jnp.int32)
    ranks = jnp.sum((jnp.cumsum(onehot, axis=0) - 1) * onehot, axis=1)
    target = (flat_ids * CAP + ranks).reshape(tok_rows, TOP)
    hits = target[:, :, None] == jnp.arange(EXPERTS * CAP, dtype=jnp.int32)[None, None, :]
    placing = jnp.any(hits, axis=1).astype(jnp.bfloat16)
    combining = jnp.sum(jnp.where(hits, gates[:, :, None], 0.0), axis=1)
    width = moe_in.shape[1]
    tp_width = width // tp_count
    moe_cols = lax.dynamic_slice_in_dim(moe_in, tp_index * tp_width, tp_width, 1)
    packed = jnp.einsum(
        "te,td->ed", placing, moe_cols, preferred_element_type=jnp.float32
    ).astype(jnp.bfloat16)
    splits = max(1, seq_count // EXPERTS)
    per_device = w_gate_up.shape[0]
    outgoing = jnp.repeat(packed.reshape(EXPERTS, CAP, tp_width), splits, axis=0).reshape(
        seq_count, per_device, CAP, tp_width
    )
    received = lax.all_to_all(outgoing, "seq", split_axis=0, concat_axis=0, tiled=True)
    count = received.shape[2]
    rows = tp_gather(received[:, 0].reshape(-1, tp_width), 1)
    gate = jnp.dot(rows, w_gate_up[0, 0], preferred_element_type=jnp.float32)
    upper = jnp.dot(rows, w_gate_up[0, 1], preferred_element_type=jnp.float32)
    inner = (jax.nn.gelu(gate, approximate=True) * upper).astype(jnp.bfloat16)
    results = jnp.dot(inner, w_down[0], preferred_element_type=jnp.float32).astype(jnp.bfloat16)
    share = lax.dynamic_slice_in_dim(results, tp_index * tp_width, tp_width, 1).astype(
        jnp.float32
    )
    for k in range(1, tp_count):
        target_cols = lax.dynamic_slice_in_dim(
            results, ((tp_index + k) % tp_count) * tp_width, tp_width, 1
        )
        share = share + lax.ppermute(
            target_cols, "tp", [(i, (i + k) % tp_count) for i in range(tp_count)]
        ).astype(jnp.float32)
    produced = share.reshape(seq_count, 1, count, tp_width)
    returned = lax.all_to_all(
        produced.astype(jnp.bfloat16), "seq", split_axis=0, concat_axis=0, tiled=True
    ).astype(jnp.float32)
    folded = jnp.sum(returned.reshape(EXPERTS, splits, CAP, tp_width), axis=1).reshape(
        EXPERTS * CAP, tp_width
    )
    mixture = jnp.dot(combining, folded, precision=lax.Precision.HIGHEST)
    mid_part = lax.dynamic_slice_in_dim(mid, tp_index * tp_width, tp_width, 1)
    return (mid_part + mixture).astype(jnp.bfloat16)

def solution(mesh):
    in_specs = (
        P("seq", None),
        P(),
        P(),
        P("seq", None),
        P(None, "tp"),
        P(None, "tp"),
        P(None, "tp"),
        P("tp", None),
        P("seq", None, "tp"),
        P("seq", None, "tp"),
        P(),
        P(),
        P("seq", None, None, "tp"),
        P("seq", "tp", None),
    )
    out_specs = P("seq", "tp")
    return jax.shard_map(shards, mesh=mesh, in_specs=in_specs, out_specs=out_specs, check_vma=False)
```

```python
import jax
import jax.numpy as jnp
from jax import lax
from jax.sharding import PartitionSpec as P
from jax.experimental import pallas as pl
from jax.experimental.pallas import tpu as pltpu

DH = 64
EXPERTS = 32
TOP = 2
PAGE = 128
MAXP = 256
SPAN_DEVS = 4
CAP = 10


NEGATIVE = -1e30


def passed_along(value, axis, steps):
    count = lax.axis_size(axis)
    pairs = [(source, (source + steps) % count) for source in range(count)]
    return lax.ppermute(value, axis, pairs)


def rms_rows(values):
    return values * lax.rsqrt(jnp.mean(values * values, axis=-1, keepdims=True) + 1e-06)


def online_update(state, queries, keys, values, mask):
    m_old, l_old, accum = state
    scale = queries.shape[2] ** (-0.5)
    scores = jnp.einsum("nhd,khd->hnk", queries, keys, preferred_element_type=jnp.float32) * scale
    scores = jnp.where(mask[None], scores, NEGATIVE)
    m_new = jnp.maximum(m_old, jnp.max(scores, axis=-1).T)
    probs = jnp.where(mask[None], jnp.exp(scores - m_new.T[:, :, None]), 0.0)
    factor = jnp.exp(m_old - m_new)
    l_new = l_old * factor + jnp.sum(probs, axis=-1).T
    weighted = jnp.einsum(
        "hnk,khd->nhd", probs.astype(jnp.bfloat16), values, preferred_element_type=jnp.float32
    )
    return (m_new, l_new, accum * factor[:, :, None] + weighted)


def attend_kernel(
    own_ref, page_ref, limit_ref, offset_ref, fresh_ref,
    q_ref, k_ref, v_ref, nk_ref, nv_ref, acc_ref, stat_ref,
):
    step = pl.program_id(0)
    owner = own_ref[step]
    first = (step == 0) | (own_ref[jnp.maximum(step - 1, 0)] != owner)
    heads = acc_ref.shape[2]

    @pl.when(first)
    def _():
        acc_ref[...] = jnp.zeros(acc_ref.shape, acc_ref.dtype)
        stat_ref[:, :, :heads, :] = jnp.full(
            stat_ref.shape[:2] + (heads, stat_ref.shape[3]), NEGATIVE, jnp.float32
        )
        stat_ref[:, :, heads:, :] = jnp.zeros(
            stat_ref.shape[:2] + (heads, stat_ref.shape[3]), jnp.float32
        )

    is_fresh = fresh_ref[step] == 1
    keys = jnp.where(is_fresh, nk_ref[0], k_ref[0])
    vals = jnp.where(is_fresh, nv_ref[0], v_ref[0])
    rows, cols = keys.shape[0], q_ref.shape[1]
    quarters, piece = acc_ref.shape[0], acc_ref.shape[4]
    k_pos = lax.broadcasted_iota(jnp.int32, (rows, cols), 0)
    q_pos = lax.broadcasted_iota(jnp.int32, (rows, cols), 1)
    valid = (k_pos < limit_ref[step]) & (q_pos >= offset_ref[step] + k_pos)

    def joined(read):
        return jnp.concatenate([read(c) for c in range(quarters)], axis=1)

    for h in range(heads):
        lanes = slice(h * DH, (h + 1) * DH)
        s = lax.dot_general(
            keys[:, lanes], q_ref[0, :, lanes], (((1,), (1,)), ((), ())),
            preferred_element_type=jnp.float32,
        ) * (DH ** (-0.5))
        s = jnp.where(valid, s, NEGATIVE)
        m_prev = joined(lambda c: stat_ref[c, 0, h : h + 1, :])
        l_prev = joined(lambda c: stat_ref[c, 0, heads + h : heads + h + 1, :])
        acc_prev = joined(lambda c: acc_ref[c, 0, h])
        m_cur = jnp.maximum(m_prev, jnp.max(s, axis=0, keepdims=True))
        p = jnp.where(valid, jnp.exp(s - m_cur), 0.0)
        alpha = jnp.exp(m_prev - m_cur)
        l_cur = alpha * l_prev + jnp.sum(p, axis=0, keepdims=True)
        pv = lax.dot_general(
            vals[:, lanes], p.astype(jnp.bfloat16), (((0,), (0,)), ((), ())),
            preferred_element_type=jnp.float32,
        )
        acc_cur = alpha * acc_prev + pv
        for c in range(quarters):
            cut = slice(c * piece, (c + 1) * piece)
            acc_ref[c, 0, h] = acc_cur[:, cut]
            stat_ref[c, 0, h : h + 1, :] = m_cur[:, cut]
            stat_ref[c, 0, heads + h : heads + h + 1, :] = l_cur[:, cut]


def local_attention(
    owner, page, limit, offset, fresh, everyone, cache_k, cache_v, new_k, new_v, heads, requests,
    piece,
):
    span_rows, width = everyone.shape[1], everyone.shape[2]
    page_rows = cache_k.shape[1]
    blocks = owner.shape[0]
    by_owner = lambda b, own, pg, lim, off, fr: (own[b], 0, 0)
    by_page = lambda b, own, pg, lim, off, fr: (pg[b], 0, 0)
    fixed = lambda b, own, pg, lim, off, fr: (0, 0, 0)
    acc_map = lambda b, own, pg, lim, off, fr: (0, own[b], 0, 0, 0)
    stat_map = lambda b, own, pg, lim, off, fr: (0, own[b], 0, 0)
    quarters = span_rows // piece
    grid_spec = pltpu.PrefetchScalarGridSpec(
        num_scalar_prefetch=5,
        grid=(blocks,),
        in_specs=[
            pl.BlockSpec((1, span_rows, width), by_owner),
            pl.BlockSpec((1, page_rows, width), by_page),
            pl.BlockSpec((1, page_rows, width), by_page),
            pl.BlockSpec((1, page_rows, width), fixed),
            pl.BlockSpec((1, page_rows, width), fixed),
        ],
        out_specs=[
            pl.BlockSpec((quarters, 1, heads, DH, piece), acc_map),
            pl.BlockSpec((quarters, 1, 2 * heads, piece), stat_map),
        ],
    )
    return pl.pallas_call(
        attend_kernel,
        grid_spec=grid_spec,
        out_shape=[
            jax.ShapeDtypeStruct((quarters, requests, heads, DH, piece), jnp.float32),
            jax.ShapeDtypeStruct((quarters, requests, 2 * heads, piece), jnp.float32),
        ],
        compiler_params=pltpu.CompilerParams(dimension_semantics=("arbitrary",)),
    )(owner, page, limit, offset, fresh, everyone, cache_k, cache_v, new_k, new_v)


def shards(
    hidden,
    page_table,
    cache_len,
    expert_ids,
    w_query,
    w_key,
    w_value,
    w_out,
    cache_k,
    cache_v,
    moe_gain,
    router,
    w_gate_up,
    w_down,
):
    tok_rows = hidden.shape[0]
    span_rows = tok_rows * SPAN_DEVS
    seq_count = lax.axis_size("seq")
    seq_index = lax.axis_index("seq")
    local_heads = w_query.shape[1] // DH
    request_total = page_table.shape[0]
    normed = rms_rows(hidden.astype(jnp.float32)).astype(jnp.bfloat16)
    queries = jnp.dot(normed, w_query, preferred_element_type=jnp.float32).astype(jnp.bfloat16)
    new_keys = (
        jnp.dot(normed, w_key, preferred_element_type=jnp.float32)
        .astype(jnp.bfloat16)
        .reshape(tok_rows, local_heads, DH)
    )
    new_values = (
        jnp.dot(normed, w_value, preferred_element_type=jnp.float32)
        .astype(jnp.bfloat16)
        .reshape(tok_rows, local_heads, DH)
    )
    page_count = cache_k.shape[0]
    page_ids = seq_index * page_count + jnp.arange(page_count, dtype=jnp.int32)
    listing = page_table.reshape(-1)
    matches = listing[None, :] == page_ids[:, None]
    entry_index = jnp.arange(listing.shape[0], dtype=jnp.int32)
    found = jnp.sum(jnp.where(matches, entry_index[None, :] + 1, 0), axis=1) - 1
    page_owner = jnp.where(found >= 0, found // MAXP, -1)
    page_order = jnp.where(found >= 0, found % MAXP, 0)
    page_limit = jnp.where(found >= 0, cache_len[jnp.maximum(page_owner, 0)], 0)
    own_request = seq_index * tok_rows // span_rows
    own_offset = seq_index * tok_rows % span_rows
    slot_range = jnp.arange(PAGE, dtype=jnp.int32)
    page_valid = (found >= 0)[:, None] & (
        page_order[:, None] * PAGE + slot_range[None, :] < page_limit[:, None]
    )
    block_total = page_count + 1
    owners = jnp.concatenate([jnp.maximum(page_owner, 0), own_request[None]], axis=0)
    key_limits = jnp.concatenate(
        [jnp.clip(page_limit - page_order * PAGE, 0, PAGE), jnp.full((1,), PAGE, jnp.int32)], axis=0
    )
    query_offsets = jnp.concatenate(
        [jnp.full((page_count,), -span_rows - PAGE, jnp.int32), own_offset[None]], axis=0
    )
    block_order = jnp.argsort(owners, stable=True).astype(jnp.int32)
    sorted_owner = owners[block_order]
    sorted_limit = key_limits[block_order]
    sorted_offset = query_offsets[block_order]
    sorted_fresh = (block_order == page_count).astype(jnp.int32)
    sorted_page = jnp.minimum(block_order, page_count - 1)
    block_tables = (sorted_owner, sorted_page, sorted_limit, sorted_offset, sorted_fresh)
    fresh_kv = (
        new_keys.reshape(1, tok_rows, local_heads * DH),
        new_values.reshape(1, tok_rows, local_heads * DH),
    )
    gathered = queries
    held_bits = []
    gather_count = seq_count.bit_length() - 1
    for bit in ([5, 4, 2, 3, 1, 0] if gather_count == 6 else list(range(gather_count - 1, -1, -1))):
        pairs = [(source, source ^ (1 << bit)) for source in range(seq_count)]
        got = lax.ppermute(gathered, "seq", pairs)
        low_side = ((seq_index >> bit) & 1) == 0
        position = sum(1 for held in held_bits if held > bit)
        gathered = jnp.stack(
            [jnp.where(low_side, gathered, got), jnp.where(low_side, got, gathered)], axis=position
        )
        held_bits.insert(position, bit)
        if len(held_bits) == gather_count - 1:
            gathered, block_tables, fresh_kv = lax.optimization_barrier(
                (gathered, block_tables, fresh_kv)
            )
    everyone = gathered.reshape(request_total, span_rows, local_heads * DH)
    width_heads = local_heads * DH
    sorted_owner, sorted_page, sorted_limit, sorted_offset, sorted_fresh = block_tables
    acc_out, stat_out = local_attention(
        sorted_owner,
        sorted_page,
        sorted_limit,
        sorted_offset,
        sorted_fresh,
        everyone,
        cache_k,
        cache_v,
        fresh_kv[0],
        fresh_kv[1],
        local_heads,
        request_total,
        tok_rows,
    )
    visited = jnp.any(
        sorted_owner[:, None] == jnp.arange(request_total, dtype=jnp.int32)[None, :], axis=0
    )
    stat_init = jnp.where(jnp.arange(2 * local_heads) < local_heads, NEGATIVE, 0.0)
    acc_req = jnp.where(visited[None, :, None, None, None], acc_out, 0.0)
    stats = jnp.where(visited[None, :, None, None], stat_out, stat_init[None, None, :, None])
    quarters = span_rows // tok_rows
    quarter_bits = quarters.bit_length() - 1
    request_bits = request_total.bit_length() - 1
    acc_req = acc_req.reshape((2,) * (quarter_bits + request_bits) + (local_heads, DH, tok_rows))
    stats = stats.reshape((2,) * (quarter_bits + request_bits) + (2 * local_heads, tok_rows))
    bit_names = list(range(quarter_bits - 1, -1, -1))
    bit_names += [quarter_bits + k for k in range(request_bits - 1, -1, -1)]
    acc_names = bit_names + ["h", "d", "q"]
    stat_names = bit_names + ["s", "q"]
    flat_ids = expert_ids.reshape(-1)
    onehot = (flat_ids[:, None] == jnp.arange(EXPERTS, dtype=jnp.int32)[None, :]).astype(jnp.int32)
    ranks = jnp.sum((jnp.cumsum(onehot, axis=0) - 1) * onehot, axis=1)
    target = (flat_ids * CAP + ranks).reshape(tok_rows, TOP)
    slot_hits = target[:, :, None] == jnp.arange(EXPERTS * CAP, dtype=jnp.int32)[None, None, :]
    placing = jnp.any(slot_hits, axis=1).astype(jnp.bfloat16)
    routing = (target, placing)
    bit_count = request_bits + quarter_bits
    for bit in ([0, 1, 3, 2, 4, 5] if bit_count == 6 else list(range(bit_count))):
        acc_axis = acc_names.index(bit)
        stat_axis = stat_names.index(bit)
        acc_names.pop(acc_axis)
        stat_names.pop(stat_axis)
        own_bit = (seq_index >> bit) & 1
        keep_acc = lax.dynamic_index_in_dim(acc_req, own_bit, acc_axis, keepdims=False)
        send_acc = lax.dynamic_index_in_dim(acc_req, 1 - own_bit, acc_axis, keepdims=False)
        keep_stats = lax.dynamic_index_in_dim(stats, own_bit, stat_axis, keepdims=False)
        send_stats = lax.dynamic_index_in_dim(stats, 1 - own_bit, stat_axis, keepdims=False)
        pairs = [(source, source ^ (1 << bit)) for source in range(seq_count)]
        got_acc = lax.ppermute(send_acc.astype(jnp.bfloat16), "seq", pairs).astype(jnp.float32)
        got_stats = lax.ppermute(send_stats, "seq", pairs)
        s_axis = stat_names.index("s")
        keep_m = lax.slice_in_dim(keep_stats, 0, local_heads, axis=s_axis)
        keep_l = lax.slice_in_dim(keep_stats, local_heads, 2 * local_heads, axis=s_axis)
        got_m = lax.slice_in_dim(got_stats, 0, local_heads, axis=s_axis)
        got_l = lax.slice_in_dim(got_stats, local_heads, 2 * local_heads, axis=s_axis)
        m_new = jnp.maximum(keep_m, got_m)
        keep_factor = jnp.exp(keep_m - m_new)
        got_factor = jnp.exp(got_m - m_new)
        l_new = keep_l * keep_factor + got_l * got_factor
        d_axis = acc_names.index("d")
        acc_req = keep_acc * jnp.expand_dims(keep_factor, d_axis) + got_acc * jnp.expand_dims(
            got_factor, d_axis
        )
        stats = jnp.concatenate([m_new, l_new], axis=s_axis)
        if bit == 0:
            acc_req, stats, routing = lax.optimization_barrier((acc_req, stats, routing))
    target, placing = routing
    attention = acc_req / stats[local_heads:][:, None, :]
    attention = jnp.transpose(attention, (2, 0, 1)).reshape(tok_rows, -1).astype(jnp.bfloat16)
    tp_count = lax.axis_size("tp")
    tp_index = lax.axis_index("tp")

    def tp_gather(value, axis):
        pieces = [value] + [
            lax.ppermute(value, "tp", [(i, (i + k) % tp_count) for i in range(tp_count)])
            for k in range(1, tp_count)
        ]
        stacked = jnp.stack(pieces, axis=0)
        ordered = jnp.take(stacked, (tp_index - jnp.arange(tp_count)) % tp_count, axis=0)
        return jnp.concatenate([ordered[j] for j in range(tp_count)], axis=axis)

    full_attention = tp_gather(attention, 1)
    full_w_out = tp_gather(w_out, 0)
    mid = hidden.astype(jnp.float32) + jnp.dot(
        full_attention, full_w_out, preferred_element_type=jnp.float32
    )
    moe_in = (rms_rows(mid) * moe_gain).astype(jnp.bfloat16)
    logits = jnp.dot(moe_in.astype(jnp.float32), router, precision=lax.Precision.HIGHEST)
    chosen = jax.nn.sigmoid(jnp.take_along_axis(logits, expert_ids, axis=1))
    gates = chosen / jnp.sum(chosen, axis=1, keepdims=True)
    hits = target[:, :, None] == jnp.arange(EXPERTS * CAP, dtype=jnp.int32)[None, None, :]
    combining = jnp.sum(jnp.where(hits, gates[:, :, None], 0.0), axis=1)
    width = moe_in.shape[1]
    tp_width = width // tp_count
    moe_cols = lax.dynamic_slice_in_dim(moe_in, tp_index * tp_width, tp_width, 1)
    packed = jnp.einsum(
        "te,td->ed", placing, moe_cols, preferred_element_type=jnp.float32
    ).astype(jnp.bfloat16)
    splits = max(1, seq_count // EXPERTS)
    per_device = w_gate_up.shape[0]
    outgoing = jnp.repeat(packed.reshape(EXPERTS, CAP, tp_width), splits, axis=0).reshape(
        seq_count, per_device, CAP, tp_width
    )
    received = lax.all_to_all(outgoing, "seq", split_axis=0, concat_axis=0, tiled=True)
    count = received.shape[2]
    rows = tp_gather(received[:, 0].reshape(-1, tp_width), 1)
    gate = jnp.dot(rows, w_gate_up[0, 0], preferred_element_type=jnp.float32)
    upper = jnp.dot(rows, w_gate_up[0, 1], preferred_element_type=jnp.float32)
    inner = (jax.nn.gelu(gate, approximate=True) * upper).astype(jnp.bfloat16)
    results = jnp.dot(inner, w_down[0], preferred_element_type=jnp.float32).astype(jnp.bfloat16)
    share = lax.dynamic_slice_in_dim(results, tp_index * tp_width, tp_width, 1).astype(
        jnp.float32
    )
    for k in range(1, tp_count):
        target_cols = lax.dynamic_slice_in_dim(
            results, ((tp_index + k) % tp_count) * tp_width, tp_width, 1
        )
        share = share + lax.ppermute(
            target_cols, "tp", [(i, (i + k) % tp_count) for i in range(tp_count)]
        ).astype(jnp.float32)
    produced = share.reshape(seq_count, 1, count, tp_width)
    returned = lax.all_to_all(
        produced.astype(jnp.bfloat16), "seq", split_axis=0, concat_axis=0, tiled=True
    ).astype(jnp.float32)
    folded = jnp.sum(returned.reshape(EXPERTS, splits, CAP, tp_width), axis=1).reshape(
        EXPERTS * CAP, tp_width
    )
    mixture = jnp.dot(combining, folded, precision=lax.Precision.HIGHEST)
    mid_part = lax.dynamic_slice_in_dim(mid, tp_index * tp_width, tp_width, 1)
    return (mid_part + mixture).astype(jnp.bfloat16)

def solution(mesh):
    in_specs = (
        P("seq", None),
        P(),
        P(),
        P("seq", None),
        P(None, "tp"),
        P(None, "tp"),
        P(None, "tp"),
        P("tp", None),
        P("seq", None, "tp"),
        P("seq", None, "tp"),
        P(),
        P(),
        P("seq", None, None, "tp"),
        P("seq", "tp", None),
    )
    out_specs = P("seq", "tp")
    return jax.shard_map(shards, mesh=mesh, in_specs=in_specs, out_specs=out_specs, check_vma=False)
```

```python
import jax
import jax.numpy as jnp
from jax import lax
from jax.sharding import PartitionSpec as P
from jax.experimental import pallas as pl
from jax.experimental.pallas import tpu as pltpu

DH = 64
EXPERTS = 32
TOP = 2
PAGE = 128
MAXP = 256
SPAN_DEVS = 4
CAP = 10


NEGATIVE = -1e30


def passed_along(value, axis, steps):
    count = lax.axis_size(axis)
    pairs = [(source, (source + steps) % count) for source in range(count)]
    return lax.ppermute(value, axis, pairs)


def rms_rows(values):
    return values * lax.rsqrt(jnp.mean(values * values, axis=-1, keepdims=True) + 1e-06)


def online_update(state, queries, keys, values, mask):
    m_old, l_old, accum = state
    scale = queries.shape[2] ** (-0.5)
    scores = jnp.einsum("nhd,khd->hnk", queries, keys, preferred_element_type=jnp.float32) * scale
    scores = jnp.where(mask[None], scores, NEGATIVE)
    m_new = jnp.maximum(m_old, jnp.max(scores, axis=-1).T)
    probs = jnp.where(mask[None], jnp.exp(scores - m_new.T[:, :, None]), 0.0)
    factor = jnp.exp(m_old - m_new)
    l_new = l_old * factor + jnp.sum(probs, axis=-1).T
    weighted = jnp.einsum(
        "hnk,khd->nhd", probs.astype(jnp.bfloat16), values, preferred_element_type=jnp.float32
    )
    return (m_new, l_new, accum * factor[:, :, None] + weighted)


def attend_kernel(
    own_ref, page_ref, limit_ref, offset_ref, fresh_ref,
    q_ref, k_ref, v_ref, nk_ref, nv_ref, acc_ref, stat_ref,
):
    step = pl.program_id(0)
    owner = own_ref[step]
    first = (step == 0) | (own_ref[jnp.maximum(step - 1, 0)] != owner)
    heads = acc_ref.shape[2]

    @pl.when(first)
    def _():
        acc_ref[...] = jnp.zeros(acc_ref.shape, acc_ref.dtype)
        stat_ref[:, :, :heads, :] = jnp.full(
            stat_ref.shape[:2] + (heads, stat_ref.shape[3]), NEGATIVE, jnp.float32
        )
        stat_ref[:, :, heads:, :] = jnp.zeros(
            stat_ref.shape[:2] + (heads, stat_ref.shape[3]), jnp.float32
        )

    is_fresh = fresh_ref[step] == 1
    keys = jnp.where(is_fresh, nk_ref[0], k_ref[0])
    vals = jnp.where(is_fresh, nv_ref[0], v_ref[0])
    rows, cols = keys.shape[0], q_ref.shape[1]
    quarters, piece = acc_ref.shape[0], acc_ref.shape[4]
    k_pos = lax.broadcasted_iota(jnp.int32, (rows, cols), 0)
    q_pos = lax.broadcasted_iota(jnp.int32, (rows, cols), 1)
    valid = (k_pos < limit_ref[step]) & (q_pos >= offset_ref[step] + k_pos)

    def joined(read):
        return jnp.concatenate([read(c) for c in range(quarters)], axis=1)

    for h in range(heads):
        lanes = slice(h * DH, (h + 1) * DH)
        s = lax.dot_general(
            keys[:, lanes], q_ref[0, :, lanes], (((1,), (1,)), ((), ())),
            preferred_element_type=jnp.float32,
        ) * (DH ** (-0.5))
        s = jnp.where(valid, s, NEGATIVE)
        m_prev = joined(lambda c: stat_ref[c, 0, h : h + 1, :])
        l_prev = joined(lambda c: stat_ref[c, 0, heads + h : heads + h + 1, :])
        acc_prev = joined(lambda c: acc_ref[c, 0, h])
        m_cur = jnp.maximum(m_prev, jnp.max(s, axis=0, keepdims=True))
        p = jnp.where(valid, jnp.exp(s - m_cur), 0.0)
        alpha = jnp.exp(m_prev - m_cur)
        l_cur = alpha * l_prev + jnp.sum(p, axis=0, keepdims=True)
        pv = lax.dot_general(
            vals[:, lanes], p.astype(jnp.bfloat16), (((0,), (0,)), ((), ())),
            preferred_element_type=jnp.float32,
        )
        acc_cur = alpha * acc_prev + pv
        for c in range(quarters):
            cut = slice(c * piece, (c + 1) * piece)
            acc_ref[c, 0, h] = acc_cur[:, cut]
            stat_ref[c, 0, h : h + 1, :] = m_cur[:, cut]
            stat_ref[c, 0, heads + h : heads + h + 1, :] = l_cur[:, cut]


def local_attention(
    owner, page, limit, offset, fresh, everyone, cache_k, cache_v, new_k, new_v, heads, requests,
    piece,
):
    span_rows, width = everyone.shape[1], everyone.shape[2]
    page_rows = cache_k.shape[1]
    blocks = owner.shape[0]
    by_owner = lambda b, own, pg, lim, off, fr: (own[b], 0, 0)
    by_page = lambda b, own, pg, lim, off, fr: (pg[b], 0, 0)
    fixed = lambda b, own, pg, lim, off, fr: (0, 0, 0)
    acc_map = lambda b, own, pg, lim, off, fr: (0, own[b], 0, 0, 0)
    stat_map = lambda b, own, pg, lim, off, fr: (0, own[b], 0, 0)
    quarters = span_rows // piece
    grid_spec = pltpu.PrefetchScalarGridSpec(
        num_scalar_prefetch=5,
        grid=(blocks,),
        in_specs=[
            pl.BlockSpec((1, span_rows, width), by_owner),
            pl.BlockSpec((1, page_rows, width), by_page),
            pl.BlockSpec((1, page_rows, width), by_page),
            pl.BlockSpec((1, page_rows, width), fixed),
            pl.BlockSpec((1, page_rows, width), fixed),
        ],
        out_specs=[
            pl.BlockSpec((quarters, 1, heads, DH, piece), acc_map),
            pl.BlockSpec((quarters, 1, 2 * heads, piece), stat_map),
        ],
    )
    return pl.pallas_call(
        attend_kernel,
        grid_spec=grid_spec,
        out_shape=[
            jax.ShapeDtypeStruct((quarters, requests, heads, DH, piece), jnp.float32),
            jax.ShapeDtypeStruct((quarters, requests, 2 * heads, piece), jnp.float32),
        ],
        compiler_params=pltpu.CompilerParams(dimension_semantics=("arbitrary",)),
    )(owner, page, limit, offset, fresh, everyone, cache_k, cache_v, new_k, new_v)


def shards(
    hidden,
    page_table,
    cache_len,
    expert_ids,
    w_query,
    w_key,
    w_value,
    w_out,
    cache_k,
    cache_v,
    moe_gain,
    router,
    w_gate_up,
    w_down,
):
    tok_rows = hidden.shape[0]
    span_rows = tok_rows * SPAN_DEVS
    seq_count = lax.axis_size("seq")
    seq_index = lax.axis_index("seq")
    local_heads = w_query.shape[1] // DH
    request_total = page_table.shape[0]
    normed = rms_rows(hidden.astype(jnp.float32)).astype(jnp.bfloat16)
    queries = jnp.dot(normed, w_query, preferred_element_type=jnp.float32).astype(jnp.bfloat16)
    new_keys = (
        jnp.dot(normed, w_key, preferred_element_type=jnp.float32)
        .astype(jnp.bfloat16)
        .reshape(tok_rows, local_heads, DH)
    )
    new_values = (
        jnp.dot(normed, w_value, preferred_element_type=jnp.float32)
        .astype(jnp.bfloat16)
        .reshape(tok_rows, local_heads, DH)
    )
    page_count = cache_k.shape[0]
    page_ids = seq_index * page_count + jnp.arange(page_count, dtype=jnp.int32)
    listing = page_table.reshape(-1)
    matches = listing[None, :] == page_ids[:, None]
    entry_index = jnp.arange(listing.shape[0], dtype=jnp.int32)
    found = jnp.sum(jnp.where(matches, entry_index[None, :] + 1, 0), axis=1) - 1
    page_owner = jnp.where(found >= 0, found // MAXP, -1)
    page_order = jnp.where(found >= 0, found % MAXP, 0)
    page_limit = jnp.where(found >= 0, cache_len[jnp.maximum(page_owner, 0)], 0)
    own_request = seq_index * tok_rows // span_rows
    own_offset = seq_index * tok_rows % span_rows
    slot_range = jnp.arange(PAGE, dtype=jnp.int32)
    page_valid = (found >= 0)[:, None] & (
        page_order[:, None] * PAGE + slot_range[None, :] < page_limit[:, None]
    )
    block_total = page_count + 1
    owners = jnp.concatenate([jnp.maximum(page_owner, 0), own_request[None]], axis=0)
    key_limits = jnp.concatenate(
        [jnp.clip(page_limit - page_order * PAGE, 0, PAGE), jnp.full((1,), PAGE, jnp.int32)], axis=0
    )
    query_offsets = jnp.concatenate(
        [jnp.full((page_count,), -span_rows - PAGE, jnp.int32), own_offset[None]], axis=0
    )
    block_order = jnp.argsort(owners, stable=True).astype(jnp.int32)
    sorted_owner = owners[block_order]
    sorted_limit = key_limits[block_order]
    sorted_offset = query_offsets[block_order]
    sorted_fresh = (block_order == page_count).astype(jnp.int32)
    sorted_page = jnp.minimum(block_order, page_count - 1)
    block_tables = (sorted_owner, sorted_page, sorted_limit, sorted_offset, sorted_fresh)
    fresh_kv = (
        new_keys.reshape(1, tok_rows, local_heads * DH),
        new_values.reshape(1, tok_rows, local_heads * DH),
    )
    flat_ids = expert_ids.reshape(-1)
    onehot = (flat_ids[:, None] == jnp.arange(EXPERTS, dtype=jnp.int32)[None, :]).astype(jnp.int32)
    ranks = jnp.sum((jnp.cumsum(onehot, axis=0) - 1) * onehot, axis=1)
    target = (flat_ids * CAP + ranks).reshape(tok_rows, TOP)
    slot_hits = target[:, :, None] == jnp.arange(EXPERTS * CAP, dtype=jnp.int32)[None, None, :]
    routing = (target, jnp.any(slot_hits, axis=1).astype(jnp.bfloat16))
    gathered = queries
    held_bits = []
    gather_count = seq_count.bit_length() - 1
    for bit in ([5, 4, 2, 3, 1, 0] if gather_count == 6 else list(range(gather_count - 1, -1, -1))):
        pairs = [(source, source ^ (1 << bit)) for source in range(seq_count)]
        got = lax.ppermute(gathered, "seq", pairs)
        low_side = ((seq_index >> bit) & 1) == 0
        position = sum(1 for held in held_bits if held > bit)
        gathered = jnp.stack(
            [jnp.where(low_side, gathered, got), jnp.where(low_side, got, gathered)], axis=position
        )
        held_bits.insert(position, bit)
        if len(held_bits) == gather_count - 1:
            gathered, block_tables, fresh_kv, routing = lax.optimization_barrier(
                (gathered, block_tables, fresh_kv, routing)
            )
    everyone = gathered.reshape(request_total, span_rows, local_heads * DH)
    width_heads = local_heads * DH
    sorted_owner, sorted_page, sorted_limit, sorted_offset, sorted_fresh = block_tables
    acc_out, stat_out = local_attention(
        sorted_owner,
        sorted_page,
        sorted_limit,
        sorted_offset,
        sorted_fresh,
        everyone,
        cache_k,
        cache_v,
        fresh_kv[0],
        fresh_kv[1],
        local_heads,
        request_total,
        tok_rows,
    )
    visited = jnp.any(
        sorted_owner[:, None] == jnp.arange(request_total, dtype=jnp.int32)[None, :], axis=0
    )
    stat_init = jnp.where(jnp.arange(2 * local_heads) < local_heads, NEGATIVE, 0.0)
    acc_req = jnp.where(visited[None, :, None, None, None], acc_out, 0.0)
    stats = jnp.where(visited[None, :, None, None], stat_out, stat_init[None, None, :, None])
    quarters = span_rows // tok_rows
    quarter_bits = quarters.bit_length() - 1
    request_bits = request_total.bit_length() - 1
    acc_req = acc_req.reshape((2,) * (quarter_bits + request_bits) + (local_heads, DH, tok_rows))
    stats = stats.reshape((2,) * (quarter_bits + request_bits) + (2 * local_heads, tok_rows))
    bit_names = list(range(quarter_bits - 1, -1, -1))
    bit_names += [quarter_bits + k for k in range(request_bits - 1, -1, -1)]
    acc_names = bit_names + ["h", "d", "q"]
    stat_names = bit_names + ["s", "q"]
    bit_count = request_bits + quarter_bits
    for bit in ([0, 1, 3, 2, 4, 5] if bit_count == 6 else list(range(bit_count))):
        acc_axis = acc_names.index(bit)
        stat_axis = stat_names.index(bit)
        acc_names.pop(acc_axis)
        stat_names.pop(stat_axis)
        own_bit = (seq_index >> bit) & 1
        keep_acc = lax.dynamic_index_in_dim(acc_req, own_bit, acc_axis, keepdims=False)
        send_acc = lax.dynamic_index_in_dim(acc_req, 1 - own_bit, acc_axis, keepdims=False)
        keep_stats = lax.dynamic_index_in_dim(stats, own_bit, stat_axis, keepdims=False)
        send_stats = lax.dynamic_index_in_dim(stats, 1 - own_bit, stat_axis, keepdims=False)
        pairs = [(source, source ^ (1 << bit)) for source in range(seq_count)]
        got_acc = lax.ppermute(send_acc.astype(jnp.bfloat16), "seq", pairs).astype(jnp.float32)
        got_stats = lax.ppermute(send_stats, "seq", pairs)
        s_axis = stat_names.index("s")
        keep_m = lax.slice_in_dim(keep_stats, 0, local_heads, axis=s_axis)
        keep_l = lax.slice_in_dim(keep_stats, local_heads, 2 * local_heads, axis=s_axis)
        got_m = lax.slice_in_dim(got_stats, 0, local_heads, axis=s_axis)
        got_l = lax.slice_in_dim(got_stats, local_heads, 2 * local_heads, axis=s_axis)
        m_new = jnp.maximum(keep_m, got_m)
        keep_factor = jnp.exp(keep_m - m_new)
        got_factor = jnp.exp(got_m - m_new)
        l_new = keep_l * keep_factor + got_l * got_factor
        d_axis = acc_names.index("d")
        acc_req = keep_acc * jnp.expand_dims(keep_factor, d_axis) + got_acc * jnp.expand_dims(
            got_factor, d_axis
        )
        stats = jnp.concatenate([m_new, l_new], axis=s_axis)
    attention = acc_req / stats[local_heads:][:, None, :]
    attention = jnp.transpose(attention, (2, 0, 1)).reshape(tok_rows, -1).astype(jnp.bfloat16)
    tp_count = lax.axis_size("tp")
    tp_index = lax.axis_index("tp")

    def tp_gather(value, axis):
        pieces = [value] + [
            lax.ppermute(value, "tp", [(i, (i + k) % tp_count) for i in range(tp_count)])
            for k in range(1, tp_count)
        ]
        stacked = jnp.stack(pieces, axis=0)
        ordered = jnp.take(stacked, (tp_index - jnp.arange(tp_count)) % tp_count, axis=0)
        return jnp.concatenate([ordered[j] for j in range(tp_count)], axis=axis)

    full_attention = tp_gather(attention, 1)
    full_w_out = tp_gather(w_out, 0)
    mid = hidden.astype(jnp.float32) + jnp.dot(
        full_attention, full_w_out, preferred_element_type=jnp.float32
    )
    moe_in = (rms_rows(mid) * moe_gain).astype(jnp.bfloat16)
    logits = jnp.dot(moe_in.astype(jnp.float32), router, precision=lax.Precision.HIGHEST)
    chosen = jax.nn.sigmoid(jnp.take_along_axis(logits, expert_ids, axis=1))
    gates = chosen / jnp.sum(chosen, axis=1, keepdims=True)
    target, placing = routing
    hits = target[:, :, None] == jnp.arange(EXPERTS * CAP, dtype=jnp.int32)[None, None, :]
    combining = jnp.sum(jnp.where(hits, gates[:, :, None], 0.0), axis=1)
    width = moe_in.shape[1]
    tp_width = width // tp_count
    moe_cols = lax.dynamic_slice_in_dim(moe_in, tp_index * tp_width, tp_width, 1)
    packed = jnp.einsum(
        "te,td->ed", placing, moe_cols, preferred_element_type=jnp.float32
    ).astype(jnp.bfloat16)
    splits = max(1, seq_count // EXPERTS)
    per_device = w_gate_up.shape[0]
    outgoing = jnp.repeat(packed.reshape(EXPERTS, CAP, tp_width), splits, axis=0).reshape(
        seq_count, per_device, CAP, tp_width
    )
    received = lax.all_to_all(outgoing, "seq", split_axis=0, concat_axis=0, tiled=True)
    count = received.shape[2]
    rows = tp_gather(received[:, 0].reshape(-1, tp_width), 1)
    gate = jnp.dot(rows, w_gate_up[0, 0], preferred_element_type=jnp.float32)
    upper = jnp.dot(rows, w_gate_up[0, 1], preferred_element_type=jnp.float32)
    inner = (jax.nn.gelu(gate, approximate=True) * upper).astype(jnp.bfloat16)
    results = jnp.dot(inner, w_down[0], preferred_element_type=jnp.float32).astype(jnp.bfloat16)
    share = lax.dynamic_slice_in_dim(results, tp_index * tp_width, tp_width, 1).astype(
        jnp.float32
    )
    for k in range(1, tp_count):
        target_cols = lax.dynamic_slice_in_dim(
            results, ((tp_index + k) % tp_count) * tp_width, tp_width, 1
        )
        share = share + lax.ppermute(
            target_cols, "tp", [(i, (i + k) % tp_count) for i in range(tp_count)]
        ).astype(jnp.float32)
    produced = share.reshape(seq_count, 1, count, tp_width)
    returned = lax.all_to_all(
        produced.astype(jnp.bfloat16), "seq", split_axis=0, concat_axis=0, tiled=True
    ).astype(jnp.float32)
    folded = jnp.sum(returned.reshape(EXPERTS, splits, CAP, tp_width), axis=1).reshape(
        EXPERTS * CAP, tp_width
    )
    mixture = jnp.dot(combining, folded, precision=lax.Precision.HIGHEST)
    mid_part = lax.dynamic_slice_in_dim(mid, tp_index * tp_width, tp_width, 1)
    return (mid_part + mixture).astype(jnp.bfloat16)

def solution(mesh):
    in_specs = (
        P("seq", None),
        P(),
        P(),
        P("seq", None),
        P(None, "tp"),
        P(None, "tp"),
        P(None, "tp"),
        P("tp", None),
        P("seq", None, "tp"),
        P("seq", None, "tp"),
        P(),
        P(),
        P("seq", None, None, "tp"),
        P("seq", "tp", None),
    )
    out_specs = P("seq", "tp")
    return jax.shard_map(shards, mesh=mesh, in_specs=in_specs, out_specs=out_specs, check_vma=False)
```
